32 devices in a mesh: groups: 2 (over y), ctx: 4 (over z), mp: 4 (over x, core).
Axes of the slice: x: 2, y: 2, z: 4, core: 2. Of those that a mesh axis runs over, the one named last changes fastest.
Arguments:
- features: bfloat16 [4, 512, 1536], P('groups', 'ctx'), parts along dimension 0, may hold values from -6 to 6
- frame_counts: int32 [4], P('groups'), parts along dimension 0, may hold values from 1 to 512, 768 in all
- attn_gain: float32 [1536], replicated, may hold values from 0.25 to 1.75
- w_qkv: bfloat16 [3, 1536, 1024], P(None, None, 'mp'), may hold values from -2 to 2
- w_out: bfloat16 [1024, 1536], P('mp'), may hold values from -0.375 to 0.375
- conv_gain: float32 [1536], replicated, may hold values from 0.25 to 1.75
- w_glu: bfloat16 [2, 1536, 1536], P(None, None, 'mp'), may hold values from -0.15625 to 0.15625
- kernel: float32 [31, 1536], P(None, 'mp'), may hold values from -2 to 2
- bn_scale: float32 [1536], P('mp'), may hold values from 0.5 to 2
- bn_shift: float32 [1536], P('mp'), may hold values from -2.5 to 2.5
- w_pw: bfloat16 [1536, 1536], P('mp'), may hold values from -0.15625 to 0.15625
- clip_level: int32 [1536], replicated, may hold values from 6 to 39
Outputs:
- encoded: bfloat16 [4, 512, 1536], P('groups', ('ctx', 'mp')), parts along dimension 0
The draws below stay inside these ranges and needn't reach their ends.
There are 2 independent parts, one for each index of `groups`. The reference program is written for one: setup_inputs(seed, part) draws one part's arguments, and reference() takes and returns one part's arrays. A program takes and returns all parts, laid end to end along the dimension named above; an argument that names none is the same for every part. Nothing has to cross between parts.
Inputs may be any that keep to these rules, and one draw needn't show every extreme that they name: frame_counts[s] frames of recording s fill slots 0 to frame_counts[s] - 1, later slots are padding; some recording fills all 512 slots.
All inputs are finite; a program needn't handle non-finite values.
Results may differ from the reference program's by a relative error of at most 0.023.
Values may be sent and summed in bfloat16 or wider, within the bound.
No kernel may reach another device: no remote copies, remote signals or barrier semaphores. Data moves between devices by JAX's collectives and lax.ppermute only.
A program may use at most 128 MiB of HBM per device.

```python
import math
import jax
import jax.numpy as jnp
import numpy as np
from jax import lax

D = 1536
HEADS = 16
HEAD_DIM = 64
KERNEL = 31
SEQS = 2
LENGTH = 512
N_MP = 4


def draw_w_qkv(key, part):
    columns = HEADS * HEAD_DIM
    sub_keys = jax.random.split(key, 1)
    base = jax.random.normal(sub_keys[0], (3, D, columns), jnp.float32) / math.sqrt(D)
    drawn = base * jnp.array([2.0, 2.0, 1.0], jnp.float32)[:, None, None]
    return jnp.clip(drawn, -2.0, 2.0).astype(jnp.bfloat16)


def plant(values, stream_key, least, top_value):
    shape = values.shape
    spot = [jax.random.randint(jax.random.fold_in(stream_key, axis), (), 0, shape[axis]) for axis in range(len(shape))]
    values = values.at[tuple(spot)].set(least)
    longest = shape.index(max(shape))
    spot[longest] = (spot[longest] + 1) % shape[longest]
    return values.at[tuple(spot)].set(top_value)


def block_scale(stream_key, extent, cuts, smallest, high):
    level = 1.0
    for position, parts in cuts:
        draws = jax.random.uniform(jax.random.fold_in(jax.random.fold_in(stream_key, 6), position), (parts,), jnp.float32, smallest / len(cuts), high / len(cuts))
        level = level * jnp.repeat(jnp.exp(draws), extent[position] // parts).reshape((-1,) + (1,) * (len(extent) - 1 - position))
    return level


def profile(amount, total, reach, lean):
    weights = [(1 << 20) // math.isqrt(standing ** lean) + 1 for standing in range(2, amount + 1)]
    surplus, given = total - reach - (amount - 1), [1] * (amount - 1)
    while surplus > 0:
        free = [i for i in range(amount - 1) if given[i] < reach]
        mass, budget = sum([weights[i] for i in free]), surplus
        for i in free:
            addition = min(reach - given[i], max(1, budget * weights[i] // mass), surplus)
            given[i] = given[i] + addition
            surplus = surplus - addition
    return np.array([reach] + given)


def uneven_parts(stream_key, count, total, limit, skew):
    if count == 2:
        one = jax.random.randint(stream_key, (), max(1, total - limit), min(limit, total - 1) + 1)
        return jnp.stack([one, total - one])
    sizes = jnp.asarray(profile(count, total, limit, skew), jnp.int32)
    couples = (count - 1) // 2
    giver, sink = sizes[1:1 + 2 * couples:2], sizes[2:2 + 2 * couples:2]
    margin = jnp.minimum(giver - 1, limit - sink)
    passed = jax.random.randint(jax.random.fold_in(stream_key, 1), (couples,), 0, 1 << 20) % (margin + 1)
    sizes = sizes.at[1:1 + 2 * couples:2].set(giver - passed).at[2:2 + 2 * couples:2].set(sink + passed)
    return sizes[jax.random.permutation(jax.random.fold_in(stream_key, 2), count)]


def bell_draw(stream_key, shape, scale, reach, cuts=(), kind=jnp.bfloat16):
    values = scale * jax.random.normal(stream_key, shape, jnp.float32)
    if cuts:
        values = values * block_scale(stream_key, shape, cuts, -0.22, 0.18)
    return jnp.clip(values, -reach, reach).astype(kind)


def setup_inputs(seed: int = 0, part: int = 0) -> dict:
    keys = jax.random.split(jax.random.key(seed), 13)
    part_keys = jax.random.split(jax.random.fold_in(keys[12], part), 13)
    features = bell_draw(part_keys[0], (SEQS, LENGTH, D), 1.0, 6.0, ((1, 4),))
    frame_counts = uneven_parts(part_keys[1], SEQS, 3 * SEQS * LENGTH // 4, LENGTH, 2).astype(jnp.int32)
    attn_gain = jnp.clip(1.0 + 0.15 * jax.random.normal(keys[2], (D,), jnp.float32), 0.25, 1.75)
    w_qkv = draw_w_qkv(jax.random.fold_in(keys[12], 71), part)
    w_out = bell_draw(keys[4], (HEADS * HEAD_DIM, D), (HEADS * HEAD_DIM // 4) ** -0.5, 0.375, ((0, 4),))
    conv_gain = jnp.clip(1.0 + 0.15 * jax.random.normal(keys[5], (D,), jnp.float32), 0.25, 1.75)
    w_glu = bell_draw(keys[6], (2, D, D), D ** -0.5, 0.15625, ((2, 4),))
    kernel = bell_draw(keys[7], (KERNEL, D), (KERNEL // 4) ** -0.5, 2.0, ((1, 4),), jnp.float32)
    bn_scale = jnp.clip(jnp.exp(math.log(2.0) - 1.3862944 * jax.random.uniform(keys[8], (D,), jnp.float32) ** block_scale(keys[8], (D,), ((0, 4),), -0.2, 0.2)), 0.5, 2.0)
    bn_shift = bell_draw(keys[9], (D,), 0.5, 2.5, ((0, 4),), jnp.float32)
    w_pw = bell_draw(keys[10], (D, D), D ** -0.5, 0.15625, ((0, 4),))
    clip_level = plant(jax.random.randint(keys[11], (D,), 6, 40), jax.random.fold_in(keys[11], 1), 6, 39).astype(jnp.int32)
    return {"features": features, "frame_counts": frame_counts, "attn_gain": attn_gain, "w_qkv": w_qkv, "w_out": w_out, "conv_gain": conv_gain, "w_glu": w_glu, "kernel": kernel, "bn_scale": bn_scale, "bn_shift": bn_shift, "w_pw": w_pw, "clip_level": clip_level}


epsilon = 1e-05
masked_score = -1e+30

def layer_norm(values, gain):
    centre = lax.optimization_barrier(jnp.mean(values, axis=-1, keepdims=True))
    centred = values - centre
    variance = lax.optimization_barrier(jnp.mean(centred * centred, axis=-1, keepdims=True))
    return centred * lax.rsqrt(variance + epsilon) * gain

def grouped_sum(row_operand, weight_rows):
    group_width = row_operand.shape[1] // N_MP
    total_sum = jnp.zeros((row_operand.shape[0], weight_rows.shape[1]), jnp.float32)
    for group_index in range(N_MP):
        lower = group_index * group_width
        group_term = jnp.dot(row_operand[:, lower:lower + group_width], weight_rows[lower:lower + group_width], preferred_element_type=jnp.float32)
        total_sum = total_sum + lax.optimization_barrier(group_term.astype(jnp.bfloat16)).astype(jnp.float32)
    return total_sum

def reference(features, frame_counts, attn_gain, w_qkv, w_out, conv_gain, w_glu, kernel, bn_scale, bn_shift, w_pw, clip_level):
    records, length, model_width = features.shape
    flat_rows = records * length
    normed = layer_norm(features.astype(jnp.float32), attn_gain).astype(jnp.bfloat16).reshape(flat_rows, model_width)
    stacked = []
    for slot_index in range(3):
        projected = jnp.dot(normed, w_qkv[slot_index], preferred_element_type=jnp.float32).astype(jnp.bfloat16)
        stacked.append(lax.optimization_barrier(projected).astype(jnp.float32).reshape(records, length, HEADS, HEAD_DIM))
    positions = jnp.arange(length, dtype=jnp.int32)

    def attend(record_item):
        queries, key_rows, value_rows, limit_here = record_item
        scores = jnp.einsum('qhe,khe->hqk', queries, key_rows) * HEAD_DIM ** (-0.5)
        scores = jnp.where((positions < limit_here)[None, None, :], scores, masked_score)
        row_max = lax.optimization_barrier(jnp.max(scores, axis=-1, keepdims=True))
        weights = jnp.exp(scores - row_max)
        row_sum = lax.optimization_barrier(jnp.sum(weights, axis=-1))
        rounded = lax.optimization_barrier(weights.astype(jnp.bfloat16)).astype(jnp.float32)
        mixture = jnp.einsum('hqk,khe->qhe', rounded, value_rows) / jnp.transpose(row_sum)[:, :, None]
        return mixture.astype(jnp.bfloat16).reshape(length, HEADS * HEAD_DIM)
    attended = lax.map(attend, (stacked[0], stacked[1], stacked[2], frame_counts)).reshape(flat_rows, HEADS * HEAD_DIM)
    residual = features.astype(jnp.float32).reshape(flat_rows, model_width) + grouped_sum(attended, w_out)
    normed_conv = layer_norm(residual, conv_gain).astype(jnp.bfloat16)
    value_half = jnp.dot(normed_conv, w_glu[0], preferred_element_type=jnp.float32)
    gate_half = jnp.dot(normed_conv, w_glu[1], preferred_element_type=jnp.float32)
    gated_rows = (value_half * jax.nn.sigmoid(gate_half)).astype(jnp.bfloat16).reshape(records, length, model_width)
    frame_live = positions[None, :] < frame_counts[:, None]
    gated_rows = jnp.where(frame_live[..., None], gated_rows, jnp.zeros((), jnp.bfloat16))
    rim_width = KERNEL // 2
    padded = jnp.pad(lax.optimization_barrier(gated_rows), ((0, 0), (rim_width, rim_width), (0, 0)))
    depthwise = jnp.zeros((records, length, model_width), jnp.float32)
    for tap_index in range(KERNEL):
        depthwise = depthwise + padded[:, tap_index:tap_index + length, :].astype(jnp.float32) * kernel[tap_index]
    activated = jax.nn.silu(depthwise * bn_scale + bn_shift).astype(jnp.bfloat16).reshape(flat_rows, model_width)
    combined = residual + grouped_sum(activated, w_pw)
    clip_bound = clip_level.astype(jnp.float32) / 16.0
    clipped = jnp.clip(combined, -clip_bound, clip_bound).reshape(records, length, model_width)
    return jnp.where(frame_live[..., None], clipped, 0.0).astype(jnp.bfloat16)
```

```python
import jax
import jax.numpy as jnp
from jax import lax
from jax.sharding import PartitionSpec as P

HEAD_DIM = 64


epsilon = 1e-05
masked_score = -1e30


def with_halo(x, sides, width):
    for axis, dim in sides:
        devices, length = (lax.axis_size(axis), x.shape[dim])
        up = [(i, (i + 1) % devices) for i in range(devices - 1)]
        down = [(j, i) for i, j in up]
        last = lax.slice_in_dim(x, length - width, length, axis=dim)
        initial = lax.slice_in_dim(x, 0, width, axis=dim)
        before = lax.ppermute(last, axis, up)
        after = lax.ppermute(initial, axis, down)
        x = jnp.concatenate([before, x, after], axis=dim)
    return x


def layer_norm(values, gain):
    centre = jnp.mean(values, axis=-1, keepdims=True)
    centred = values - centre
    variance = jnp.mean(centred * centred, axis=-1, keepdims=True)
    return centred * lax.rsqrt(variance + epsilon) * gain


def gated_units(normed, w_glu):
    halves = jnp.einsum("std,gdc->gstc", normed, w_glu, preferred_element_type=jnp.float32)
    return (halves[0] * jax.nn.sigmoid(halves[1])).astype(jnp.bfloat16)


def xor_pairs(count, mask):
    return [(i, i ^ mask) for i in range(count)]


def bit_count(count):
    bits = count.bit_length() - 1
    assert (1 << bits) == count
    return bits


def reduce_scatter_rows(x, axis, dim):
    count, rank = lax.axis_size(axis), lax.axis_index(axis)
    bits = bit_count(count)
    shape = x.shape
    block = shape[dim] // count
    acc = x.reshape(shape[:dim] + (2,) * bits + (block,) + shape[dim + 1 :])
    for b in range(bits):
        bit_axis = dim + bits - 1 - b
        mine = (rank >> b) & 1
        keep = lax.dynamic_index_in_dim(acc, mine, bit_axis, keepdims=False)
        send = lax.dynamic_index_in_dim(acc, 1 - mine, bit_axis, keepdims=False)
        got = lax.ppermute(send.astype(jnp.bfloat16), axis, xor_pairs(count, 1 << b))
        acc = keep.astype(jnp.float32) + got.astype(jnp.float32)
    return acc


def all_gather_rows(x, axis, dim):
    count, rank = lax.axis_size(axis), lax.axis_index(axis)
    bits = bit_count(count)
    shape = x.shape
    acc = x
    for k, b in enumerate(reversed(range(bits))):
        mine = ((rank >> b) & 1) == 0
        got = lax.ppermute(acc, axis, xor_pairs(count, 1 << b))
        low = jnp.where(mine, acc, got)
        high = jnp.where(mine, got, acc)
        acc = jnp.stack([low, high], axis=dim + k)
    return acc.reshape(shape[:dim] + (shape[dim] * count,) + shape[dim + 1 :])


def ring_gather(x, axis):
    count = lax.axis_size(axis)
    right = [(i, (i + 1) % count) for i in range(count)]
    left = [(i, (i - 1) % count) for i in range(count)]
    right_steps = count // 2
    left_steps = count - 1 - right_steps
    from_left, from_right = [], []
    going_right, going_left = x, x
    for step in range(right_steps):
        going_right = lax.ppermute(going_right, axis, right)
        from_left.append(going_right)
        if step < left_steps:
            going_left = lax.ppermute(going_left, axis, left)
            from_right.append(going_left)
    return jnp.stack([x] + from_right + from_left[::-1], axis=0)


def shards(
    features,
    frame_counts,
    attn_gain,
    w_qkv,
    w_out,
    conv_gain,
    w_glu,
    kernel,
    bn_scale,
    bn_shift,
    w_pw,
    clip_level,
):
    records, frames_here, model_width = features.shape
    head_count = w_qkv.shape[2] // HEAD_DIM
    ctx_rank = lax.axis_index("ctx")
    ctx_count = lax.axis_size("ctx")
    score_scale = HEAD_DIM ** (-0.5)
    first_frame = ctx_rank * frames_here
    normed = layer_norm(features.astype(jnp.float32), attn_gain).astype(jnp.bfloat16)
    projected = jnp.einsum(
        "std,idc->istc", normed, w_qkv, preferred_element_type=jnp.float32
    ).astype(jnp.bfloat16)
    queries = projected[0]
    query_heads = queries.reshape(records, frames_here, head_count, HEAD_DIM)
    kv_all = ring_gather(projected[1:], "ctx")
    key_heads = kv_all[:, 0].reshape(ctx_count, records, frames_here, head_count, HEAD_DIM)
    value_heads = kv_all[:, 1].reshape(ctx_count, records, frames_here, head_count, HEAD_DIM)
    scores = (
        jnp.einsum("sqhe,cskhe->shqck", query_heads, key_heads, preferred_element_type=jnp.float32)
        * score_scale
    )
    block_rank = (ctx_rank + jnp.arange(ctx_count, dtype=jnp.int32)) % ctx_count
    positions = block_rank[:, None] * frames_here + jnp.arange(frames_here, dtype=jnp.int32)
    is_live = positions[None] < frame_counts[:, None, None]
    scores = jnp.where(is_live[:, None, None], scores, masked_score)
    row_max = jnp.max(scores, axis=(-2, -1), keepdims=True)
    weights = jnp.exp(scores - row_max)
    row_sum = jnp.sum(weights, axis=(-2, -1))
    contrib = jnp.einsum(
        "shqck,cskhe->shqe",
        weights.astype(jnp.bfloat16),
        value_heads,
        preferred_element_type=jnp.float32,
    )
    attended = (contrib / row_sum[..., None]).astype(jnp.bfloat16)
    attended = attended.transpose(0, 2, 1, 3).reshape(records, frames_here, head_count * HEAD_DIM)
    attn_part = jnp.einsum("stc,cd->std", attended, w_out, preferred_element_type=jnp.float32)
    mp_count = lax.axis_size("mp")
    mp_rank = lax.axis_index("mp")
    rows_mine = frames_here // mp_count
    row_start = mp_rank * rows_mine
    attn_mine = reduce_scatter_rows(attn_part.astype(jnp.bfloat16), "mp", 1)
    features_mine = lax.dynamic_slice_in_dim(features, row_start, rows_mine, 1)
    residual_mine = features_mine.astype(jnp.float32) + attn_mine
    normed_mine = layer_norm(residual_mine, conv_gain).astype(jnp.bfloat16)
    normed_conv = all_gather_rows(normed_mine, "mp", 1)
    gated_rows = gated_units(normed_conv, w_glu)
    frame_ids = first_frame + jnp.arange(frames_here, dtype=jnp.int32)
    frame_live = frame_ids[None, :] < frame_counts[:, None]
    gated_rows = jnp.where(frame_live[..., None], gated_rows, jnp.zeros((), jnp.bfloat16))
    rim_width = kernel.shape[0] // 2
    padded = with_halo(gated_rows, (("ctx", 1),), rim_width)
    depthwise = jnp.zeros(gated_rows.shape, jnp.float32)
    for tap_index in range(kernel.shape[0]):
        depthwise = (
            depthwise
            + padded[:, tap_index : tap_index + frames_here, :].astype(jnp.float32)
            * kernel[tap_index]
        )
    activated = jax.nn.silu(depthwise * bn_scale + bn_shift).astype(jnp.bfloat16)
    conv_part = jnp.einsum("stc,cd->std", activated, w_pw, preferred_element_type=jnp.float32)
    conv_rows = reduce_scatter_rows(conv_part.astype(jnp.bfloat16), "mp", 1)
    combined = residual_mine + conv_rows
    clip_bound = clip_level.astype(jnp.float32) / 16.0
    clipped = jnp.clip(combined, -clip_bound, clip_bound)
    mine_ids = first_frame + row_start + jnp.arange(rows_mine, dtype=jnp.int32)
    mine_live = mine_ids[None, :] < frame_counts[:, None]
    return jnp.where(mine_live[..., None], clipped, 0.0).astype(jnp.bfloat16)


def solution(mesh):
    return jax.shard_map(
        shards,
        mesh=mesh,
        in_specs=(
            P("groups", "ctx", None),
            P("groups"),
            P(),
            P(None, None, "mp"),
            P("mp", None),
            P(),
            P(None, None, "mp"),
            P(None, "mp"),
            P("mp"),
            P("mp"),
            P("mp", None),
            P(),
        ),
        out_specs=P("groups", ("ctx", "mp"), None),
        check_vma=False,
    )
```

```python
import jax
import jax.numpy as jnp
from jax import lax
from jax.sharding import PartitionSpec as P

HEAD_DIM = 64


epsilon = 1e-05
masked_score = -1e30


def with_halo(x, sides, width):
    for axis, dim in sides:
        devices, length = (lax.axis_size(axis), x.shape[dim])
        up = [(i, (i + 1) % devices) for i in range(devices - 1)]
        down = [(j, i) for i, j in up]
        last = lax.slice_in_dim(x, length - width, length, axis=dim)
        initial = lax.slice_in_dim(x, 0, width, axis=dim)
        before = lax.ppermute(last, axis, up)
        after = lax.ppermute(initial, axis, down)
        x = jnp.concatenate([before, x, after], axis=dim)
    return x


def layer_norm(values, gain):
    centre = jnp.mean(values, axis=-1, keepdims=True)
    centred = values - centre
    variance = jnp.mean(centred * centred, axis=-1, keepdims=True)
    return centred * lax.rsqrt(variance + epsilon) * gain


def gated_units(normed, w_glu):
    halves = jnp.einsum("std,gdc->gstc", normed, w_glu, preferred_element_type=jnp.float32)
    return (halves[0] * jax.nn.sigmoid(halves[1])).astype(jnp.bfloat16)


def xor_pairs(count, mask):
    return [(i, i ^ mask) for i in range(count)]


def bit_count(count):
    bits = count.bit_length() - 1
    assert (1 << bits) == count
    return bits


def reduce_scatter_rows(x, axis, dim):
    count, rank = lax.axis_size(axis), lax.axis_index(axis)
    bits = bit_count(count)
    shape = x.shape
    block = shape[dim] // count
    acc = x.reshape(shape[:dim] + (2,) * bits + (block,) + shape[dim + 1 :])
    for b in range(bits):
        bit_axis = dim + bits - 1 - b
        mine = (rank >> b) & 1
        keep = lax.dynamic_index_in_dim(acc, mine, bit_axis, keepdims=False)
        send = lax.dynamic_index_in_dim(acc, 1 - mine, bit_axis, keepdims=False)
        got = lax.ppermute(send.astype(jnp.bfloat16), axis, xor_pairs(count, 1 << b))
        acc = keep.astype(jnp.float32) + got.astype(jnp.float32)
    return acc


def all_gather_rows(x, axis, dim):
    count, rank = lax.axis_size(axis), lax.axis_index(axis)
    bits = bit_count(count)
    shape = x.shape
    acc = x
    for k, b in enumerate(reversed(range(bits))):
        mine = ((rank >> b) & 1) == 0
        got = lax.ppermute(acc, axis, xor_pairs(count, 1 << b))
        low = jnp.where(mine, acc, got)
        high = jnp.where(mine, got, acc)
        acc = jnp.stack([low, high], axis=dim + k)
    return acc.reshape(shape[:dim] + (shape[dim] * count,) + shape[dim + 1 :])


def ring_gather(x, axis):
    count = lax.axis_size(axis)
    right = [(i, (i + 1) % count) for i in range(count)]
    left = [(i, (i - 1) % count) for i in range(count)]
    right_steps = count // 2
    left_steps = count - 1 - right_steps
    from_left, from_right = [], []
    going_right, going_left = x, x
    for step in range(right_steps):
        going_right = lax.ppermute(going_right, axis, right)
        from_left.append(going_right)
        if step < left_steps:
            going_left = lax.ppermute(going_left, axis, left)
            from_right.append(going_left)
    return jnp.stack([x] + from_right + from_left[::-1], axis=0)


def chunk(
    features,
    frame_counts,
    attn_gain,
    w_qkv,
    w_out,
    conv_gain,
    w_glu,
    kernel,
    bn_scale,
    bn_shift,
    w_pw,
    clip_level,
):
    records, frames_here, model_width = features.shape
    head_count = w_qkv.shape[2] // HEAD_DIM
    ctx_rank = lax.axis_index("ctx")
    ctx_count = lax.axis_size("ctx")
    score_scale = HEAD_DIM ** (-0.5)
    first_frame = ctx_rank * frames_here
    normed = layer_norm(features.astype(jnp.float32), attn_gain).astype(jnp.bfloat16)
    projected = jnp.einsum(
        "std,idc->istc", normed, w_qkv, preferred_element_type=jnp.float32
    ).astype(jnp.bfloat16)
    queries = projected[0]
    query_heads = queries.reshape(records, frames_here, head_count, HEAD_DIM)
    kv_all = ring_gather(projected[1:], "ctx")
    key_heads = kv_all[:, 0].reshape(ctx_count, records, frames_here, head_count, HEAD_DIM)
    value_heads = kv_all[:, 1].reshape(ctx_count, records, frames_here, head_count, HEAD_DIM)
    scores = (
        jnp.einsum("sqhe,cskhe->shqck", query_heads, key_heads, preferred_element_type=jnp.float32)
        * score_scale
    )
    block_rank = (ctx_rank + jnp.arange(ctx_count, dtype=jnp.int32)) % ctx_count
    positions = block_rank[:, None] * frames_here + jnp.arange(frames_here, dtype=jnp.int32)
    is_live = positions[None] < frame_counts[:, None, None]
    scores = jnp.where(is_live[:, None, None], scores, masked_score)
    row_max = jnp.max(scores, axis=(-2, -1), keepdims=True)
    weights = jnp.exp(scores - row_max)
    row_sum = jnp.sum(weights, axis=(-2, -1))
    contrib = jnp.einsum(
        "shqck,cskhe->shqe",
        weights.astype(jnp.bfloat16),
        value_heads,
        preferred_element_type=jnp.float32,
    )
    attended = (contrib / row_sum[..., None]).astype(jnp.bfloat16)
    attended = attended.transpose(0, 2, 1, 3).reshape(records, frames_here, head_count * HEAD_DIM)
    attn_part = jnp.einsum("stc,cd->std", attended, w_out, preferred_element_type=jnp.float32)
    mp_count = lax.axis_size("mp")
    mp_rank = lax.axis_index("mp")
    rows_mine = frames_here // mp_count
    row_start = mp_rank * rows_mine
    attn_mine = reduce_scatter_rows(attn_part.astype(jnp.bfloat16), "mp", 1)
    features_mine = lax.dynamic_slice_in_dim(features, row_start, rows_mine, 1)
    residual_mine = features_mine.astype(jnp.float32) + attn_mine
    normed_mine = layer_norm(residual_mine, conv_gain).astype(jnp.bfloat16)
    normed_conv = all_gather_rows(normed_mine, "mp", 1)
    gated_rows = gated_units(normed_conv, w_glu)
    frame_ids = first_frame + jnp.arange(frames_here, dtype=jnp.int32)
    frame_live = frame_ids[None, :] < frame_counts[:, None]
    gated_rows = jnp.where(frame_live[..., None], gated_rows, jnp.zeros((), jnp.bfloat16))
    rim_width = kernel.shape[0] // 2
    padded = with_halo(gated_rows, (("ctx", 1),), rim_width)
    depthwise = jnp.zeros(gated_rows.shape, jnp.float32)
    for tap_index in range(kernel.shape[0]):
        depthwise = (
            depthwise
            + padded[:, tap_index : tap_index + frames_here, :].astype(jnp.float32)
            * kernel[tap_index]
        )
    activated = jax.nn.silu(depthwise * bn_scale + bn_shift).astype(jnp.bfloat16)
    conv_part = jnp.einsum("stc,cd->std", activated, w_pw, preferred_element_type=jnp.float32)
    conv_rows = reduce_scatter_rows(conv_part.astype(jnp.bfloat16), "mp", 1)
    combined = residual_mine + conv_rows
    clip_bound = clip_level.astype(jnp.float32) / 16.0
    clipped = jnp.clip(combined, -clip_bound, clip_bound)
    mine_ids = first_frame + row_start + jnp.arange(rows_mine, dtype=jnp.int32)
    mine_live = mine_ids[None, :] < frame_counts[:, None]
    return jnp.where(mine_live[..., None], clipped, 0.0).astype(jnp.bfloat16)


def shards(features, frame_counts, *weights):
    records = features.shape[0]
    pieces = 2 if records % 2 == 0 else 1
    size = records // pieces
    outs = [
        chunk(
            features[p * size : (p + 1) * size],
            frame_counts[p * size : (p + 1) * size],
            *weights,
        )
        for p in range(pieces)
    ]
    return jnp.concatenate(outs, axis=0)


def solution(mesh):
    return jax.shard_map(
        shards,
        mesh=mesh,
        in_specs=(
            P("groups", "ctx", None),
            P("groups"),
            P(),
            P(None, None, "mp"),
            P("mp", None),
            P(),
            P(None, None, "mp"),
            P(None, "mp"),
            P("mp"),
            P("mp"),
            P("mp", None),
            P(),
        ),
        out_specs=P("groups", ("ctx", "mp"), None),
        check_vma=False,
    )
```

```python
import jax
import jax.numpy as jnp
from jax import lax
from jax.sharding import PartitionSpec as P

HEAD_DIM = 64


epsilon = 1e-05
masked_score = -1e30


def with_halo(x, sides, width):
    for axis, dim in sides:
        devices, length = (lax.axis_size(axis), x.shape[dim])
        up = [(i, (i + 1) % devices) for i in range(devices - 1)]
        down = [(j, i) for i, j in up]
        last = lax.slice_in_dim(x, length - width, length, axis=dim)
        initial = lax.slice_in_dim(x, 0, width, axis=dim)
        before = lax.ppermute(last, axis, up)
        after = lax.ppermute(initial, axis, down)
        x = jnp.concatenate([before, x, after], axis=dim)
    return x


def layer_norm(values, gain):
    centre = jnp.mean(values, axis=-1, keepdims=True)
    centred = values - centre
    variance = jnp.mean(centred * centred, axis=-1, keepdims=True)
    return centred * lax.rsqrt(variance + epsilon) * gain


def gated_units(normed, w_glu):
    halves = jnp.einsum("std,gdc->gstc", normed, w_glu, preferred_element_type=jnp.float32)
    return (halves[0] * jax.nn.sigmoid(halves[1])).astype(jnp.bfloat16)


def xor_pairs(count, mask):
    return [(i, i ^ mask) for i in range(count)]


def bit_count(count):
    bits = count.bit_length() - 1
    assert (1 << bits) == count
    return bits


def reduce_scatter_rows(x, axis, dim):
    count, rank = lax.axis_size(axis), lax.axis_index(axis)
    bits = bit_count(count)
    shape = x.shape
    block = shape[dim] // count
    acc = x.reshape(shape[:dim] + (2,) * bits + (block,) + shape[dim + 1 :])
    for b in range(bits):
        bit_axis = dim + bits - 1 - b
        mine = (rank >> b) & 1
        keep = lax.dynamic_index_in_dim(acc, mine, bit_axis, keepdims=False)
        send = lax.dynamic_index_in_dim(acc, 1 - mine, bit_axis, keepdims=False)
        got = lax.ppermute(send.astype(jnp.bfloat16), axis, xor_pairs(count, 1 << b))
        acc = keep.astype(jnp.float32) + got.astype(jnp.float32)
    return acc


def all_gather_rows(x, axis, dim):
    count, rank = lax.axis_size(axis), lax.axis_index(axis)
    bits = bit_count(count)
    shape = x.shape
    acc = x
    for k, b in enumerate(reversed(range(bits))):
        mine = ((rank >> b) & 1) == 0
        got = lax.ppermute(acc, axis, xor_pairs(count, 1 << b))
        low = jnp.where(mine, acc, got)
        high = jnp.where(mine, got, acc)
        acc = jnp.stack([low, high], axis=dim + k)
    return acc.reshape(shape[:dim] + (shape[dim] * count,) + shape[dim + 1 :])


def ring_gather(x, axis):
    count = lax.axis_size(axis)
    right = [(i, (i + 1) % count) for i in range(count)]
    left = [(i, (i - 1) % count) for i in range(count)]
    right_steps = count // 2
    left_steps = count - 1 - right_steps
    blocks = [(0, x)]
    going_right, going_left = x, x
    for step in range(right_steps):
        going_right = lax.ppermute(going_right, axis, right)
        blocks.append((count - 1 - step, going_right))
        if step < left_steps:
            going_left = lax.ppermute(going_left, axis, left)
            blocks.append((step + 1, going_left))
    return blocks


def shards(
    features,
    frame_counts,
    attn_gain,
    w_qkv,
    w_out,
    conv_gain,
    w_glu,
    kernel,
    bn_scale,
    bn_shift,
    w_pw,
    clip_level,
):
    records, frames_here, model_width = features.shape
    head_count = w_qkv.shape[2] // HEAD_DIM
    ctx_rank = lax.axis_index("ctx")
    ctx_count = lax.axis_size("ctx")
    score_scale = HEAD_DIM ** (-0.5)
    first_frame = ctx_rank * frames_here
    normed = layer_norm(features.astype(jnp.float32), attn_gain).astype(jnp.bfloat16)
    projected = jnp.einsum(
        "std,idc->istc", normed, w_qkv, preferred_element_type=jnp.float32
    ).astype(jnp.bfloat16)
    queries = projected[0]
    query_heads = queries.reshape(records, frames_here, head_count, HEAD_DIM)
    blocks = ring_gather(projected[1:], "ctx")
    frame_steps = jnp.arange(frames_here, dtype=jnp.int32)
    block_scores, block_values = [], []
    for offset, block in blocks:
        key_heads = block[0].reshape(records, frames_here, head_count, HEAD_DIM)
        block_values.append(block[1].reshape(records, frames_here, head_count, HEAD_DIM))
        scores = (
            jnp.einsum("sqhe,skhe->shqk", query_heads, key_heads, preferred_element_type=jnp.float32)
            * score_scale
        )
        block_rank = (ctx_rank + offset) % ctx_count
        positions = block_rank * frames_here + frame_steps
        is_live = positions[None, :] < frame_counts[:, None]
        block_scores.append(jnp.where(is_live[:, None, None, :], scores, masked_score))
    row_max = block_scores[0].max(axis=-1)
    for scores in block_scores[1:]:
        row_max = jnp.maximum(row_max, scores.max(axis=-1))
    row_sum = 0.0
    contrib = 0.0
    for scores, value_heads in zip(block_scores, block_values):
        weights = jnp.exp(scores - row_max[..., None])
        row_sum = row_sum + jnp.sum(weights, axis=-1)
        contrib = contrib + jnp.einsum(
            "shqk,skhe->shqe",
            weights.astype(jnp.bfloat16),
            value_heads,
            preferred_element_type=jnp.float32,
        )
    attended = (contrib / row_sum[..., None]).astype(jnp.bfloat16)
    attended = attended.transpose(0, 2, 1, 3).reshape(records, frames_here, head_count * HEAD_DIM)
    attn_part = jnp.einsum("stc,cd->std", attended, w_out, preferred_element_type=jnp.float32)
    mp_count = lax.axis_size("mp")
    mp_rank = lax.axis_index("mp")
    rows_mine = frames_here // mp_count
    row_start = mp_rank * rows_mine
    attn_mine = reduce_scatter_rows(attn_part.astype(jnp.bfloat16), "mp", 1)
    features_mine = lax.dynamic_slice_in_dim(features, row_start, rows_mine, 1)
    residual_mine = features_mine.astype(jnp.float32) + attn_mine
    normed_mine = layer_norm(residual_mine, conv_gain).astype(jnp.bfloat16)
    normed_conv = all_gather_rows(normed_mine, "mp", 1)
    gated_rows = gated_units(normed_conv, w_glu)
    frame_ids = first_frame + jnp.arange(frames_here, dtype=jnp.int32)
    frame_live = frame_ids[None, :] < frame_counts[:, None]
    gated_rows = jnp.where(frame_live[..., None], gated_rows, jnp.zeros((), jnp.bfloat16))
    rim_width = kernel.shape[0] // 2
    padded = with_halo(gated_rows, (("ctx", 1),), rim_width)
    depthwise = jnp.zeros(gated_rows.shape, jnp.float32)
    for tap_index in range(kernel.shape[0]):
        depthwise = (
            depthwise
            + padded[:, tap_index : tap_index + frames_here, :].astype(jnp.float32)
            * kernel[tap_index]
        )
    activated = jax.nn.silu(depthwise * bn_scale + bn_shift).astype(jnp.bfloat16)
    conv_part = jnp.einsum("stc,cd->std", activated, w_pw, preferred_element_type=jnp.float32)
    conv_rows = reduce_scatter_rows(conv_part.astype(jnp.bfloat16), "mp", 1)
    combined = residual_mine + conv_rows
    clip_bound = clip_level.astype(jnp.float32) / 16.0
    clipped = jnp.clip(combined, -clip_bound, clip_bound)
    mine_ids = first_frame + row_start + jnp.arange(rows_mine, dtype=jnp.int32)
    mine_live = mine_ids[None, :] < frame_counts[:, None]
    return jnp.where(mine_live[..., None], clipped, 0.0).astype(jnp.bfloat16)


def solution(mesh):
    return jax.shard_map(
        shards,
        mesh=mesh,
        in_specs=(
            P("groups", "ctx", None),
            P("groups"),
            P(),
            P(None, None, "mp"),
            P("mp", None),
            P(),
            P(None, None, "mp"),
            P(None, "mp"),
            P("mp"),
            P("mp"),
            P("mp", None),
            P(),
        ),
        out_specs=P("groups", ("ctx", "mp"), None),
        check_vma=False,
    )
```

```python
import jax
import jax.numpy as jnp
from jax import lax
from jax.sharding import PartitionSpec as P

HEAD_DIM = 64


epsilon = 1e-05
masked_score = -1e30


def with_halo(x, sides, width):
    for axis, dim in sides:
        devices, length = (lax.axis_size(axis), x.shape[dim])
        up = [(i, (i + 1) % devices) for i in range(devices - 1)]
        down = [(j, i) for i, j in up]
        last = lax.slice_in_dim(x, length - width, length, axis=dim)
        initial = lax.slice_in_dim(x, 0, width, axis=dim)
        before = lax.ppermute(last, axis, up)
        after = lax.ppermute(initial, axis, down)
        x = jnp.concatenate([before, x, after], axis=dim)
    return x


def layer_norm(values, gain):
    centre = jnp.mean(values, axis=-1, keepdims=True)
    centred = values - centre
    variance = jnp.mean(centred * centred, axis=-1, keepdims=True)
    return centred * lax.rsqrt(variance + epsilon) * gain


def gated_units(normed, w_glu):
    halves = jnp.einsum("std,gdc->gstc", normed, w_glu, preferred_element_type=jnp.float32)
    return (halves[0] * jax.nn.sigmoid(halves[1])).astype(jnp.bfloat16)


def xor_pairs(count, mask):
    return [(i, i ^ mask) for i in range(count)]


def bit_count(count):
    bits = count.bit_length() - 1
    assert (1 << bits) == count
    return bits


def reduce_scatter_rows(x, axis, dim):
    count, rank = lax.axis_size(axis), lax.axis_index(axis)
    bits = bit_count(count)
    shape = x.shape
    block = shape[dim] // count
    acc = x.reshape(shape[:dim] + (2,) * bits + (block,) + shape[dim + 1 :])
    for b in range(bits):
        bit_axis = dim + bits - 1 - b
        mine = (rank >> b) & 1
        keep = lax.dynamic_index_in_dim(acc, mine, bit_axis, keepdims=False)
        send = lax.dynamic_index_in_dim(acc, 1 - mine, bit_axis, keepdims=False)
        got = lax.ppermute(send.astype(jnp.bfloat16), axis, xor_pairs(count, 1 << b))
        acc = keep.astype(jnp.float32) + got.astype(jnp.float32)
    return acc


def all_gather_rows(x, axis, dim):
    count, rank = lax.axis_size(axis), lax.axis_index(axis)
    bits = bit_count(count)
    shape = x.shape
    acc = x
    for k, b in enumerate(reversed(range(bits))):
        mine = ((rank >> b) & 1) == 0
        got = lax.ppermute(acc, axis, xor_pairs(count, 1 << b))
        low = jnp.where(mine, acc, got)
        high = jnp.where(mine, got, acc)
        acc = jnp.stack([low, high], axis=dim + k)
    return acc.reshape(shape[:dim] + (shape[dim] * count,) + shape[dim + 1 :])


def ring_gather(x, axis):
    count = lax.axis_size(axis)
    right = [(i, (i + 1) % count) for i in range(count)]
    left = [(i, (i - 1) % count) for i in range(count)]
    right_steps = count // 2
    left_steps = count - 1 - right_steps
    from_left, from_right = [], []
    going_right, going_left = x, x
    for step in range(right_steps):
        going_right = lax.ppermute(going_right, axis, right)
        from_left.append(going_right)
        if step < left_steps:
            going_left = lax.ppermute(going_left, axis, left)
            from_right.append(going_left)
    return jnp.stack([x] + from_right + from_left[::-1], axis=0)


def shards(
    features,
    frame_counts,
    attn_gain,
    w_qkv,
    w_out,
    conv_gain,
    w_glu,
    kernel,
    bn_scale,
    bn_shift,
    w_pw,
    clip_level,
):
    records, frames_here, model_width = features.shape
    head_count = w_qkv.shape[2] // HEAD_DIM
    ctx_rank = lax.axis_index("ctx")
    ctx_count = lax.axis_size("ctx")
    score_scale = HEAD_DIM ** (-0.5)
    first_frame = ctx_rank * frames_here
    normed = layer_norm(features.astype(jnp.float32), attn_gain).astype(jnp.bfloat16)
    projected = jnp.einsum(
        "std,idc->istc", normed, w_qkv, preferred_element_type=jnp.float32
    ).astype(jnp.bfloat16)
    queries = projected[0]
    query_heads = queries.reshape(records, frames_here, head_count, HEAD_DIM)
    kv_all = ring_gather(projected[1:], "ctx")
    key_heads = kv_all[:, 0].reshape(ctx_count, records, frames_here, head_count, HEAD_DIM)
    value_heads = kv_all[:, 1].reshape(ctx_count, records, frames_here, head_count, HEAD_DIM)
    scores = (
        jnp.einsum("sqhe,cskhe->shqck", query_heads, key_heads, preferred_element_type=jnp.float32)
        * score_scale
    )
    block_rank = (ctx_rank + jnp.arange(ctx_count, dtype=jnp.int32)) % ctx_count
    positions = block_rank[:, None] * frames_here + jnp.arange(frames_here, dtype=jnp.int32)
    is_live = positions[None] < frame_counts[:, None, None]
    scores = jnp.where(is_live[:, None, None], scores, masked_score)
    row_max = jnp.max(scores, axis=(-2, -1), keepdims=True)
    weights = jnp.exp(scores - row_max)
    row_sum = jnp.sum(weights, axis=(-2, -1))
    contrib = jnp.einsum(
        "shqck,cskhe->shqe",
        weights.astype(jnp.bfloat16),
        value_heads,
        preferred_element_type=jnp.float32,
    )
    attended = (contrib / row_sum[..., None]).astype(jnp.bfloat16)
    attended = attended.transpose(0, 2, 1, 3).reshape(records, frames_here, head_count * HEAD_DIM)
    attn_part = jnp.einsum("stc,cd->std", attended, w_out, preferred_element_type=jnp.float32)
    mp_count = lax.axis_size("mp")
    mp_rank = lax.axis_index("mp")
    rows_mine = frames_here // mp_count
    row_start = mp_rank * rows_mine
    attn_mine = reduce_scatter_rows(attn_part.astype(jnp.bfloat16), "mp", 1)
    features_mine = lax.dynamic_slice_in_dim(features, row_start, rows_mine, 1)
    residual_mine = features_mine.astype(jnp.float32) + attn_mine
    normed_mine = layer_norm(residual_mine, conv_gain).astype(jnp.bfloat16)
    normed_conv = all_gather_rows(normed_mine, "mp", 1)
    rim_width = kernel.shape[0] // 2
    frame_ids = first_frame + jnp.arange(frames_here, dtype=jnp.int32)
    frame_live = (frame_ids[None, :] < frame_counts[:, None])[..., None]
    edges = jnp.concatenate(
        [normed_conv[:, :rim_width], normed_conv[:, frames_here - rim_width :]], axis=1
    )
    edge_live = jnp.concatenate(
        [frame_live[:, :rim_width], frame_live[:, frames_here - rim_width :]], axis=1
    )
    gated_edges = jnp.where(edge_live, gated_units(edges, w_glu), jnp.zeros((), jnp.bfloat16))
    ctx_up = [(i, i + 1) for i in range(ctx_count - 1)]
    ctx_down = [(j, i) for i, j in ctx_up]
    before = lax.ppermute(gated_edges[:, rim_width:], "ctx", ctx_up)
    after = lax.ppermute(gated_edges[:, :rim_width], "ctx", ctx_down)
    gated_rows = gated_units(normed_conv, w_glu)
    gated_rows = jnp.where(frame_live, gated_rows, jnp.zeros((), jnp.bfloat16))
    padded = jnp.concatenate([before, gated_rows, after], axis=1)
    depthwise = lax.conv_general_dilated(
        padded.astype(jnp.float32),
        kernel[:, None, :],
        window_strides=(1,),
        padding="VALID",
        dimension_numbers=("NWC", "WIO", "NWC"),
        feature_group_count=kernel.shape[1],
        precision=lax.Precision.HIGHEST,
    )
    activated = jax.nn.silu(depthwise * bn_scale + bn_shift).astype(jnp.bfloat16)
    conv_part = jnp.einsum("stc,cd->std", activated, w_pw, preferred_element_type=jnp.float32)
    conv_rows = reduce_scatter_rows(conv_part.astype(jnp.bfloat16), "mp", 1)
    combined = residual_mine + conv_rows
    clip_bound = clip_level.astype(jnp.float32) / 16.0
    clipped = jnp.clip(combined, -clip_bound, clip_bound)
    mine_ids = first_frame + row_start + jnp.arange(rows_mine, dtype=jnp.int32)
    mine_live = mine_ids[None, :] < frame_counts[:, None]
    return jnp.where(mine_live[..., None], clipped, 0.0).astype(jnp.bfloat16)


def solution(mesh):
    return jax.shard_map(
        shards,
        mesh=mesh,
        in_specs=(
            P("groups", "ctx", None),
            P("groups"),
            P(),
            P(None, None, "mp"),
            P("mp", None),
            P(),
            P(None, None, "mp"),
            P(None, "mp"),
            P("mp"),
            P("mp"),
            P("mp", None),
            P(),
        ),
        out_specs=P("groups", ("ctx", "mp"), None),
        check_vma=False,
    )
```

```python
import jax
import jax.numpy as jnp
import functools

from jax import lax
from jax.experimental import pallas as pl
from jax.experimental.pallas import tpu as pltpu
from jax.sharding import PartitionSpec as P

HEAD_DIM = 64


epsilon = 1e-05
masked_score = -1e30


def with_halo(x, sides, width):
    for axis, dim in sides:
        devices, length = (lax.axis_size(axis), x.shape[dim])
        up = [(i, (i + 1) % devices) for i in range(devices - 1)]
        down = [(j, i) for i, j in up]
        last = lax.slice_in_dim(x, length - width, length, axis=dim)
        initial = lax.slice_in_dim(x, 0, width, axis=dim)
        before = lax.ppermute(last, axis, up)
        after = lax.ppermute(initial, axis, down)
        x = jnp.concatenate([before, x, after], axis=dim)
    return x


def layer_norm(values, gain):
    centre = jnp.mean(values, axis=-1, keepdims=True)
    centred = values - centre
    variance = jnp.mean(centred * centred, axis=-1, keepdims=True)
    return centred * lax.rsqrt(variance + epsilon) * gain


def gated_units(normed, w_glu):
    halves = jnp.einsum("std,gdc->gstc", normed, w_glu, preferred_element_type=jnp.float32)
    return (halves[0] * jax.nn.sigmoid(halves[1])).astype(jnp.bfloat16)


def xor_pairs(count, mask):
    return [(i, i ^ mask) for i in range(count)]


def bit_count(count):
    bits = count.bit_length() - 1
    assert (1 << bits) == count
    return bits


def reduce_scatter_rows(x, axis, dim):
    count, rank = lax.axis_size(axis), lax.axis_index(axis)
    bits = bit_count(count)
    shape = x.shape
    block = shape[dim] // count
    acc = x.reshape(shape[:dim] + (2,) * bits + (block,) + shape[dim + 1 :])
    for b in range(bits):
        bit_axis = dim + bits - 1 - b
        mine = (rank >> b) & 1
        keep = lax.dynamic_index_in_dim(acc, mine, bit_axis, keepdims=False)
        send = lax.dynamic_index_in_dim(acc, 1 - mine, bit_axis, keepdims=False)
        got = lax.ppermute(send.astype(jnp.bfloat16), axis, xor_pairs(count, 1 << b))
        acc = keep.astype(jnp.float32) + got.astype(jnp.float32)
    return acc


def all_gather_rows(x, axis, dim):
    count, rank = lax.axis_size(axis), lax.axis_index(axis)
    bits = bit_count(count)
    shape = x.shape
    acc = x
    for k, b in enumerate(reversed(range(bits))):
        mine = ((rank >> b) & 1) == 0
        got = lax.ppermute(acc, axis, xor_pairs(count, 1 << b))
        low = jnp.where(mine, acc, got)
        high = jnp.where(mine, got, acc)
        acc = jnp.stack([low, high], axis=dim + k)
    return acc.reshape(shape[:dim] + (shape[dim] * count,) + shape[dim + 1 :])


def ring_gather(x, axis):
    count = lax.axis_size(axis)
    right = [(i, (i + 1) % count) for i in range(count)]
    left = [(i, (i - 1) % count) for i in range(count)]
    right_steps = count // 2
    left_steps = count - 1 - right_steps
    blocks = []
    going_right, going_left = x, x
    for step in range(right_steps):
        going_right = lax.ppermute(going_right, axis, right)
        blocks.append((count - 1 - step, going_right))
        if step < left_steps:
            going_left = lax.ppermute(going_left, axis, left)
            blocks.append((step + 1, going_left))
    return blocks


def attention_kernel(counts_ref, starts_ref, proj_ref, *refs, blocks, frames, heads):
    others, out_ref = refs[:-1], refs[-1]
    record = pl.program_id(0)
    limit = counts_ref[record]
    queries = proj_ref[0, 0]
    key_rows = jnp.concatenate([proj_ref[1, 0]] + [r[0, 0] for r in others], axis=0)
    value_rows = jnp.concatenate([proj_ref[2, 0]] + [r[1, 0] for r in others], axis=0)
    slot = lax.broadcasted_iota(jnp.int32, (1, blocks * frames), 1)
    block_of = slot // frames
    start = jnp.zeros_like(slot)
    for b in range(blocks):
        start = jnp.where(block_of == b, starts_ref[b], start)
    live = start + slot % frames < limit
    for h in range(heads):
        cols = slice(h * HEAD_DIM, (h + 1) * HEAD_DIM)
        scores = lax.dot_general(
            queries[:, cols], key_rows[:, cols], (((1,), (1,)), ((), ())),
            preferred_element_type=jnp.float32,
        ) * HEAD_DIM ** (-0.5)
        scores = jnp.where(live, scores, masked_score)
        row_max = jnp.max(scores, axis=1, keepdims=True)
        weights = jnp.exp(scores - row_max)
        row_sum = jnp.sum(weights, axis=1, keepdims=True)
        contrib = jnp.dot(weights.astype(jnp.bfloat16), value_rows[:, cols],
                          preferred_element_type=jnp.float32)
        out_ref[0, :, cols] = (contrib / row_sum).astype(out_ref.dtype)


def attention(projected, others, frame_counts, starts):
    _, records, frames, width = projected.shape
    blocks = 1 + len(others)
    heads = width // HEAD_DIM
    kernel = functools.partial(attention_kernel, blocks=blocks, frames=frames, heads=heads)
    return pl.pallas_call(
        kernel,
        out_shape=jax.ShapeDtypeStruct((records, frames, width), jnp.bfloat16),
        grid_spec=pltpu.PrefetchScalarGridSpec(
            num_scalar_prefetch=2,
            grid=(records,),
            in_specs=[pl.BlockSpec((3, 1, frames, width), lambda s, c, o: (0, s, 0, 0))]
            + [pl.BlockSpec((2, 1, frames, width), lambda s, c, o: (0, s, 0, 0)) for _ in others],
            out_specs=pl.BlockSpec((1, frames, width), lambda s, c, o: (s, 0, 0)),
        ),
    )(frame_counts, starts, projected, *others)


def shards(
    features,
    frame_counts,
    attn_gain,
    w_qkv,
    w_out,
    conv_gain,
    w_glu,
    kernel,
    bn_scale,
    bn_shift,
    w_pw,
    clip_level,
):
    records, frames_here, model_width = features.shape
    head_count = w_qkv.shape[2] // HEAD_DIM
    ctx_rank = lax.axis_index("ctx")
    ctx_count = lax.axis_size("ctx")
    score_scale = HEAD_DIM ** (-0.5)
    first_frame = ctx_rank * frames_here
    normed = layer_norm(features.astype(jnp.float32), attn_gain).astype(jnp.bfloat16)
    projected = jnp.einsum(
        "std,idc->istc", normed, w_qkv, preferred_element_type=jnp.float32
    ).astype(jnp.bfloat16)
    blocks = ring_gather(projected[1:], "ctx")
    offsets = jnp.array([0] + [offset for offset, _ in blocks], jnp.int32)
    starts = ((ctx_rank + offsets) % ctx_count) * frames_here
    attended = attention(projected, [block for _, block in blocks], frame_counts, starts)
    attn_part = jnp.einsum("stc,cd->std", attended, w_out, preferred_element_type=jnp.float32)
    mp_count = lax.axis_size("mp")
    mp_rank = lax.axis_index("mp")
    rows_mine = frames_here // mp_count
    row_start = mp_rank * rows_mine
    attn_mine = reduce_scatter_rows(attn_part.astype(jnp.bfloat16), "mp", 1)
    features_mine = lax.dynamic_slice_in_dim(features, row_start, rows_mine, 1)
    residual_mine = features_mine.astype(jnp.float32) + attn_mine
    normed_mine = layer_norm(residual_mine, conv_gain).astype(jnp.bfloat16)
    normed_conv = all_gather_rows(normed_mine, "mp", 1)
    gated_rows = gated_units(normed_conv, w_glu)
    frame_ids = first_frame + jnp.arange(frames_here, dtype=jnp.int32)
    frame_live = frame_ids[None, :] < frame_counts[:, None]
    gated_rows = jnp.where(frame_live[..., None], gated_rows, jnp.zeros((), jnp.bfloat16))
    rim_width = kernel.shape[0] // 2
    padded = with_halo(gated_rows, (("ctx", 1),), rim_width)
    depthwise = lax.conv_general_dilated(
        padded.astype(jnp.float32),
        kernel[:, None, :],
        window_strides=(1,),
        padding="VALID",
        dimension_numbers=("NWC", "WIO", "NWC"),
        feature_group_count=kernel.shape[1],
        precision=lax.Precision.HIGHEST,
    )
    activated = jax.nn.silu(depthwise * bn_scale + bn_shift).astype(jnp.bfloat16)
    conv_part = jnp.einsum("stc,cd->std", activated, w_pw, preferred_element_type=jnp.float32)
    conv_rows = reduce_scatter_rows(conv_part.astype(jnp.bfloat16), "mp", 1)
    combined = residual_mine + conv_rows
    clip_bound = clip_level.astype(jnp.float32) / 16.0
    clipped = jnp.clip(combined, -clip_bound, clip_bound)
    mine_ids = first_frame + row_start + jnp.arange(rows_mine, dtype=jnp.int32)
    mine_live = mine_ids[None, :] < frame_counts[:, None]
    return jnp.where(mine_live[..., None], clipped, 0.0).astype(jnp.bfloat16)


def solution(mesh):
    return jax.shard_map(
        shards,
        mesh=mesh,
        in_specs=(
            P("groups", "ctx", None),
            P("groups"),
            P(),
            P(None, None, "mp"),
            P("mp", None),
            P(),
            P(None, None, "mp"),
            P(None, "mp"),
            P("mp"),
            P("mp"),
            P("mp", None),
            P(),
        ),
        out_specs=P("groups", ("ctx", "mp"), None),
        check_vma=False,
    )
```

```python
import jax
import jax.numpy as jnp
from jax import lax
from jax.sharding import PartitionSpec as P

HEAD_DIM = 64


epsilon = 1e-05
masked_score = -1e30


def with_halo(x, sides, width):
    for axis, dim in sides:
        devices, length = (lax.axis_size(axis), x.shape[dim])
        up = [(i, (i + 1) % devices) for i in range(devices - 1)]
        down = [(j, i) for i, j in up]
        last = lax.slice_in_dim(x, length - width, length, axis=dim)
        initial = lax.slice_in_dim(x, 0, width, axis=dim)
        before = lax.ppermute(last, axis, up)
        after = lax.ppermute(initial, axis, down)
        x = jnp.concatenate([before, x, after], axis=dim)
    return x


def row_mean(values):
    width = values.shape[-1]
    ones = jnp.full((width, 128), 1.0 / width, jnp.float32)
    sums = jnp.einsum(
        "...d,dk->...k", values, ones, precision=lax.Precision.HIGHEST,
        preferred_element_type=jnp.float32,
    )
    return sums[..., :1]


def layer_norm(values, gain):
    centre = row_mean(values)
    centred = values - centre
    variance = row_mean(centred * centred)
    return centred * lax.rsqrt(variance + epsilon) * gain


def gated_units(normed, w_glu):
    halves = jnp.einsum("std,gdc->gstc", normed, w_glu, preferred_element_type=jnp.float32)
    return (halves[0] * jax.nn.sigmoid(halves[1])).astype(jnp.bfloat16)


def xor_pairs(count, mask):
    return [(i, i ^ mask) for i in range(count)]


def bit_count(count):
    bits = count.bit_length() - 1
    assert (1 << bits) == count
    return bits


def reduce_scatter_rows(x, axis, dim):
    count, rank = lax.axis_size(axis), lax.axis_index(axis)
    bits = bit_count(count)
    shape = x.shape
    block = shape[dim] // count
    acc = x.reshape(shape[:dim] + (2,) * bits + (block,) + shape[dim + 1 :])
    for b in range(bits):
        bit_axis = dim + bits - 1 - b
        mine = (rank >> b) & 1
        keep = lax.dynamic_index_in_dim(acc, mine, bit_axis, keepdims=False)
        send = lax.dynamic_index_in_dim(acc, 1 - mine, bit_axis, keepdims=False)
        got = lax.ppermute(send.astype(jnp.bfloat16), axis, xor_pairs(count, 1 << b))
        acc = keep.astype(jnp.float32) + got.astype(jnp.float32)
    return acc


def all_gather_rows(x, axis, dim):
    count, rank = lax.axis_size(axis), lax.axis_index(axis)
    bits = bit_count(count)
    shape = x.shape
    acc = x
    for k, b in enumerate(reversed(range(bits))):
        mine = ((rank >> b) & 1) == 0
        got = lax.ppermute(acc, axis, xor_pairs(count, 1 << b))
        low = jnp.where(mine, acc, got)
        high = jnp.where(mine, got, acc)
        acc = jnp.stack([low, high], axis=dim + k)
    return acc.reshape(shape[:dim] + (shape[dim] * count,) + shape[dim + 1 :])


def ring_gather(x, axis):
    count = lax.axis_size(axis)
    right = [(i, (i + 1) % count) for i in range(count)]
    left = [(i, (i - 1) % count) for i in range(count)]
    right_steps = count // 2
    left_steps = count - 1 - right_steps
    from_left, from_right = [], []
    going_right, going_left = x, x
    for step in range(right_steps):
        going_right = lax.ppermute(going_right, axis, right)
        from_left.append(going_right)
        if step < left_steps:
            going_left = lax.ppermute(going_left, axis, left)
            from_right.append(going_left)
    return jnp.stack([x] + from_right + from_left[::-1], axis=0)


def shards(
    features,
    frame_counts,
    attn_gain,
    w_qkv,
    w_out,
    conv_gain,
    w_glu,
    kernel,
    bn_scale,
    bn_shift,
    w_pw,
    clip_level,
):
    records, frames_here, model_width = features.shape
    head_count = w_qkv.shape[2] // HEAD_DIM
    ctx_rank = lax.axis_index("ctx")
    ctx_count = lax.axis_size("ctx")
    score_scale = HEAD_DIM ** (-0.5)
    first_frame = ctx_rank * frames_here
    normed = layer_norm(features.astype(jnp.float32), attn_gain).astype(jnp.bfloat16)
    projected = jnp.einsum(
        "std,idc->istc", normed, w_qkv, preferred_element_type=jnp.float32
    ).astype(jnp.bfloat16)
    queries = projected[0]
    query_heads = queries.reshape(records, frames_here, head_count, HEAD_DIM)
    kv_all = ring_gather(projected[1:], "ctx")
    key_heads = kv_all[:, 0].reshape(ctx_count, records, frames_here, head_count, HEAD_DIM)
    value_heads = kv_all[:, 1].reshape(ctx_count, records, frames_here, head_count, HEAD_DIM)
    scores = (
        jnp.einsum("sqhe,cskhe->shqck", query_heads, key_heads, preferred_element_type=jnp.float32)
        * score_scale
    )
    block_rank = (ctx_rank + jnp.arange(ctx_count, dtype=jnp.int32)) % ctx_count
    positions = block_rank[:, None] * frames_here + jnp.arange(frames_here, dtype=jnp.int32)
    is_live = positions[None] < frame_counts[:, None, None]
    scores = jnp.where(is_live[:, None, None], scores, masked_score)
    row_max = jnp.max(scores, axis=(-2, -1), keepdims=True)
    weights = jnp.exp(scores - row_max)
    row_sum = jnp.sum(weights, axis=(-2, -1))
    contrib = jnp.einsum(
        "shqck,cskhe->shqe",
        weights.astype(jnp.bfloat16),
        value_heads,
        preferred_element_type=jnp.float32,
    )
    attended = (contrib / row_sum[..., None]).astype(jnp.bfloat16)
    attended = attended.transpose(0, 2, 1, 3).reshape(records, frames_here, head_count * HEAD_DIM)
    attn_part = jnp.einsum("stc,cd->std", attended, w_out, preferred_element_type=jnp.float32)
    mp_count = lax.axis_size("mp")
    mp_rank = lax.axis_index("mp")
    rows_mine = frames_here // mp_count
    row_start = mp_rank * rows_mine
    attn_mine = reduce_scatter_rows(attn_part.astype(jnp.bfloat16), "mp", 1)
    features_mine = lax.dynamic_slice_in_dim(features, row_start, rows_mine, 1)
    residual_mine = features_mine.astype(jnp.float32) + attn_mine
    normed_mine = layer_norm(residual_mine, conv_gain).astype(jnp.bfloat16)
    normed_conv = all_gather_rows(normed_mine, "mp", 1)
    gated_rows = gated_units(normed_conv, w_glu)
    frame_ids = first_frame + jnp.arange(frames_here, dtype=jnp.int32)
    frame_live = frame_ids[None, :] < frame_counts[:, None]
    gated_rows = jnp.where(frame_live[..., None], gated_rows, jnp.zeros((), jnp.bfloat16))
    rim_width = kernel.shape[0] // 2
    padded = with_halo(gated_rows, (("ctx", 1),), rim_width)
    depthwise = lax.conv_general_dilated(
        padded.astype(jnp.float32),
        kernel[:, None, :],
        window_strides=(1,),
        padding="VALID",
        dimension_numbers=("NWC", "WIO", "NWC"),
        feature_group_count=kernel.shape[1],
        precision=lax.Precision.HIGHEST,
    )
    activated = jax.nn.silu(depthwise * bn_scale + bn_shift).astype(jnp.bfloat16)
    conv_part = jnp.einsum("stc,cd->std", activated, w_pw, preferred_element_type=jnp.float32)
    conv_rows = reduce_scatter_rows(conv_part.astype(jnp.bfloat16), "mp", 1)
    combined = residual_mine + conv_rows
    clip_bound = clip_level.astype(jnp.float32) / 16.0
    clipped = jnp.clip(combined, -clip_bound, clip_bound)
    mine_ids = first_frame + row_start + jnp.arange(rows_mine, dtype=jnp.int32)
    mine_live = mine_ids[None, :] < frame_counts[:, None]
    return jnp.where(mine_live[..., None], clipped, 0.0).astype(jnp.bfloat16)


def solution(mesh):
    return jax.shard_map(
        shards,
        mesh=mesh,
        in_specs=(
            P("groups", "ctx", None),
            P("groups"),
            P(),
            P(None, None, "mp"),
            P("mp", None),
            P(),
            P(None, None, "mp"),
            P(None, "mp"),
            P("mp"),
            P("mp"),
            P("mp", None),
            P(),
        ),
        out_specs=P("groups", ("ctx", "mp"), None),
        check_vma=False,
    )
```

```python
import jax
import jax.numpy as jnp
from jax import lax
from jax.sharding import PartitionSpec as P

HEAD_DIM = 64


epsilon = 1e-05
masked_score = -1e30


def with_halo(x, sides, width):
    for axis, dim in sides:
        devices, length = (lax.axis_size(axis), x.shape[dim])
        up = [(i, (i + 1) % devices) for i in range(devices - 1)]
        down = [(j, i) for i, j in up]
        last = lax.slice_in_dim(x, length - width, length, axis=dim)
        initial = lax.slice_in_dim(x, 0, width, axis=dim)
        before = lax.ppermute(last, axis, up)
        after = lax.ppermute(initial, axis, down)
        x = jnp.concatenate([before, x, after], axis=dim)
    return x


def layer_norm(values, gain):
    centre = jnp.mean(values, axis=-1, keepdims=True)
    centred = values - centre
    variance = jnp.mean(centred * centred, axis=-1, keepdims=True)
    return centred * lax.rsqrt(variance + epsilon) * gain


def gated_units(normed, w_glu):
    halves = jnp.einsum("std,gdc->gstc", normed, w_glu, preferred_element_type=jnp.float32)
    return (halves[0] * jax.nn.sigmoid(halves[1])).astype(jnp.bfloat16)


def xor_pairs(count, mask):
    return [(i, i ^ mask) for i in range(count)]


def bit_count(count):
    bits = count.bit_length() - 1
    assert (1 << bits) == count
    return bits


def reduce_scatter_rows(x, axis, dim):
    count, rank = lax.axis_size(axis), lax.axis_index(axis)
    bits = bit_count(count)
    shape = x.shape
    block = shape[dim] // count
    acc = x.reshape(shape[:dim] + (2,) * bits + (block,) + shape[dim + 1 :])
    for b in range(bits):
        bit_axis = dim + bits - 1 - b
        mine = (rank >> b) & 1
        keep = lax.dynamic_index_in_dim(acc, mine, bit_axis, keepdims=False)
        send = lax.dynamic_index_in_dim(acc, 1 - mine, bit_axis, keepdims=False)
        got = lax.ppermute(send.astype(jnp.bfloat16), axis, xor_pairs(count, 1 << b))
        acc = keep.astype(jnp.float32) + got.astype(jnp.float32)
    return acc


def all_gather_rows(x, axis, dim):
    count, rank = lax.axis_size(axis), lax.axis_index(axis)
    bits = bit_count(count)
    shape = x.shape
    acc = x
    for k, b in enumerate(reversed(range(bits))):
        mine = ((rank >> b) & 1) == 0
        got = lax.ppermute(acc, axis, xor_pairs(count, 1 << b))
        low = jnp.where(mine, acc, got)
        high = jnp.where(mine, got, acc)
        acc = jnp.stack([low, high], axis=dim + k)
    return acc.reshape(shape[:dim] + (shape[dim] * count,) + shape[dim + 1 :])


def ring_gather(x, axis):
    count = lax.axis_size(axis)
    right = [(i, (i + 1) % count) for i in range(count)]
    left = [(i, (i - 1) % count) for i in range(count)]
    right_steps = count // 2
    left_steps = count - 1 - right_steps
    from_left, from_right = [], []
    going_right, going_left = x, x
    for step in range(right_steps):
        going_right = lax.ppermute(going_right, axis, right)
        from_left.append(going_right)
        if step < left_steps:
            going_left = lax.ppermute(going_left, axis, left)
            from_right.append(going_left)
    return jnp.stack([x] + from_right + from_left[::-1], axis=0)


def attend(queries, key_rows, value_rows, positions, frame_counts):
    scores = jnp.einsum(
        "sqhe,skhe->shqk", queries, key_rows, preferred_element_type=jnp.float32
    ) * HEAD_DIM ** (-0.5)
    is_live = positions[None, :] < frame_counts[:, None]
    scores = jnp.where(is_live[:, None, None, :], scores, masked_score)
    row_max = jnp.max(scores, axis=-1, keepdims=True)
    weights = jnp.exp(scores - row_max)
    row_sum = jnp.sum(weights, axis=-1)
    contrib = jnp.einsum(
        "shqk,skhe->shqe",
        weights.astype(jnp.bfloat16),
        value_rows,
        preferred_element_type=jnp.float32,
    )
    return (contrib / row_sum[..., None]).astype(jnp.bfloat16)


def attend_by_heads(projected, frame_counts, axis):
    _, records, frames, width = projected.shape
    count, rank = lax.axis_size(axis), lax.axis_index(axis)
    group = width // HEAD_DIM // count
    split = projected.reshape(3, records, frames, count, group, HEAD_DIM)
    pieces = [lax.dynamic_index_in_dim(split, rank, 3, keepdims=False)]
    sources = [rank]
    for shift in range(1, count):
        target = (rank + shift) % count
        send = lax.dynamic_index_in_dim(split, target, 3, keepdims=False)
        pairs = [(i, (i + shift) % count) for i in range(count)]
        pieces.append(lax.ppermute(send, axis, pairs))
        sources.append((rank - shift) % count)
    every = jnp.concatenate(pieces, axis=2)
    frame_steps = jnp.arange(frames, dtype=jnp.int32)
    positions = jnp.concatenate([source * frames + frame_steps for source in sources])
    attended = attend(every[0], every[1], every[2], positions, frame_counts)
    back = [attended[:, :, :frames]]
    for shift in range(1, count):
        rows = attended[:, :, shift * frames : (shift + 1) * frames]
        pairs = [(i, (i - shift) % count) for i in range(count)]
        back.append(lax.ppermute(rows, axis, pairs))
    ordered = jnp.roll(jnp.stack(back, axis=1), rank, axis=1)
    return ordered.transpose(0, 3, 1, 2, 4).reshape(records, frames, width)


def shards(
    features,
    frame_counts,
    attn_gain,
    w_qkv,
    w_out,
    conv_gain,
    w_glu,
    kernel,
    bn_scale,
    bn_shift,
    w_pw,
    clip_level,
):
    records, frames_here, model_width = features.shape
    head_count = w_qkv.shape[2] // HEAD_DIM
    ctx_rank = lax.axis_index("ctx")
    ctx_count = lax.axis_size("ctx")
    score_scale = HEAD_DIM ** (-0.5)
    first_frame = ctx_rank * frames_here
    normed = layer_norm(features.astype(jnp.float32), attn_gain).astype(jnp.bfloat16)
    projected = jnp.einsum(
        "std,idc->istc", normed, w_qkv, preferred_element_type=jnp.float32
    ).astype(jnp.bfloat16)
    if head_count % ctx_count == 0:
        attended = attend_by_heads(projected, frame_counts, "ctx")
    else:
        query_heads = projected[0].reshape(records, frames_here, head_count, HEAD_DIM)
        kv_all = ring_gather(projected[1:], "ctx")
        key_heads = kv_all[:, 0].reshape(ctx_count, records, frames_here, head_count, HEAD_DIM)
        value_heads = kv_all[:, 1].reshape(ctx_count, records, frames_here, head_count, HEAD_DIM)
        block_rank = (ctx_rank + jnp.arange(ctx_count, dtype=jnp.int32)) % ctx_count
        positions = block_rank[:, None] * frames_here + jnp.arange(frames_here, dtype=jnp.int32)
        key_heads = key_heads.transpose(1, 0, 2, 3, 4).reshape(records, -1, head_count, HEAD_DIM)
        value_heads = value_heads.transpose(1, 0, 2, 3, 4).reshape(records, -1, head_count, HEAD_DIM)
        attended = attend(query_heads, key_heads, value_heads, positions.reshape(-1), frame_counts)
        attended = attended.transpose(0, 2, 1, 3).reshape(records, frames_here, head_count * HEAD_DIM)
    attn_part = jnp.einsum("stc,cd->std", attended, w_out, preferred_element_type=jnp.float32)
    mp_count = lax.axis_size("mp")
    mp_rank = lax.axis_index("mp")
    rows_mine = frames_here // mp_count
    row_start = mp_rank * rows_mine
    attn_mine = reduce_scatter_rows(attn_part.astype(jnp.bfloat16), "mp", 1)
    features_mine = lax.dynamic_slice_in_dim(features, row_start, rows_mine, 1)
    residual_mine = features_mine.astype(jnp.float32) + attn_mine
    normed_mine = layer_norm(residual_mine, conv_gain).astype(jnp.bfloat16)
    normed_conv = all_gather_rows(normed_mine, "mp", 1)
    gated_rows = gated_units(normed_conv, w_glu)
    frame_ids = first_frame + jnp.arange(frames_here, dtype=jnp.int32)
    frame_live = frame_ids[None, :] < frame_counts[:, None]
    gated_rows = jnp.where(frame_live[..., None], gated_rows, jnp.zeros((), jnp.bfloat16))
    rim_width = kernel.shape[0] // 2
    padded = with_halo(gated_rows, (("ctx", 1),), rim_width)
    depthwise = jnp.zeros(gated_rows.shape, jnp.float32)
    for tap_index in range(kernel.shape[0]):
        depthwise = (
            depthwise
            + padded[:, tap_index : tap_index + frames_here, :].astype(jnp.float32)
            * kernel[tap_index]
        )
    activated = jax.nn.silu(depthwise * bn_scale + bn_shift).astype(jnp.bfloat16)
    conv_part = jnp.einsum("stc,cd->std", activated, w_pw, preferred_element_type=jnp.float32)
    conv_rows = reduce_scatter_rows(conv_part.astype(jnp.bfloat16), "mp", 1)
    combined = residual_mine + conv_rows
    clip_bound = clip_level.astype(jnp.float32) / 16.0
    clipped = jnp.clip(combined, -clip_bound, clip_bound)
    mine_ids = first_frame + row_start + jnp.arange(rows_mine, dtype=jnp.int32)
    mine_live = mine_ids[None, :] < frame_counts[:, None]
    return jnp.where(mine_live[..., None], clipped, 0.0).astype(jnp.bfloat16)


def solution(mesh):
    return jax.shard_map(
        shards,
        mesh=mesh,
        in_specs=(
            P("groups", "ctx", None),
            P("groups"),
            P(),
            P(None, None, "mp"),
            P("mp", None),
            P(),
            P(None, None, "mp"),
            P(None, "mp"),
            P("mp"),
            P("mp"),
            P("mp", None),
            P(),
        ),
        out_specs=P("groups", ("ctx", "mp"), None),
        check_vma=False,
    )
```

```python
import jax
import jax.numpy as jnp
from jax import lax
from jax.sharding import PartitionSpec as P

HEAD_DIM = 64


epsilon = 1e-05
masked_score = -1e30


def with_halo(x, sides, width):
    for axis, dim in sides:
        devices, length = (lax.axis_size(axis), x.shape[dim])
        up = [(i, (i + 1) % devices) for i in range(devices - 1)]
        down = [(j, i) for i, j in up]
        last = lax.slice_in_dim(x, length - width, length, axis=dim)
        initial = lax.slice_in_dim(x, 0, width, axis=dim)
        before = lax.ppermute(last, axis, up)
        after = lax.ppermute(initial, axis, down)
        x = jnp.concatenate([before, x, after], axis=dim)
    return x


def layer_norm(values, gain):
    centre = jnp.mean(values, axis=-1, keepdims=True)
    centred = values - centre
    variance = jnp.mean(centred * centred, axis=-1, keepdims=True)
    return centred * lax.rsqrt(variance + epsilon) * gain


def gated_units(normed, w_glu):
    halves = jnp.einsum("std,gdc->gstc", normed, w_glu, preferred_element_type=jnp.float32)
    return (halves[0] * jax.nn.sigmoid(halves[1])).astype(jnp.bfloat16)


def xor_pairs(count, mask):
    return [(i, i ^ mask) for i in range(count)]


def bit_count(count):
    bits = count.bit_length() - 1
    assert (1 << bits) == count
    return bits


def reduce_scatter_rows(x, axis, dim):
    count, rank = lax.axis_size(axis), lax.axis_index(axis)
    bits = bit_count(count)
    shape = x.shape
    block = shape[dim] // count
    acc = x.reshape(shape[:dim] + (2,) * bits + (block,) + shape[dim + 1 :])
    for b in range(bits):
        bit_axis = dim + bits - 1 - b
        mine = (rank >> b) & 1
        keep = lax.dynamic_index_in_dim(acc, mine, bit_axis, keepdims=False)
        send = lax.dynamic_index_in_dim(acc, 1 - mine, bit_axis, keepdims=False)
        got = lax.ppermute(send.astype(jnp.bfloat16), axis, xor_pairs(count, 1 << b))
        acc = keep.astype(jnp.float32) + got.astype(jnp.float32)
    return acc


def all_gather_rows(x, axis, dim):
    count, rank = lax.axis_size(axis), lax.axis_index(axis)
    bits = bit_count(count)
    shape = x.shape
    acc = x
    for k, b in enumerate(reversed(range(bits))):
        mine = ((rank >> b) & 1) == 0
        got = lax.ppermute(acc, axis, xor_pairs(count, 1 << b))
        low = jnp.where(mine, acc, got)
        high = jnp.where(mine, got, acc)
        acc = jnp.stack([low, high], axis=dim + k)
    return acc.reshape(shape[:dim] + (shape[dim] * count,) + shape[dim + 1 :])


def ring_gather(x, axis):
    count = lax.axis_size(axis)
    right = [(i, (i + 1) % count) for i in range(count)]
    left = [(i, (i - 1) % count) for i in range(count)]
    right_steps = count // 2
    left_steps = count - 1 - right_steps
    from_left, from_right = [], []
    going_right, going_left = x, x
    for step in range(right_steps):
        going_right = lax.ppermute(going_right, axis, right)
        from_left.append(going_right)
        if step < left_steps:
            going_left = lax.ppermute(going_left, axis, left)
            from_right.append(going_left)
    return jnp.stack([x] + from_right + from_left[::-1], axis=0)


def attend(queries, key_rows, value_rows, positions, frame_counts):
    scores = jnp.einsum(
        "sqhe,skhe->shqk", queries, key_rows, preferred_element_type=jnp.float32
    ) * HEAD_DIM ** (-0.5)
    is_live = positions[None, :] < frame_counts[:, None]
    scores = jnp.where(is_live[:, None, None, :], scores, masked_score)
    row_max = jnp.max(scores, axis=-1, keepdims=True)
    weights = jnp.exp(scores - row_max)
    row_sum = jnp.sum(weights, axis=-1)
    contrib = jnp.einsum(
        "shqk,skhe->shqe",
        weights.astype(jnp.bfloat16),
        value_rows,
        preferred_element_type=jnp.float32,
    )
    return (contrib / row_sum[..., None]).astype(jnp.bfloat16)


def attend_by_heads(projected, frame_counts, axis):
    _, records, frames, width = projected.shape
    count = lax.axis_size(axis)
    every = lax.all_to_all(projected, axis, 3, 2, tiled=True)
    group = every.shape[-1] // HEAD_DIM
    every = every.reshape(3, records, count * frames, group, HEAD_DIM)
    positions = jnp.arange(count * frames, dtype=jnp.int32)
    attended = attend(every[0], every[1], every[2], positions, frame_counts)
    attended = attended.transpose(0, 2, 1, 3).reshape(records, count * frames, group * HEAD_DIM)
    return lax.all_to_all(attended, axis, 1, 2, tiled=True)


def shards(
    features,
    frame_counts,
    attn_gain,
    w_qkv,
    w_out,
    conv_gain,
    w_glu,
    kernel,
    bn_scale,
    bn_shift,
    w_pw,
    clip_level,
):
    records, frames_here, model_width = features.shape
    head_count = w_qkv.shape[2] // HEAD_DIM
    ctx_rank = lax.axis_index("ctx")
    ctx_count = lax.axis_size("ctx")
    score_scale = HEAD_DIM ** (-0.5)
    first_frame = ctx_rank * frames_here
    normed = layer_norm(features.astype(jnp.float32), attn_gain).astype(jnp.bfloat16)
    projected = jnp.einsum(
        "std,idc->istc", normed, w_qkv, preferred_element_type=jnp.float32
    ).astype(jnp.bfloat16)
    if head_count % ctx_count == 0:
        attended = attend_by_heads(projected, frame_counts, "ctx")
    else:
        query_heads = projected[0].reshape(records, frames_here, head_count, HEAD_DIM)
        kv_all = ring_gather(projected[1:], "ctx")
        key_heads = kv_all[:, 0].reshape(ctx_count, records, frames_here, head_count, HEAD_DIM)
        value_heads = kv_all[:, 1].reshape(ctx_count, records, frames_here, head_count, HEAD_DIM)
        block_rank = (ctx_rank + jnp.arange(ctx_count, dtype=jnp.int32)) % ctx_count
        positions = block_rank[:, None] * frames_here + jnp.arange(frames_here, dtype=jnp.int32)
        key_heads = key_heads.transpose(1, 0, 2, 3, 4).reshape(records, -1, head_count, HEAD_DIM)
        value_heads = value_heads.transpose(1, 0, 2, 3, 4).reshape(records, -1, head_count, HEAD_DIM)
        attended = attend(query_heads, key_heads, value_heads, positions.reshape(-1), frame_counts)
        attended = attended.transpose(0, 2, 1, 3).reshape(records, frames_here, head_count * HEAD_DIM)
    attn_part = jnp.einsum("stc,cd->std", attended, w_out, preferred_element_type=jnp.float32)
    mp_count = lax.axis_size("mp")
    mp_rank = lax.axis_index("mp")
    rows_mine = frames_here // mp_count
    row_start = mp_rank * rows_mine
    attn_mine = reduce_scatter_rows(attn_part.astype(jnp.bfloat16), "mp", 1)
    features_mine = lax.dynamic_slice_in_dim(features, row_start, rows_mine, 1)
    residual_mine = features_mine.astype(jnp.float32) + attn_mine
    normed_mine = layer_norm(residual_mine, conv_gain).astype(jnp.bfloat16)
    normed_conv = all_gather_rows(normed_mine, "mp", 1)
    gated_rows = gated_units(normed_conv, w_glu)
    frame_ids = first_frame + jnp.arange(frames_here, dtype=jnp.int32)
    frame_live = frame_ids[None, :] < frame_counts[:, None]
    gated_rows = jnp.where(frame_live[..., None], gated_rows, jnp.zeros((), jnp.bfloat16))
    rim_width = kernel.shape[0] // 2
    padded = with_halo(gated_rows, (("ctx", 1),), rim_width)
    depthwise = jnp.zeros(gated_rows.shape, jnp.float32)
    for tap_index in range(kernel.shape[0]):
        depthwise = (
            depthwise
            + padded[:, tap_index : tap_index + frames_here, :].astype(jnp.float32)
            * kernel[tap_index]
        )
    activated = jax.nn.silu(depthwise * bn_scale + bn_shift).astype(jnp.bfloat16)
    conv_part = jnp.einsum("stc,cd->std", activated, w_pw, preferred_element_type=jnp.float32)
    conv_rows = reduce_scatter_rows(conv_part.astype(jnp.bfloat16), "mp", 1)
    combined = residual_mine + conv_rows
    clip_bound = clip_level.astype(jnp.float32) / 16.0
    clipped = jnp.clip(combined, -clip_bound, clip_bound)
    mine_ids = first_frame + row_start + jnp.arange(rows_mine, dtype=jnp.int32)
    mine_live = mine_ids[None, :] < frame_counts[:, None]
    return jnp.where(mine_live[..., None], clipped, 0.0).astype(jnp.bfloat16)


def solution(mesh):
    return jax.shard_map(
        shards,
        mesh=mesh,
        in_specs=(
            P("groups", "ctx", None),
            P("groups"),
            P(),
            P(None, None, "mp"),
            P("mp", None),
            P(),
            P(None, None, "mp"),
            P(None, "mp"),
            P("mp"),
            P("mp"),
            P("mp", None),
            P(),
        ),
        out_specs=P("groups", ("ctx", "mp"), None),
        check_vma=False,
    )
```

```python
import jax
import jax.numpy as jnp
from jax import lax
from jax.sharding import PartitionSpec as P

HEAD_DIM = 64


epsilon = 1e-05
masked_score = -1e30


def with_halo(x, sides, width):
    for axis, dim in sides:
        devices, length = (lax.axis_size(axis), x.shape[dim])
        up = [(i, (i + 1) % devices) for i in range(devices - 1)]
        down = [(j, i) for i, j in up]
        last = lax.slice_in_dim(x, length - width, length, axis=dim)
        initial = lax.slice_in_dim(x, 0, width, axis=dim)
        before = lax.ppermute(last, axis, up)
        after = lax.ppermute(initial, axis, down)
        x = jnp.concatenate([before, x, after], axis=dim)
    return x


def layer_norm(values, gain):
    centre = jnp.mean(values, axis=-1, keepdims=True)
    centred = values - centre
    variance = jnp.mean(centred * centred, axis=-1, keepdims=True)
    return centred * lax.rsqrt(variance + epsilon) * gain


def gated_units(normed, w_glu):
    halves = jnp.einsum("std,gdc->gstc", normed, w_glu, preferred_element_type=jnp.float32)
    return (halves[0] * jax.nn.sigmoid(halves[1])).astype(jnp.bfloat16)


def xor_pairs(count, mask):
    return [(i, i ^ mask) for i in range(count)]


def bit_count(count):
    bits = count.bit_length() - 1
    assert (1 << bits) == count
    return bits


def reduce_scatter_rows(x, axis, dim):
    count, rank = lax.axis_size(axis), lax.axis_index(axis)
    bits = bit_count(count)
    shape = x.shape
    block = shape[dim] // count
    acc = x.reshape(shape[:dim] + (2,) * bits + (block,) + shape[dim + 1 :])
    for b in range(bits):
        bit_axis = dim + bits - 1 - b
        mine = (rank >> b) & 1
        keep = lax.dynamic_index_in_dim(acc, mine, bit_axis, keepdims=False)
        send = lax.dynamic_index_in_dim(acc, 1 - mine, bit_axis, keepdims=False)
        got = lax.ppermute(send.astype(jnp.bfloat16), axis, xor_pairs(count, 1 << b))
        acc = keep.astype(jnp.float32) + got.astype(jnp.float32)
    return acc


def all_gather_rows(x, axis, dim):
    count, rank = lax.axis_size(axis), lax.axis_index(axis)
    bits = bit_count(count)
    shape = x.shape
    acc = x
    for k, b in enumerate(reversed(range(bits))):
        mine = (rank >> b) & 1
        got = lax.ppermute(acc, axis, xor_pairs(count, 1 << b))
        both = jnp.zeros(acc.shape[: dim + k] + (2,) + acc.shape[dim + k :], acc.dtype)
        both = lax.dynamic_update_index_in_dim(both, acc, mine, dim + k)
        acc = lax.dynamic_update_index_in_dim(both, got, 1 - mine, dim + k)
    return acc.reshape(shape[:dim] + (shape[dim] * count,) + shape[dim + 1 :])


def ring_gather(x, axis):
    count = lax.axis_size(axis)
    right = [(i, (i + 1) % count) for i in range(count)]
    left = [(i, (i - 1) % count) for i in range(count)]
    right_steps = count // 2
    left_steps = count - 1 - right_steps
    from_left, from_right = [], []
    going_right, going_left = x, x
    for step in range(right_steps):
        going_right = lax.ppermute(going_right, axis, right)
        from_left.append(going_right)
        if step < left_steps:
            going_left = lax.ppermute(going_left, axis, left)
            from_right.append(going_left)
    return jnp.stack([x] + from_right + from_left[::-1], axis=0)


def attend(queries, key_rows, value_rows, positions, frame_counts):
    scores = jnp.einsum(
        "sqhe,skhe->shqk", queries, key_rows, preferred_element_type=jnp.float32
    ) * HEAD_DIM ** (-0.5)
    is_live = positions[None, :] < frame_counts[:, None]
    scores = jnp.where(is_live[:, None, None, :], scores, masked_score)
    row_max = jnp.max(scores, axis=-1, keepdims=True)
    weights = jnp.exp(scores - row_max)
    row_sum = jnp.sum(weights, axis=-1)
    contrib = jnp.einsum(
        "shqk,skhe->shqe",
        weights.astype(jnp.bfloat16),
        value_rows,
        preferred_element_type=jnp.float32,
    )
    return (contrib / row_sum[..., None]).astype(jnp.bfloat16)


def attend_by_heads(projected, frame_counts, axis):
    _, records, frames, width = projected.shape
    count, rank = lax.axis_size(axis), lax.axis_index(axis)
    group = width // HEAD_DIM // count
    split = projected.reshape(3, records, frames, count, group, HEAD_DIM)
    pieces = [lax.dynamic_index_in_dim(split, rank, 3, keepdims=False)]
    sources = [rank]
    for shift in range(1, count):
        target = (rank + shift) % count
        send = lax.dynamic_index_in_dim(split, target, 3, keepdims=False)
        pairs = [(i, (i + shift) % count) for i in range(count)]
        pieces.append(lax.ppermute(send, axis, pairs))
        sources.append((rank - shift) % count)
    every = jnp.concatenate(pieces, axis=2)
    frame_steps = jnp.arange(frames, dtype=jnp.int32)
    positions = jnp.concatenate([source * frames + frame_steps for source in sources])
    attended = attend(every[0], every[1], every[2], positions, frame_counts)
    back = [attended[:, :, :frames]]
    for shift in range(1, count):
        rows = attended[:, :, shift * frames : (shift + 1) * frames]
        pairs = [(i, (i - shift) % count) for i in range(count)]
        back.append(lax.ppermute(rows, axis, pairs))
    ordered = jnp.roll(jnp.stack(back, axis=1), rank, axis=1)
    return ordered.transpose(0, 3, 1, 2, 4).reshape(records, frames, width)


def shards(
    features,
    frame_counts,
    attn_gain,
    w_qkv,
    w_out,
    conv_gain,
    w_glu,
    kernel,
    bn_scale,
    bn_shift,
    w_pw,
    clip_level,
):
    records, frames_here, model_width = features.shape
    head_count = w_qkv.shape[2] // HEAD_DIM
    ctx_rank = lax.axis_index("ctx")
    ctx_count = lax.axis_size("ctx")
    score_scale = HEAD_DIM ** (-0.5)
    first_frame = ctx_rank * frames_here
    normed = layer_norm(features.astype(jnp.float32), attn_gain).astype(jnp.bfloat16)
    projected = jnp.einsum(
        "std,idc->istc", normed, w_qkv, preferred_element_type=jnp.float32
    ).astype(jnp.bfloat16)
    if head_count % ctx_count == 0:
        attended = attend_by_heads(projected, frame_counts, "ctx")
    else:
        query_heads = projected[0].reshape(records, frames_here, head_count, HEAD_DIM)
        kv_all = ring_gather(projected[1:], "ctx")
        key_heads = kv_all[:, 0].reshape(ctx_count, records, frames_here, head_count, HEAD_DIM)
        value_heads = kv_all[:, 1].reshape(ctx_count, records, frames_here, head_count, HEAD_DIM)
        block_rank = (ctx_rank + jnp.arange(ctx_count, dtype=jnp.int32)) % ctx_count
        positions = block_rank[:, None] * frames_here + jnp.arange(frames_here, dtype=jnp.int32)
        key_heads = key_heads.transpose(1, 0, 2, 3, 4).reshape(records, -1, head_count, HEAD_DIM)
        value_heads = value_heads.transpose(1, 0, 2, 3, 4).reshape(records, -1, head_count, HEAD_DIM)
        attended = attend(query_heads, key_heads, value_heads, positions.reshape(-1), frame_counts)
        attended = attended.transpose(0, 2, 1, 3).reshape(records, frames_here, head_count * HEAD_DIM)
    attn_part = jnp.einsum("stc,cd->std", attended, w_out, preferred_element_type=jnp.float32)
    mp_count = lax.axis_size("mp")
    mp_rank = lax.axis_index("mp")
    rows_mine = frames_here // mp_count
    row_start = mp_rank * rows_mine
    attn_mine = reduce_scatter_rows(attn_part.astype(jnp.bfloat16), "mp", 1)
    features_mine = lax.dynamic_slice_in_dim(features, row_start, rows_mine, 1)
    residual_mine = features_mine.astype(jnp.float32) + attn_mine
    normed_mine = layer_norm(residual_mine, conv_gain).astype(jnp.bfloat16)
    normed_conv = all_gather_rows(normed_mine, "mp", 1)
    gated_rows = gated_units(normed_conv, w_glu)
    frame_ids = first_frame + jnp.arange(frames_here, dtype=jnp.int32)
    frame_live = frame_ids[None, :] < frame_counts[:, None]
    gated_rows = jnp.where(frame_live[..., None], gated_rows, jnp.zeros((), jnp.bfloat16))
    rim_width = kernel.shape[0] // 2
    padded = with_halo(gated_rows, (("ctx", 1),), rim_width)
    depthwise = lax.conv_general_dilated(
        padded.astype(jnp.float32),
        kernel[:, None, :],
        window_strides=(1,),
        padding="VALID",
        dimension_numbers=("NWC", "WIO", "NWC"),
        feature_group_count=kernel.shape[1],
        precision=lax.Precision.HIGHEST,
    )
    activated = jax.nn.silu(depthwise * bn_scale + bn_shift).astype(jnp.bfloat16)
    conv_part = jnp.einsum("stc,cd->std", activated, w_pw, preferred_element_type=jnp.float32)
    conv_rows = reduce_scatter_rows(conv_part.astype(jnp.bfloat16), "mp", 1)
    combined = residual_mine + conv_rows
    clip_bound = clip_level.astype(jnp.float32) / 16.0
    clipped = jnp.clip(combined, -clip_bound, clip_bound)
    mine_ids = first_frame + row_start + jnp.arange(rows_mine, dtype=jnp.int32)
    mine_live = mine_ids[None, :] < frame_counts[:, None]
    return jnp.where(mine_live[..., None], clipped, 0.0).astype(jnp.bfloat16)


def solution(mesh):
    return jax.shard_map(
        shards,
        mesh=mesh,
        in_specs=(
            P("groups", "ctx", None),
            P("groups"),
            P(),
            P(None, None, "mp"),
            P("mp", None),
            P(),
            P(None, None, "mp"),
            P(None, "mp"),
            P("mp"),
            P("mp"),
            P("mp", None),
            P(),
        ),
        out_specs=P("groups", ("ctx", "mp"), None),
        check_vma=False,
    )
```

```python
import jax
import jax.numpy as jnp
from jax import lax
from jax.sharding import PartitionSpec as P

HEAD_DIM = 64


epsilon = 1e-05
masked_score = -1e30


def with_halo(x, sides, width):
    for axis, dim in sides:
        devices, length = (lax.axis_size(axis), x.shape[dim])
        up = [(i, (i + 1) % devices) for i in range(devices - 1)]
        down = [(j, i) for i, j in up]
        last = lax.slice_in_dim(x, length - width, length, axis=dim)
        initial = lax.slice_in_dim(x, 0, width, axis=dim)
        before = lax.ppermute(last, axis, up)
        after = lax.ppermute(initial, axis, down)
        x = jnp.concatenate([before, x, after], axis=dim)
    return x


def layer_norm(values, gain):
    centre = jnp.mean(values, axis=-1, keepdims=True)
    centred = values - centre
    variance = jnp.mean(centred * centred, axis=-1, keepdims=True)
    return centred * lax.rsqrt(variance + epsilon) * gain


def gated_units(normed, w_glu):
    halves = jnp.einsum("std,gdc->gstc", normed, w_glu, preferred_element_type=jnp.float32)
    return (halves[0] * jax.nn.sigmoid(halves[1])).astype(jnp.bfloat16)


def xor_pairs(count, mask):
    return [(i, i ^ mask) for i in range(count)]


def bit_count(count):
    bits = count.bit_length() - 1
    assert (1 << bits) == count
    return bits


def reduce_scatter_rows(x, axis, dim):
    count, rank = lax.axis_size(axis), lax.axis_index(axis)
    bits = bit_count(count)
    shape = x.shape
    block = shape[dim] // count
    acc = x.reshape(shape[:dim] + (2,) * bits + (block,) + shape[dim + 1 :])
    for b in range(bits):
        bit_axis = dim + bits - 1 - b
        mine = (rank >> b) & 1
        keep = lax.dynamic_index_in_dim(acc, mine, bit_axis, keepdims=False)
        send = lax.dynamic_index_in_dim(acc, 1 - mine, bit_axis, keepdims=False)
        got = lax.ppermute(send.astype(jnp.bfloat16), axis, xor_pairs(count, 1 << b))
        acc = keep.astype(jnp.float32) + got.astype(jnp.float32)
    return acc


def all_gather_rows(x, axis, dim):
    count, rank = lax.axis_size(axis), lax.axis_index(axis)
    bits = bit_count(count)
    shape = x.shape
    acc = x
    for k, b in enumerate(reversed(range(bits))):
        mine = (rank >> b) & 1
        got = lax.ppermute(acc, axis, xor_pairs(count, 1 << b))
        both = jnp.zeros(acc.shape[: dim + k] + (2,) + acc.shape[dim + k :], acc.dtype)
        both = lax.dynamic_update_index_in_dim(both, acc, mine, dim + k)
        acc = lax.dynamic_update_index_in_dim(both, got, 1 - mine, dim + k)
    return acc.reshape(shape[:dim] + (shape[dim] * count,) + shape[dim + 1 :])


def ring_gather(x, axis):
    count = lax.axis_size(axis)
    right = [(i, (i + 1) % count) for i in range(count)]
    left = [(i, (i - 1) % count) for i in range(count)]
    right_steps = count // 2
    left_steps = count - 1 - right_steps
    from_left, from_right = [], []
    going_right, going_left = x, x
    for step in range(right_steps):
        going_right = lax.ppermute(going_right, axis, right)
        from_left.append(going_right)
        if step < left_steps:
            going_left = lax.ppermute(going_left, axis, left)
            from_right.append(going_left)
    return jnp.stack([x] + from_right + from_left[::-1], axis=0)


def attend(queries, key_rows, value_rows, positions, frame_counts):
    scores = jnp.einsum(
        "sqhe,skhe->shqk", queries, key_rows, preferred_element_type=jnp.float32
    ) * HEAD_DIM ** (-0.5)
    is_live = positions[None, :] < frame_counts[:, None]
    scores = jnp.where(is_live[:, None, None, :], scores, masked_score)
    row_max = jnp.max(scores, axis=-1, keepdims=True)
    weights = jnp.exp(scores - row_max)
    row_sum = jnp.sum(weights, axis=-1)
    contrib = jnp.einsum(
        "shqk,skhe->shqe",
        weights.astype(jnp.bfloat16),
        value_rows,
        preferred_element_type=jnp.float32,
    )
    return (contrib / row_sum[..., None]).astype(jnp.bfloat16)


def attend_by_heads(projected, frame_counts, axis):
    _, records, frames, width = projected.shape
    count, rank = lax.axis_size(axis), lax.axis_index(axis)
    group = width // HEAD_DIM // count
    split = projected.reshape(3, records, frames, count, group, HEAD_DIM)
    pieces = [lax.dynamic_index_in_dim(split, rank, 3, keepdims=False)]
    sources = [rank]
    for shift in range(1, count):
        target = (rank + shift) % count
        send = lax.dynamic_index_in_dim(split, target, 3, keepdims=False)
        pairs = [(i, (i + shift) % count) for i in range(count)]
        pieces.append(lax.ppermute(send, axis, pairs))
        sources.append((rank - shift) % count)
    every = jnp.concatenate(pieces, axis=2)
    frame_steps = jnp.arange(frames, dtype=jnp.int32)
    positions = jnp.concatenate([source * frames + frame_steps for source in sources])
    attended = attend(every[0], every[1], every[2], positions, frame_counts)
    blocks = attended.reshape(records, group, count, frames, HEAD_DIM)
    natural = (rank - jnp.arange(count, dtype=jnp.int32)) % count
    return swap_blocks(jnp.take(blocks, natural, axis=2), axis).reshape(records, frames, width)


def swap_blocks(chunks, axis):
    count, rank = lax.axis_size(axis), lax.axis_index(axis)
    bits = bit_count(count)
    records, group, _, frames, depth = chunks.shape
    held = chunks.reshape((records, group) + (2,) * bits + (1, frames, depth))
    for b in range(bits):
        mine = (rank >> b) & 1
        dest_axis = 2 + bits - 1 - b
        keep = lax.dynamic_index_in_dim(held, mine, dest_axis, keepdims=False)
        send = lax.dynamic_index_in_dim(held, 1 - mine, dest_axis, keepdims=False)
        got = lax.ppermute(send, axis, xor_pairs(count, 1 << b))
        src_axis = 2 + bits - 1 - b
        both = jnp.zeros(keep.shape[:src_axis] + (2,) + keep.shape[src_axis:], keep.dtype)
        both = lax.dynamic_update_index_in_dim(both, keep, mine, src_axis)
        held = lax.dynamic_update_index_in_dim(both, got, 1 - mine, src_axis)
    held = held.reshape(records, group, count, frames, depth)
    return held.transpose(0, 3, 2, 1, 4)


def shards(
    features,
    frame_counts,
    attn_gain,
    w_qkv,
    w_out,
    conv_gain,
    w_glu,
    kernel,
    bn_scale,
    bn_shift,
    w_pw,
    clip_level,
):
    records, frames_here, model_width = features.shape
    head_count = w_qkv.shape[2] // HEAD_DIM
    ctx_rank = lax.axis_index("ctx")
    ctx_count = lax.axis_size("ctx")
    score_scale = HEAD_DIM ** (-0.5)
    first_frame = ctx_rank * frames_here
    normed = layer_norm(features.astype(jnp.float32), attn_gain).astype(jnp.bfloat16)
    projected = jnp.einsum(
        "std,idc->istc", normed, w_qkv, preferred_element_type=jnp.float32
    ).astype(jnp.bfloat16)
    if head_count % ctx_count == 0:
        attended = attend_by_heads(projected, frame_counts, "ctx")
    else:
        query_heads = projected[0].reshape(records, frames_here, head_count, HEAD_DIM)
        kv_all = ring_gather(projected[1:], "ctx")
        key_heads = kv_all[:, 0].reshape(ctx_count, records, frames_here, head_count, HEAD_DIM)
        value_heads = kv_all[:, 1].reshape(ctx_count, records, frames_here, head_count, HEAD_DIM)
        block_rank = (ctx_rank + jnp.arange(ctx_count, dtype=jnp.int32)) % ctx_count
        positions = block_rank[:, None] * frames_here + jnp.arange(frames_here, dtype=jnp.int32)
        key_heads = key_heads.transpose(1, 0, 2, 3, 4).reshape(records, -1, head_count, HEAD_DIM)
        value_heads = value_heads.transpose(1, 0, 2, 3, 4).reshape(records, -1, head_count, HEAD_DIM)
        attended = attend(query_heads, key_heads, value_heads, positions.reshape(-1), frame_counts)
        attended = attended.transpose(0, 2, 1, 3).reshape(records, frames_here, head_count * HEAD_DIM)
    attn_part = jnp.einsum("stc,cd->std", attended, w_out, preferred_element_type=jnp.float32)
    mp_count = lax.axis_size("mp")
    mp_rank = lax.axis_index("mp")
    rows_mine = frames_here // mp_count
    row_start = mp_rank * rows_mine
    attn_mine = reduce_scatter_rows(attn_part.astype(jnp.bfloat16), "mp", 1)
    features_mine = lax.dynamic_slice_in_dim(features, row_start, rows_mine, 1)
    residual_mine = features_mine.astype(jnp.float32) + attn_mine
    normed_mine = layer_norm(residual_mine, conv_gain).astype(jnp.bfloat16)
    normed_conv = all_gather_rows(normed_mine, "mp", 1)
    gated_rows = gated_units(normed_conv, w_glu)
    frame_ids = first_frame + jnp.arange(frames_here, dtype=jnp.int32)
    frame_live = frame_ids[None, :] < frame_counts[:, None]
    gated_rows = jnp.where(frame_live[..., None], gated_rows, jnp.zeros((), jnp.bfloat16))
    rim_width = kernel.shape[0] // 2
    padded = with_halo(gated_rows, (("ctx", 1),), rim_width)
    depthwise = lax.conv_general_dilated(
        padded.astype(jnp.float32),
        kernel[:, None, :],
        window_strides=(1,),
        padding="VALID",
        dimension_numbers=("NWC", "WIO", "NWC"),
        feature_group_count=kernel.shape[1],
        precision=lax.Precision.HIGHEST,
    )
    activated = jax.nn.silu(depthwise * bn_scale + bn_shift).astype(jnp.bfloat16)
    conv_part = jnp.einsum("stc,cd->std", activated, w_pw, preferred_element_type=jnp.float32)
    conv_rows = reduce_scatter_rows(conv_part.astype(jnp.bfloat16), "mp", 1)
    combined = residual_mine + conv_rows
    clip_bound = clip_level.astype(jnp.float32) / 16.0
    clipped = jnp.clip(combined, -clip_bound, clip_bound)
    mine_ids = first_frame + row_start + jnp.arange(rows_mine, dtype=jnp.int32)
    mine_live = mine_ids[None, :] < frame_counts[:, None]
    return jnp.where(mine_live[..., None], clipped, 0.0).astype(jnp.bfloat16)


def solution(mesh):
    return jax.shard_map(
        shards,
        mesh=mesh,
        in_specs=(
            P("groups", "ctx", None),
            P("groups"),
            P(),
            P(None, None, "mp"),
            P("mp", None),
            P(),
            P(None, None, "mp"),
            P(None, "mp"),
            P("mp"),
            P("mp"),
            P("mp", None),
            P(),
        ),
        out_specs=P("groups", ("ctx", "mp"), None),
        check_vma=False,
    )
```

```python
import jax
import jax.numpy as jnp
from jax import lax
from jax.sharding import PartitionSpec as P

HEAD_DIM = 64


epsilon = 1e-05
masked_score = -1e30


def with_halo(x, sides, width):
    for axis, dim in sides:
        devices, length = (lax.axis_size(axis), x.shape[dim])
        up = [(i, (i + 1) % devices) for i in range(devices - 1)]
        down = [(j, i) for i, j in up]
        last = lax.slice_in_dim(x, length - width, length, axis=dim)
        initial = lax.slice_in_dim(x, 0, width, axis=dim)
        before = lax.ppermute(last, axis, up)
        after = lax.ppermute(initial, axis, down)
        x = jnp.concatenate([before, x, after], axis=dim)
    return x


def layer_norm(values, gain):
    centre = jnp.mean(values, axis=-1, keepdims=True)
    centred = values - centre
    variance = jnp.mean(centred * centred, axis=-1, keepdims=True)
    return centred * lax.rsqrt(variance + epsilon) * gain


def gated_units(normed, w_glu):
    halves = jnp.einsum("std,gdc->gstc", normed, w_glu, preferred_element_type=jnp.float32)
    return (halves[0] * jax.nn.sigmoid(halves[1])).astype(jnp.bfloat16)


def xor_pairs(count, mask):
    return [(i, i ^ mask) for i in range(count)]


def bit_count(count):
    bits = count.bit_length() - 1
    assert (1 << bits) == count
    return bits


def reduce_scatter_rows(x, axis, dim):
    count, rank = lax.axis_size(axis), lax.axis_index(axis)
    bits = bit_count(count)
    shape = x.shape
    block = shape[dim] // count
    acc = x.reshape(shape[:dim] + (2,) * bits + (block,) + shape[dim + 1 :])
    for b in range(bits):
        bit_axis = dim + bits - 1 - b
        mine = (rank >> b) & 1
        keep = lax.dynamic_index_in_dim(acc, mine, bit_axis, keepdims=False)
        send = lax.dynamic_index_in_dim(acc, 1 - mine, bit_axis, keepdims=False)
        got = lax.ppermute(send.astype(jnp.bfloat16), axis, xor_pairs(count, 1 << b))
        acc = keep.astype(jnp.float32) + got.astype(jnp.float32)
    return acc


def all_gather_rows(x, axis, dim, rider):
    count, rank = lax.axis_size(axis), lax.axis_index(axis)
    bits = bit_count(count)
    shape = x.shape
    acc = x
    for k, b in enumerate(reversed(range(bits))):
        mine = (rank >> b) & 1
        if b == 0:
            got, rider = lax.ppermute((acc, rider), axis, xor_pairs(count, 1 << b))
        else:
            got = lax.ppermute(acc, axis, xor_pairs(count, 1 << b))
        both = jnp.zeros(acc.shape[: dim + k] + (2,) + acc.shape[dim + k :], acc.dtype)
        both = lax.dynamic_update_index_in_dim(both, acc, mine, dim + k)
        acc = lax.dynamic_update_index_in_dim(both, got, 1 - mine, dim + k)
    return acc.reshape(shape[:dim] + (shape[dim] * count,) + shape[dim + 1 :]), rider


def ring_gather(x, axis):
    count = lax.axis_size(axis)
    right = [(i, (i + 1) % count) for i in range(count)]
    left = [(i, (i - 1) % count) for i in range(count)]
    right_steps = count // 2
    left_steps = count - 1 - right_steps
    from_left, from_right = [], []
    going_right, going_left = x, x
    for step in range(right_steps):
        going_right = lax.ppermute(going_right, axis, right)
        from_left.append(going_right)
        if step < left_steps:
            going_left = lax.ppermute(going_left, axis, left)
            from_right.append(going_left)
    return jnp.stack([x] + from_right + from_left[::-1], axis=0)


def attend(queries, key_rows, value_rows, positions, frame_counts):
    scores = jnp.einsum(
        "sqhe,skhe->shqk", queries, key_rows, preferred_element_type=jnp.float32
    ) * HEAD_DIM ** (-0.5)
    is_live = positions[None, :] < frame_counts[:, None]
    scores = jnp.where(is_live[:, None, None, :], scores, masked_score)
    row_max = jnp.max(scores, axis=-1, keepdims=True)
    weights = jnp.exp(scores - row_max)
    row_sum = jnp.sum(weights, axis=-1)
    contrib = jnp.einsum(
        "shqk,skhe->shqe",
        weights.astype(jnp.bfloat16),
        value_rows,
        preferred_element_type=jnp.float32,
    )
    return (contrib / row_sum[..., None]).astype(jnp.bfloat16)


def attend_by_heads(projected, frame_counts, axis):
    _, records, frames, width = projected.shape
    count, rank = lax.axis_size(axis), lax.axis_index(axis)
    group = width // HEAD_DIM // count
    split = projected.reshape(3, records, frames, count, group, HEAD_DIM)
    pieces = [lax.dynamic_index_in_dim(split, rank, 3, keepdims=False)]
    sources = [rank]
    for shift in range(1, count):
        target = (rank + shift) % count
        send = lax.dynamic_index_in_dim(split, target, 3, keepdims=False)
        pairs = [(i, (i + shift) % count) for i in range(count)]
        pieces.append(lax.ppermute(send, axis, pairs))
        sources.append((rank - shift) % count)
    every = jnp.concatenate(pieces, axis=2)
    frame_steps = jnp.arange(frames, dtype=jnp.int32)
    positions = jnp.concatenate([source * frames + frame_steps for source in sources])
    attended = attend(every[0], every[1], every[2], positions, frame_counts)
    back = [attended[:, :, :frames]]
    for shift in range(1, count):
        rows = attended[:, :, shift * frames : (shift + 1) * frames]
        pairs = [(i, (i - shift) % count) for i in range(count)]
        back.append(lax.ppermute(rows, axis, pairs))
    ordered = jnp.roll(jnp.stack(back, axis=1), rank, axis=1)
    return ordered.transpose(0, 3, 1, 2, 4).reshape(records, frames, width)


def shards(
    features,
    frame_counts,
    attn_gain,
    w_qkv,
    w_out,
    conv_gain,
    w_glu,
    kernel,
    bn_scale,
    bn_shift,
    w_pw,
    clip_level,
):
    records, frames_here, model_width = features.shape
    head_count = w_qkv.shape[2] // HEAD_DIM
    ctx_rank = lax.axis_index("ctx")
    ctx_count = lax.axis_size("ctx")
    score_scale = HEAD_DIM ** (-0.5)
    first_frame = ctx_rank * frames_here
    normed = layer_norm(features.astype(jnp.float32), attn_gain).astype(jnp.bfloat16)
    projected = jnp.einsum(
        "std,idc->istc", normed, w_qkv, preferred_element_type=jnp.float32
    ).astype(jnp.bfloat16)
    if head_count % ctx_count == 0:
        attended = attend_by_heads(projected, frame_counts, "ctx")
    else:
        query_heads = projected[0].reshape(records, frames_here, head_count, HEAD_DIM)
        kv_all = ring_gather(projected[1:], "ctx")
        key_heads = kv_all[:, 0].reshape(ctx_count, records, frames_here, head_count, HEAD_DIM)
        value_heads = kv_all[:, 1].reshape(ctx_count, records, frames_here, head_count, HEAD_DIM)
        block_rank = (ctx_rank + jnp.arange(ctx_count, dtype=jnp.int32)) % ctx_count
        positions = block_rank[:, None] * frames_here + jnp.arange(frames_here, dtype=jnp.int32)
        key_heads = key_heads.transpose(1, 0, 2, 3, 4).reshape(records, -1, head_count, HEAD_DIM)
        value_heads = value_heads.transpose(1, 0, 2, 3, 4).reshape(records, -1, head_count, HEAD_DIM)
        attended = attend(query_heads, key_heads, value_heads, positions.reshape(-1), frame_counts)
        attended = attended.transpose(0, 2, 1, 3).reshape(records, frames_here, head_count * HEAD_DIM)
    attn_part = jnp.einsum("stc,cd->std", attended, w_out, preferred_element_type=jnp.float32)
    mp_count = lax.axis_size("mp")
    mp_rank = lax.axis_index("mp")
    rows_mine = frames_here // mp_count
    row_start = mp_rank * rows_mine
    attn_mine = reduce_scatter_rows(attn_part.astype(jnp.bfloat16), "mp", 1)
    features_mine = lax.dynamic_slice_in_dim(features, row_start, rows_mine, 1)
    residual_mine = features_mine.astype(jnp.float32) + attn_mine
    normed_mine = layer_norm(residual_mine, conv_gain).astype(jnp.bfloat16)
    rim_width = kernel.shape[0] // 2
    ctx_mp = ctx_count * mp_count
    halo_moves = []
    for pair in range(mp_count // 2):
        pairs = [((c + 1) * mp_count, c * mp_count + 2 * pair) for c in range(ctx_count - 1)]
        pairs += [
            ((c - 1) * mp_count + mp_count - 1, c * mp_count + 2 * pair + 1)
            for c in range(1, ctx_count)
        ]
        halo_moves.append(pairs)
    edge_start = jnp.where(mp_rank == 0, 0, rows_mine - rim_width)
    edge_rows = lax.dynamic_slice_in_dim(normed_mine, edge_start, rim_width, 1)
    arrived = [lax.ppermute(edge_rows, ("ctx", "mp"), pairs) for pairs in halo_moves]
    halo_piece = lax.dynamic_index_in_dim(jnp.stack(arrived), mp_rank // 2, 0, keepdims=False)
    normed_conv, halo_other = all_gather_rows(normed_mine, "mp", 1, halo_piece)
    even = (mp_rank & 1) == 0
    halo_after = jnp.where(even, halo_piece, halo_other)
    halo_before = jnp.where(even, halo_other, halo_piece)
    extended = jnp.concatenate([halo_before, normed_conv, halo_after], axis=1)
    gated_rows = gated_units(extended, w_glu)
    frame_ids = first_frame - rim_width + jnp.arange(frames_here + 2 * rim_width, dtype=jnp.int32)
    frame_live = (frame_ids[None, :] >= 0) & (frame_ids[None, :] < frame_counts[:, None])
    padded = jnp.where(frame_live[..., None], gated_rows, jnp.zeros((), jnp.bfloat16))
    depthwise = lax.conv_general_dilated(
        padded.astype(jnp.float32),
        kernel[:, None, :],
        window_strides=(1,),
        padding="VALID",
        dimension_numbers=("NWC", "WIO", "NWC"),
        feature_group_count=kernel.shape[1],
        precision=lax.Precision.HIGHEST,
    )
    activated = jax.nn.silu(depthwise * bn_scale + bn_shift).astype(jnp.bfloat16)
    conv_part = jnp.einsum("stc,cd->std", activated, w_pw, preferred_element_type=jnp.float32)
    conv_rows = reduce_scatter_rows(conv_part.astype(jnp.bfloat16), "mp", 1)
    combined = residual_mine + conv_rows
    clip_bound = clip_level.astype(jnp.float32) / 16.0
    clipped = jnp.clip(combined, -clip_bound, clip_bound)
    mine_ids = first_frame + row_start + jnp.arange(rows_mine, dtype=jnp.int32)
    mine_live = mine_ids[None, :] < frame_counts[:, None]
    return jnp.where(mine_live[..., None], clipped, 0.0).astype(jnp.bfloat16)


def solution(mesh):
    return jax.shard_map(
        shards,
        mesh=mesh,
        in_specs=(
            P("groups", "ctx", None),
            P("groups"),
            P(),
            P(None, None, "mp"),
            P("mp", None),
            P(),
            P(None, None, "mp"),
            P(None, "mp"),
            P("mp"),
            P("mp"),
            P("mp", None),
            P(),
        ),
        out_specs=P("groups", ("ctx", "mp"), None),
        check_vma=False,
    )
```

```python
import jax
import jax.numpy as jnp
from jax import lax
from jax.sharding import PartitionSpec as P

HEAD_DIM = 64


epsilon = 1e-05
masked_score = -1e30


def with_halo(x, sides, width):
    for axis, dim in sides:
        devices, length = (lax.axis_size(axis), x.shape[dim])
        up = [(i, (i + 1) % devices) for i in range(devices - 1)]
        down = [(j, i) for i, j in up]
        last = lax.slice_in_dim(x, length - width, length, axis=dim)
        initial = lax.slice_in_dim(x, 0, width, axis=dim)
        before = lax.ppermute(last, axis, up)
        after = lax.ppermute(initial, axis, down)
        x = jnp.concatenate([before, x, after], axis=dim)
    return x


def layer_norm(values, gain):
    shift = values[..., :1]
    offset = values - shift
    offset_mean = jnp.mean(offset, axis=-1, keepdims=True)
    variance = jnp.mean(offset * offset, axis=-1, keepdims=True) - offset_mean * offset_mean
    return (offset - offset_mean) * lax.rsqrt(variance + epsilon) * gain


def gated_units(normed, w_glu):
    halves = jnp.einsum("std,gdc->gstc", normed, w_glu, preferred_element_type=jnp.float32)
    return (halves[0] * jax.nn.sigmoid(halves[1])).astype(jnp.bfloat16)


def xor_pairs(count, mask):
    return [(i, i ^ mask) for i in range(count)]


def bit_count(count):
    bits = count.bit_length() - 1
    assert (1 << bits) == count
    return bits


def reduce_scatter_rows(x, axis, dim):
    count, rank = lax.axis_size(axis), lax.axis_index(axis)
    bits = bit_count(count)
    shape = x.shape
    block = shape[dim] // count
    acc = x.reshape(shape[:dim] + (2,) * bits + (block,) + shape[dim + 1 :])
    for b in range(bits):
        bit_axis = dim + bits - 1 - b
        mine = (rank >> b) & 1
        keep = lax.dynamic_index_in_dim(acc, mine, bit_axis, keepdims=False)
        send = lax.dynamic_index_in_dim(acc, 1 - mine, bit_axis, keepdims=False)
        got = lax.ppermute(send.astype(jnp.bfloat16), axis, xor_pairs(count, 1 << b))
        acc = keep.astype(jnp.float32) + got.astype(jnp.float32)
    return acc


def all_gather_rows(x, axis, dim):
    count, rank = lax.axis_size(axis), lax.axis_index(axis)
    bits = bit_count(count)
    shape = x.shape
    acc = x
    for k, b in enumerate(reversed(range(bits))):
        mine = (rank >> b) & 1
        got = lax.ppermute(acc, axis, xor_pairs(count, 1 << b))
        both = jnp.zeros(acc.shape[: dim + k] + (2,) + acc.shape[dim + k :], acc.dtype)
        both = lax.dynamic_update_index_in_dim(both, acc, mine, dim + k)
        acc = lax.dynamic_update_index_in_dim(both, got, 1 - mine, dim + k)
    return acc.reshape(shape[:dim] + (shape[dim] * count,) + shape[dim + 1 :])


def ring_gather(x, axis):
    count = lax.axis_size(axis)
    right = [(i, (i + 1) % count) for i in range(count)]
    left = [(i, (i - 1) % count) for i in range(count)]
    right_steps = count // 2
    left_steps = count - 1 - right_steps
    from_left, from_right = [], []
    going_right, going_left = x, x
    for step in range(right_steps):
        going_right = lax.ppermute(going_right, axis, right)
        from_left.append(going_right)
        if step < left_steps:
            going_left = lax.ppermute(going_left, axis, left)
            from_right.append(going_left)
    return jnp.stack([x] + from_right + from_left[::-1], axis=0)


def attend(queries, key_rows, value_rows, positions, frame_counts):
    scores = jnp.einsum(
        "sqhe,skhe->shqk", queries, key_rows, preferred_element_type=jnp.float32
    ) * HEAD_DIM ** (-0.5)
    is_live = positions[None, :] < frame_counts[:, None]
    scores = jnp.where(is_live[:, None, None, :], scores, masked_score)
    row_max = jnp.max(scores, axis=-1, keepdims=True)
    weights = jnp.exp(scores - row_max)
    row_sum = jnp.sum(weights, axis=-1)
    contrib = jnp.einsum(
        "shqk,skhe->shqe",
        weights.astype(jnp.bfloat16),
        value_rows,
        preferred_element_type=jnp.float32,
    )
    return (contrib / row_sum[..., None]).astype(jnp.bfloat16)


def attend_by_heads(projected, frame_counts, axis):
    _, records, frames, width = projected.shape
    count, rank = lax.axis_size(axis), lax.axis_index(axis)
    group = width // HEAD_DIM // count
    split = projected.reshape(3, records, frames, count, group, HEAD_DIM)
    pieces = [lax.dynamic_index_in_dim(split, rank, 3, keepdims=False)]
    sources = [rank]
    for shift in range(1, count):
        target = (rank + shift) % count
        send = lax.dynamic_index_in_dim(split, target, 3, keepdims=False)
        pairs = [(i, (i + shift) % count) for i in range(count)]
        pieces.append(lax.ppermute(send, axis, pairs))
        sources.append((rank - shift) % count)
    every = jnp.concatenate(pieces, axis=2)
    frame_steps = jnp.arange(frames, dtype=jnp.int32)
    positions = jnp.concatenate([source * frames + frame_steps for source in sources])
    attended = attend(every[0], every[1], every[2], positions, frame_counts)
    back = [attended[:, :, :frames]]
    for shift in range(1, count):
        rows = attended[:, :, shift * frames : (shift + 1) * frames]
        pairs = [(i, (i - shift) % count) for i in range(count)]
        back.append(lax.ppermute(rows, axis, pairs))
    ordered = jnp.roll(jnp.stack(back, axis=1), rank, axis=1)
    return ordered.transpose(0, 3, 1, 2, 4).reshape(records, frames, width)


def shards(
    features,
    frame_counts,
    attn_gain,
    w_qkv,
    w_out,
    conv_gain,
    w_glu,
    kernel,
    bn_scale,
    bn_shift,
    w_pw,
    clip_level,
):
    records, frames_here, model_width = features.shape
    head_count = w_qkv.shape[2] // HEAD_DIM
    ctx_rank = lax.axis_index("ctx")
    ctx_count = lax.axis_size("ctx")
    score_scale = HEAD_DIM ** (-0.5)
    first_frame = ctx_rank * frames_here
    normed = layer_norm(features.astype(jnp.float32), attn_gain).astype(jnp.bfloat16)
    projected = jnp.einsum(
        "std,idc->istc", normed, w_qkv, preferred_element_type=jnp.float32
    ).astype(jnp.bfloat16)
    if head_count % ctx_count == 0:
        attended = attend_by_heads(projected, frame_counts, "ctx")
    else:
        query_heads = projected[0].reshape(records, frames_here, head_count, HEAD_DIM)
        kv_all = ring_gather(projected[1:], "ctx")
        key_heads = kv_all[:, 0].reshape(ctx_count, records, frames_here, head_count, HEAD_DIM)
        value_heads = kv_all[:, 1].reshape(ctx_count, records, frames_here, head_count, HEAD_DIM)
        block_rank = (ctx_rank + jnp.arange(ctx_count, dtype=jnp.int32)) % ctx_count
        positions = block_rank[:, None] * frames_here + jnp.arange(frames_here, dtype=jnp.int32)
        key_heads = key_heads.transpose(1, 0, 2, 3, 4).reshape(records, -1, head_count, HEAD_DIM)
        value_heads = value_heads.transpose(1, 0, 2, 3, 4).reshape(records, -1, head_count, HEAD_DIM)
        attended = attend(query_heads, key_heads, value_heads, positions.reshape(-1), frame_counts)
        attended = attended.transpose(0, 2, 1, 3).reshape(records, frames_here, head_count * HEAD_DIM)
    attn_part = jnp.einsum("stc,cd->std", attended, w_out, preferred_element_type=jnp.float32)
    mp_count = lax.axis_size("mp")
    mp_rank = lax.axis_index("mp")
    rows_mine = frames_here // mp_count
    row_start = mp_rank * rows_mine
    attn_mine = reduce_scatter_rows(attn_part.astype(jnp.bfloat16), "mp", 1)
    features_mine = lax.dynamic_slice_in_dim(features, row_start, rows_mine, 1)
    residual_mine = features_mine.astype(jnp.float32) + attn_mine
    normed_mine = layer_norm(residual_mine, conv_gain).astype(jnp.bfloat16)
    normed_conv = all_gather_rows(normed_mine, "mp", 1)
    gated_rows = gated_units(normed_conv, w_glu)
    frame_ids = first_frame + jnp.arange(frames_here, dtype=jnp.int32)
    frame_live = frame_ids[None, :] < frame_counts[:, None]
    gated_rows = jnp.where(frame_live[..., None], gated_rows, jnp.zeros((), jnp.bfloat16))
    rim_width = kernel.shape[0] // 2
    padded = with_halo(gated_rows, (("ctx", 1),), rim_width)
    depthwise = lax.conv_general_dilated(
        padded.astype(jnp.float32),
        kernel[:, None, :],
        window_strides=(1,),
        padding="VALID",
        dimension_numbers=("NWC", "WIO", "NWC"),
        feature_group_count=kernel.shape[1],
        precision=lax.Precision.HIGHEST,
    )
    activated = jax.nn.silu(depthwise * bn_scale + bn_shift).astype(jnp.bfloat16)
    conv_part = jnp.einsum("stc,cd->std", activated, w_pw, preferred_element_type=jnp.float32)
    conv_rows = reduce_scatter_rows(conv_part.astype(jnp.bfloat16), "mp", 1)
    combined = residual_mine + conv_rows
    clip_bound = clip_level.astype(jnp.float32) / 16.0
    clipped = jnp.clip(combined, -clip_bound, clip_bound)
    mine_ids = first_frame + row_start + jnp.arange(rows_mine, dtype=jnp.int32)
    mine_live = mine_ids[None, :] < frame_counts[:, None]
    return jnp.where(mine_live[..., None], clipped, 0.0).astype(jnp.bfloat16)


def solution(mesh):
    return jax.shard_map(
        shards,
        mesh=mesh,
        in_specs=(
            P("groups", "ctx", None),
            P("groups"),
            P(),
            P(None, None, "mp"),
            P("mp", None),
            P(),
            P(None, None, "mp"),
            P(None, "mp"),
            P("mp"),
            P("mp"),
            P("mp", None),
            P(),
        ),
        out_specs=P("groups", ("ctx", "mp"), None),
        check_vma=False,
    )
```

```python
import jax
import jax.numpy as jnp
from jax import lax
from jax.sharding import PartitionSpec as P

HEAD_DIM = 64


epsilon = 1e-05
masked_score = -1e30


def with_halo(x, sides, width):
    for axis, dim in sides:
        devices, length = (lax.axis_size(axis), x.shape[dim])
        up = [(i, (i + 1) % devices) for i in range(devices - 1)]
        down = [(j, i) for i, j in up]
        last = lax.slice_in_dim(x, length - width, length, axis=dim)
        initial = lax.slice_in_dim(x, 0, width, axis=dim)
        before = lax.ppermute(last, axis, up)
        after = lax.ppermute(initial, axis, down)
        x = jnp.concatenate([before, x, after], axis=dim)
    return x


def layer_norm(values, gain):
    centre = jnp.mean(values, axis=-1, keepdims=True)
    centred = values - centre
    variance = jnp.mean(centred * centred, axis=-1, keepdims=True)
    return centred * lax.rsqrt(variance + epsilon) * gain


def gated_units(normed, w_glu):
    halves = jnp.einsum("std,gdc->gstc", normed, w_glu, preferred_element_type=jnp.float32)
    return (halves[0] * jax.nn.sigmoid(halves[1])).astype(jnp.bfloat16)


def xor_pairs(count, mask):
    return [(i, i ^ mask) for i in range(count)]


def bit_count(count):
    bits = count.bit_length() - 1
    assert (1 << bits) == count
    return bits


def reduce_scatter_rows(x, axis, dim, first_bit=0):
    count, rank = lax.axis_size(axis), lax.axis_index(axis)
    bits = bit_count(count)
    shape = x.shape
    block = shape[dim] // (count >> first_bit)
    acc = x.reshape(shape[:dim] + (2,) * (bits - first_bit) + (block,) + shape[dim + 1 :])
    for b in range(first_bit, bits):
        bit_axis = dim + bits - 1 - b
        mine = (rank >> b) & 1
        keep = lax.dynamic_index_in_dim(acc, mine, bit_axis, keepdims=False)
        send = lax.dynamic_index_in_dim(acc, 1 - mine, bit_axis, keepdims=False)
        got = lax.ppermute(send.astype(jnp.bfloat16), axis, xor_pairs(count, 1 << b))
        acc = keep.astype(jnp.float32) + got.astype(jnp.float32)
    return acc


def project_and_reduce(inputs, weights, pair_weights, axis):
    count, rank = lax.axis_size(axis), lax.axis_index(axis)
    records, frames, channels = inputs.shape
    pair_inputs = lax.ppermute(inputs, axis, xor_pairs(count, 1))
    mine = rank & 1

    def kept_rows(rows):
        rows = rows.reshape(records, count // 2, 2, frames // count, channels)
        return lax.dynamic_index_in_dim(rows, mine, 2, keepdims=False)

    part = jnp.einsum(
        "sbrc,cd->sbrd", kept_rows(inputs), weights, preferred_element_type=jnp.float32
    ) + jnp.einsum(
        "sbrc,cd->sbrd", kept_rows(pair_inputs), pair_weights, preferred_element_type=jnp.float32
    )
    part = part.astype(jnp.bfloat16).reshape(records, frames // 2, part.shape[-1])
    return reduce_scatter_rows(part, axis, 1, first_bit=1)


def all_gather_rows(x, axis, dim):
    count, rank = lax.axis_size(axis), lax.axis_index(axis)
    bits = bit_count(count)
    shape = x.shape
    acc = x
    for k, b in enumerate(reversed(range(bits))):
        mine = (rank >> b) & 1
        got = lax.ppermute(acc, axis, xor_pairs(count, 1 << b))
        both = jnp.zeros(acc.shape[: dim + k] + (2,) + acc.shape[dim + k :], acc.dtype)
        both = lax.dynamic_update_index_in_dim(both, acc, mine, dim + k)
        acc = lax.dynamic_update_index_in_dim(both, got, 1 - mine, dim + k)
    return acc.reshape(shape[:dim] + (shape[dim] * count,) + shape[dim + 1 :])


def ring_gather(x, axis):
    count = lax.axis_size(axis)
    right = [(i, (i + 1) % count) for i in range(count)]
    left = [(i, (i - 1) % count) for i in range(count)]
    right_steps = count // 2
    left_steps = count - 1 - right_steps
    from_left, from_right = [], []
    going_right, going_left = x, x
    for step in range(right_steps):
        going_right = lax.ppermute(going_right, axis, right)
        from_left.append(going_right)
        if step < left_steps:
            going_left = lax.ppermute(going_left, axis, left)
            from_right.append(going_left)
    return jnp.stack([x] + from_right + from_left[::-1], axis=0)


def attend(queries, key_rows, value_rows, positions, frame_counts):
    scores = jnp.einsum(
        "sqhe,skhe->shqk", queries, key_rows, preferred_element_type=jnp.float32
    ) * HEAD_DIM ** (-0.5)
    is_live = positions[None, :] < frame_counts[:, None]
    scores = jnp.where(is_live[:, None, None, :], scores, masked_score)
    row_max = jnp.max(scores, axis=-1, keepdims=True)
    weights = jnp.exp(scores - row_max)
    row_sum = jnp.sum(weights, axis=-1)
    contrib = jnp.einsum(
        "shqk,skhe->shqe",
        weights.astype(jnp.bfloat16),
        value_rows,
        preferred_element_type=jnp.float32,
    )
    return (contrib / row_sum[..., None]).astype(jnp.bfloat16)


def attend_by_heads(projected, frame_counts, axis):
    _, records, frames, width = projected.shape
    count, rank = lax.axis_size(axis), lax.axis_index(axis)
    group = width // HEAD_DIM // count
    split = projected.reshape(3, records, frames, count, group, HEAD_DIM)
    pieces = [lax.dynamic_index_in_dim(split, rank, 3, keepdims=False)]
    sources = [rank]
    for shift in range(1, count):
        target = (rank + shift) % count
        send = lax.dynamic_index_in_dim(split, target, 3, keepdims=False)
        pairs = [(i, (i + shift) % count) for i in range(count)]
        pieces.append(lax.ppermute(send, axis, pairs))
        sources.append((rank - shift) % count)
    every = jnp.concatenate(pieces, axis=2)
    frame_steps = jnp.arange(frames, dtype=jnp.int32)
    positions = jnp.concatenate([source * frames + frame_steps for source in sources])
    attended = attend(every[0], every[1], every[2], positions, frame_counts)
    back = [attended[:, :, :frames]]
    for shift in range(1, count):
        rows = attended[:, :, shift * frames : (shift + 1) * frames]
        pairs = [(i, (i - shift) % count) for i in range(count)]
        back.append(lax.ppermute(rows, axis, pairs))
    ordered = jnp.roll(jnp.stack(back, axis=1), rank, axis=1)
    return ordered.transpose(0, 3, 1, 2, 4).reshape(records, frames, width)


def shards(
    features,
    frame_counts,
    attn_gain,
    w_qkv,
    w_out,
    conv_gain,
    w_glu,
    kernel,
    bn_scale,
    bn_shift,
    w_pw,
    clip_level,
):
    records, frames_here, model_width = features.shape
    head_count = w_qkv.shape[2] // HEAD_DIM
    ctx_rank = lax.axis_index("ctx")
    ctx_count = lax.axis_size("ctx")
    score_scale = HEAD_DIM ** (-0.5)
    first_frame = ctx_rank * frames_here
    normed = layer_norm(features.astype(jnp.float32), attn_gain).astype(jnp.bfloat16)
    projected = jnp.einsum(
        "std,idc->istc", normed, w_qkv, preferred_element_type=jnp.float32
    ).astype(jnp.bfloat16)
    if head_count % ctx_count == 0:
        attended = attend_by_heads(projected, frame_counts, "ctx")
    else:
        query_heads = projected[0].reshape(records, frames_here, head_count, HEAD_DIM)
        kv_all = ring_gather(projected[1:], "ctx")
        key_heads = kv_all[:, 0].reshape(ctx_count, records, frames_here, head_count, HEAD_DIM)
        value_heads = kv_all[:, 1].reshape(ctx_count, records, frames_here, head_count, HEAD_DIM)
        block_rank = (ctx_rank + jnp.arange(ctx_count, dtype=jnp.int32)) % ctx_count
        positions = block_rank[:, None] * frames_here + jnp.arange(frames_here, dtype=jnp.int32)
        key_heads = key_heads.transpose(1, 0, 2, 3, 4).reshape(records, -1, head_count, HEAD_DIM)
        value_heads = value_heads.transpose(1, 0, 2, 3, 4).reshape(records, -1, head_count, HEAD_DIM)
        attended = attend(query_heads, key_heads, value_heads, positions.reshape(-1), frame_counts)
        attended = attended.transpose(0, 2, 1, 3).reshape(records, frames_here, head_count * HEAD_DIM)
    w_out_pair = lax.ppermute(w_out, "mp", xor_pairs(lax.axis_size("mp"), 1))
    w_pw_pair = lax.ppermute(w_pw, "mp", xor_pairs(lax.axis_size("mp"), 1))
    mp_count = lax.axis_size("mp")
    mp_rank = lax.axis_index("mp")
    rows_mine = frames_here // mp_count
    row_start = mp_rank * rows_mine
    attn_mine = project_and_reduce(attended, w_out, w_out_pair, "mp")
    features_mine = lax.dynamic_slice_in_dim(features, row_start, rows_mine, 1)
    residual_mine = features_mine.astype(jnp.float32) + attn_mine
    normed_mine = layer_norm(residual_mine, conv_gain).astype(jnp.bfloat16)
    normed_conv = all_gather_rows(normed_mine, "mp", 1)
    gated_rows = gated_units(normed_conv, w_glu)
    frame_ids = first_frame + jnp.arange(frames_here, dtype=jnp.int32)
    frame_live = frame_ids[None, :] < frame_counts[:, None]
    gated_rows = jnp.where(frame_live[..., None], gated_rows, jnp.zeros((), jnp.bfloat16))
    rim_width = kernel.shape[0] // 2
    padded = with_halo(gated_rows, (("ctx", 1),), rim_width)
    depthwise = lax.conv_general_dilated(
        padded.astype(jnp.float32),
        kernel[:, None, :],
        window_strides=(1,),
        padding="VALID",
        dimension_numbers=("NWC", "WIO", "NWC"),
        feature_group_count=kernel.shape[1],
        precision=lax.Precision.HIGHEST,
    )
    activated = jax.nn.silu(depthwise * bn_scale + bn_shift).astype(jnp.bfloat16)
    conv_rows = project_and_reduce(activated, w_pw, w_pw_pair, "mp")
    combined = residual_mine + conv_rows
    clip_bound = clip_level.astype(jnp.float32) / 16.0
    clipped = jnp.clip(combined, -clip_bound, clip_bound)
    mine_ids = first_frame + row_start + jnp.arange(rows_mine, dtype=jnp.int32)
    mine_live = mine_ids[None, :] < frame_counts[:, None]
    return jnp.where(mine_live[..., None], clipped, 0.0).astype(jnp.bfloat16)


def solution(mesh):
    return jax.shard_map(
        shards,
        mesh=mesh,
        in_specs=(
            P("groups", "ctx", None),
            P("groups"),
            P(),
            P(None, None, "mp"),
            P("mp", None),
            P(),
            P(None, None, "mp"),
            P(None, "mp"),
            P("mp"),
            P("mp"),
            P("mp", None),
            P(),
        ),
        out_specs=P("groups", ("ctx", "mp"), None),
        check_vma=False,
    )
```

```python
import jax
import jax.numpy as jnp
from jax import lax
from jax.sharding import PartitionSpec as P

HEAD_DIM = 64


epsilon = 1e-05
masked_score = -1e30


def with_halo(x, sides, width):
    for axis, dim in sides:
        devices, length = (lax.axis_size(axis), x.shape[dim])
        up = [(i, (i + 1) % devices) for i in range(devices - 1)]
        down = [(j, i) for i, j in up]
        last = lax.slice_in_dim(x, length - width, length, axis=dim)
        initial = lax.slice_in_dim(x, 0, width, axis=dim)
        before = lax.ppermute(last, axis, up)
        after = lax.ppermute(initial, axis, down)
        x = jnp.concatenate([before, x, after], axis=dim)
    return x


def layer_norm(values, gain):
    centre = jnp.mean(values, axis=-1, keepdims=True)
    centred = values - centre
    variance = jnp.mean(centred * centred, axis=-1, keepdims=True)
    return centred * lax.rsqrt(variance + epsilon) * gain


def gated_units(normed, w_glu):
    halves = jnp.einsum("std,gdc->gstc", normed, w_glu, preferred_element_type=jnp.float32)
    return (halves[0] * jax.nn.sigmoid(halves[1])).astype(jnp.bfloat16)


def xor_pairs(count, mask):
    return [(i, i ^ mask) for i in range(count)]


def bit_count(count):
    bits = count.bit_length() - 1
    assert (1 << bits) == count
    return bits


def reduce_scatter_rows(x, axis, dim, first_bit=0):
    count, rank = lax.axis_size(axis), lax.axis_index(axis)
    bits = bit_count(count)
    shape = x.shape
    block = shape[dim] // (count >> first_bit)
    acc = x.reshape(shape[:dim] + (2,) * (bits - first_bit) + (block,) + shape[dim + 1 :])
    for b in range(first_bit, bits):
        bit_axis = dim + bits - 1 - b
        mine = (rank >> b) & 1
        keep = lax.dynamic_index_in_dim(acc, mine, bit_axis, keepdims=False)
        send = lax.dynamic_index_in_dim(acc, 1 - mine, bit_axis, keepdims=False)
        got = lax.ppermute(send.astype(jnp.bfloat16), axis, xor_pairs(count, 1 << b))
        acc = keep.astype(jnp.float32) + got.astype(jnp.float32)
    return acc


def project_and_reduce(inputs, weights, pair_weights, axis):
    count, rank = lax.axis_size(axis), lax.axis_index(axis)
    records, frames, channels = inputs.shape
    pair_inputs = lax.ppermute(inputs, axis, xor_pairs(count, 1))
    mine = rank & 1

    part = jnp.einsum(
        "src,cd->srd", inputs, weights, preferred_element_type=jnp.float32
    ) + jnp.einsum(
        "src,cd->srd", pair_inputs, pair_weights, preferred_element_type=jnp.float32
    )
    part = part.astype(jnp.bfloat16).reshape(records, count // 2, 2, frames // count, -1)
    part = lax.dynamic_index_in_dim(part, mine, 2, keepdims=False)
    part = part.reshape(records, frames // 2, part.shape[-1])
    return reduce_scatter_rows(part, axis, 1, first_bit=1)


def all_gather_rows(x, axis, dim):
    count, rank = lax.axis_size(axis), lax.axis_index(axis)
    bits = bit_count(count)
    shape = x.shape
    acc = x
    for k, b in enumerate(reversed(range(bits))):
        mine = (rank >> b) & 1
        got = lax.ppermute(acc, axis, xor_pairs(count, 1 << b))
        both = jnp.zeros(acc.shape[: dim + k] + (2,) + acc.shape[dim + k :], acc.dtype)
        both = lax.dynamic_update_index_in_dim(both, acc, mine, dim + k)
        acc = lax.dynamic_update_index_in_dim(both, got, 1 - mine, dim + k)
    return acc.reshape(shape[:dim] + (shape[dim] * count,) + shape[dim + 1 :])


def ring_gather(x, axis):
    count = lax.axis_size(axis)
    right = [(i, (i + 1) % count) for i in range(count)]
    left = [(i, (i - 1) % count) for i in range(count)]
    right_steps = count // 2
    left_steps = count - 1 - right_steps
    from_left, from_right = [], []
    going_right, going_left = x, x
    for step in range(right_steps):
        going_right = lax.ppermute(going_right, axis, right)
        from_left.append(going_right)
        if step < left_steps:
            going_left = lax.ppermute(going_left, axis, left)
            from_right.append(going_left)
    return jnp.stack([x] + from_right + from_left[::-1], axis=0)


def attend(queries, key_rows, value_rows, positions, frame_counts):
    scores = jnp.einsum(
        "sqhe,skhe->shqk", queries, key_rows, preferred_element_type=jnp.float32
    ) * HEAD_DIM ** (-0.5)
    is_live = positions[None, :] < frame_counts[:, None]
    scores = jnp.where(is_live[:, None, None, :], scores, masked_score)
    row_max = jnp.max(scores, axis=-1, keepdims=True)
    weights = jnp.exp(scores - row_max)
    row_sum = jnp.sum(weights, axis=-1)
    contrib = jnp.einsum(
        "shqk,skhe->shqe",
        weights.astype(jnp.bfloat16),
        value_rows,
        preferred_element_type=jnp.float32,
    )
    return (contrib / row_sum[..., None]).astype(jnp.bfloat16)


def attend_by_heads(projected, frame_counts, axis):
    _, records, frames, width = projected.shape
    count, rank = lax.axis_size(axis), lax.axis_index(axis)
    group = width // HEAD_DIM // count
    split = projected.reshape(3, records, frames, count, group, HEAD_DIM)
    pieces = [lax.dynamic_index_in_dim(split, rank, 3, keepdims=False)]
    sources = [rank]
    for shift in range(1, count):
        target = (rank + shift) % count
        send = lax.dynamic_index_in_dim(split, target, 3, keepdims=False)
        pairs = [(i, (i + shift) % count) for i in range(count)]
        pieces.append(lax.ppermute(send, axis, pairs))
        sources.append((rank - shift) % count)
    every = jnp.concatenate(pieces, axis=2)
    frame_steps = jnp.arange(frames, dtype=jnp.int32)
    positions = jnp.concatenate([source * frames + frame_steps for source in sources])
    attended = attend(every[0], every[1], every[2], positions, frame_counts)
    back = [attended[:, :, :frames]]
    for shift in range(1, count):
        rows = attended[:, :, shift * frames : (shift + 1) * frames]
        pairs = [(i, (i - shift) % count) for i in range(count)]
        back.append(lax.ppermute(rows, axis, pairs))
    ordered = jnp.roll(jnp.stack(back, axis=1), rank, axis=1)
    return ordered.transpose(0, 3, 1, 2, 4).reshape(records, frames, width)


def shards(
    features,
    frame_counts,
    attn_gain,
    w_qkv,
    w_out,
    conv_gain,
    w_glu,
    kernel,
    bn_scale,
    bn_shift,
    w_pw,
    clip_level,
):
    records, frames_here, model_width = features.shape
    head_count = w_qkv.shape[2] // HEAD_DIM
    ctx_rank = lax.axis_index("ctx")
    ctx_count = lax.axis_size("ctx")
    score_scale = HEAD_DIM ** (-0.5)
    first_frame = ctx_rank * frames_here
    normed = layer_norm(features.astype(jnp.float32), attn_gain).astype(jnp.bfloat16)
    projected = jnp.einsum(
        "std,idc->istc", normed, w_qkv, preferred_element_type=jnp.float32
    ).astype(jnp.bfloat16)
    if head_count % ctx_count == 0:
        attended = attend_by_heads(projected, frame_counts, "ctx")
    else:
        query_heads = projected[0].reshape(records, frames_here, head_count, HEAD_DIM)
        kv_all = ring_gather(projected[1:], "ctx")
        key_heads = kv_all[:, 0].reshape(ctx_count, records, frames_here, head_count, HEAD_DIM)
        value_heads = kv_all[:, 1].reshape(ctx_count, records, frames_here, head_count, HEAD_DIM)
        block_rank = (ctx_rank + jnp.arange(ctx_count, dtype=jnp.int32)) % ctx_count
        positions = block_rank[:, None] * frames_here + jnp.arange(frames_here, dtype=jnp.int32)
        key_heads = key_heads.transpose(1, 0, 2, 3, 4).reshape(records, -1, head_count, HEAD_DIM)
        value_heads = value_heads.transpose(1, 0, 2, 3, 4).reshape(records, -1, head_count, HEAD_DIM)
        attended = attend(query_heads, key_heads, value_heads, positions.reshape(-1), frame_counts)
        attended = attended.transpose(0, 2, 1, 3).reshape(records, frames_here, head_count * HEAD_DIM)
    w_out_pair = lax.ppermute(w_out, "mp", xor_pairs(lax.axis_size("mp"), 1))
    w_pw_pair = lax.ppermute(w_pw, "mp", xor_pairs(lax.axis_size("mp"), 1))
    mp_count = lax.axis_size("mp")
    mp_rank = lax.axis_index("mp")
    rows_mine = frames_here // mp_count
    row_start = mp_rank * rows_mine
    attn_mine = project_and_reduce(attended, w_out, w_out_pair, "mp")
    features_mine = lax.dynamic_slice_in_dim(features, row_start, rows_mine, 1)
    residual_mine = features_mine.astype(jnp.float32) + attn_mine
    normed_mine = layer_norm(residual_mine, conv_gain).astype(jnp.bfloat16)
    normed_conv = all_gather_rows(normed_mine, "mp", 1)
    gated_rows = gated_units(normed_conv, w_glu)
    frame_ids = first_frame + jnp.arange(frames_here, dtype=jnp.int32)
    frame_live = frame_ids[None, :] < frame_counts[:, None]
    gated_rows = jnp.where(frame_live[..., None], gated_rows, jnp.zeros((), jnp.bfloat16))
    rim_width = kernel.shape[0] // 2
    padded = with_halo(gated_rows, (("ctx", 1),), rim_width)
    depthwise = lax.conv_general_dilated(
        padded.astype(jnp.float32),
        kernel[:, None, :],
        window_strides=(1,),
        padding="VALID",
        dimension_numbers=("NWC", "WIO", "NWC"),
        feature_group_count=kernel.shape[1],
        precision=lax.Precision.HIGHEST,
    )
    activated = jax.nn.silu(depthwise * bn_scale + bn_shift).astype(jnp.bfloat16)
    conv_rows = project_and_reduce(activated, w_pw, w_pw_pair, "mp")
    combined = residual_mine + conv_rows
    clip_bound = clip_level.astype(jnp.float32) / 16.0
    clipped = jnp.clip(combined, -clip_bound, clip_bound)
    mine_ids = first_frame + row_start + jnp.arange(rows_mine, dtype=jnp.int32)
    mine_live = mine_ids[None, :] < frame_counts[:, None]
    return jnp.where(mine_live[..., None], clipped, 0.0).astype(jnp.bfloat16)


def solution(mesh):
    return jax.shard_map(
        shards,
        mesh=mesh,
        in_specs=(
            P("groups", "ctx", None),
            P("groups"),
            P(),
            P(None, None, "mp"),
            P("mp", None),
            P(),
            P(None, None, "mp"),
            P(None, "mp"),
            P("mp"),
            P("mp"),
            P("mp", None),
            P(),
        ),
        out_specs=P("groups", ("ctx", "mp"), None),
        check_vma=False,
    )
```

```python
import jax
import jax.numpy as jnp
from jax import lax
from jax.sharding import PartitionSpec as P

HEAD_DIM = 64


epsilon = 1e-05
masked_score = -1e30


def with_halo(x, sides, width):
    for axis, dim in sides:
        devices, length = (lax.axis_size(axis), x.shape[dim])
        up = [(i, (i + 1) % devices) for i in range(devices - 1)]
        down = [(j, i) for i, j in up]
        last = lax.slice_in_dim(x, length - width, length, axis=dim)
        initial = lax.slice_in_dim(x, 0, width, axis=dim)
        before = lax.ppermute(last, axis, up)
        after = lax.ppermute(initial, axis, down)
        x = jnp.concatenate([before, x, after], axis=dim)
    return x


def layer_norm(values, gain):
    centre = jnp.mean(values, axis=-1, keepdims=True)
    centred = values - centre
    variance = jnp.mean(centred * centred, axis=-1, keepdims=True)
    return centred * lax.rsqrt(variance + epsilon) * gain


def gated_units(normed, w_glu):
    halves = jnp.einsum("std,gdc->gstc", normed, w_glu, preferred_element_type=jnp.float32)
    return (halves[0] * jax.nn.sigmoid(halves[1])).astype(jnp.bfloat16)


def xor_pairs(count, mask):
    return [(i, i ^ mask) for i in range(count)]


def bit_count(count):
    bits = count.bit_length() - 1
    assert (1 << bits) == count
    return bits


def reduce_scatter_rows(x, axis, dim):
    count, rank = lax.axis_size(axis), lax.axis_index(axis)
    bits = bit_count(count)
    shape = x.shape
    block = shape[dim] // count
    parts = [x.reshape(shape[:dim] + (2,) * bits + (block,) + shape[dim + 1 :])]
    for b in range(bits):
        bit_axis = dim + bits - 1 - b
        mine = (rank >> b) & 1
        keep = [lax.dynamic_index_in_dim(p, mine, bit_axis, keepdims=False) for p in parts]
        send = [lax.dynamic_index_in_dim(p, 1 - mine, bit_axis, keepdims=False) for p in parts]
        send = sum(p.astype(jnp.float32) for p in send) if len(send) > 1 else send[0]
        got = lax.ppermute(send.astype(jnp.bfloat16), axis, xor_pairs(count, 1 << b))
        parts = keep + [got]
    return sum(p.astype(jnp.float32) for p in parts)


def all_gather_rows(x, axis, dim):
    count, rank = lax.axis_size(axis), lax.axis_index(axis)
    bits = bit_count(count)
    shape = x.shape
    acc = x
    for k, b in enumerate(reversed(range(bits))):
        mine = (rank >> b) & 1
        got = lax.ppermute(acc, axis, xor_pairs(count, 1 << b))
        both = jnp.zeros(acc.shape[: dim + k] + (2,) + acc.shape[dim + k :], acc.dtype)
        both = lax.dynamic_update_index_in_dim(both, acc, mine, dim + k)
        acc = lax.dynamic_update_index_in_dim(both, got, 1 - mine, dim + k)
    return acc.reshape(shape[:dim] + (shape[dim] * count,) + shape[dim + 1 :])


def ring_gather(x, axis):
    count = lax.axis_size(axis)
    right = [(i, (i + 1) % count) for i in range(count)]
    left = [(i, (i - 1) % count) for i in range(count)]
    right_steps = count // 2
    left_steps = count - 1 - right_steps
    from_left, from_right = [], []
    going_right, going_left = x, x
    for step in range(right_steps):
        going_right = lax.ppermute(going_right, axis, right)
        from_left.append(going_right)
        if step < left_steps:
            going_left = lax.ppermute(going_left, axis, left)
            from_right.append(going_left)
    return jnp.stack([x] + from_right + from_left[::-1], axis=0)


def attend(queries, key_rows, value_rows, positions, frame_counts):
    scores = jnp.einsum(
        "sqhe,skhe->shqk", queries, key_rows, preferred_element_type=jnp.float32
    ) * HEAD_DIM ** (-0.5)
    is_live = positions[None, :] < frame_counts[:, None]
    scores = jnp.where(is_live[:, None, None, :], scores, masked_score)
    row_max = jnp.max(scores, axis=-1, keepdims=True)
    weights = jnp.exp(scores - row_max)
    row_sum = jnp.sum(weights, axis=-1)
    contrib = jnp.einsum(
        "shqk,skhe->shqe",
        weights.astype(jnp.bfloat16),
        value_rows,
        preferred_element_type=jnp.float32,
    )
    return (contrib / row_sum[..., None]).astype(jnp.bfloat16)


def attend_by_heads(projected, frame_counts, axis):
    _, records, frames, width = projected.shape
    count, rank = lax.axis_size(axis), lax.axis_index(axis)
    group = width // HEAD_DIM // count
    split = projected.reshape(3, records, frames, count, group, HEAD_DIM)
    pieces = [lax.dynamic_index_in_dim(split, rank, 3, keepdims=False)]
    sources = [rank]
    for shift in range(1, count):
        target = (rank + shift) % count
        send = lax.dynamic_index_in_dim(split, target, 3, keepdims=False)
        pairs = [(i, (i + shift) % count) for i in range(count)]
        pieces.append(lax.ppermute(send, axis, pairs))
        sources.append((rank - shift) % count)
    every = jnp.concatenate(pieces, axis=2)
    frame_steps = jnp.arange(frames, dtype=jnp.int32)
    positions = jnp.concatenate([source * frames + frame_steps for source in sources])
    attended = attend(every[0], every[1], every[2], positions, frame_counts)
    back = [attended[:, :, :frames]]
    for shift in range(1, count):
        rows = attended[:, :, shift * frames : (shift + 1) * frames]
        pairs = [(i, (i - shift) % count) for i in range(count)]
        back.append(lax.ppermute(rows, axis, pairs))
    ordered = jnp.roll(jnp.stack(back, axis=1), rank, axis=1)
    return ordered.transpose(0, 3, 1, 2, 4).reshape(records, frames, width)


def shards(
    features,
    frame_counts,
    attn_gain,
    w_qkv,
    w_out,
    conv_gain,
    w_glu,
    kernel,
    bn_scale,
    bn_shift,
    w_pw,
    clip_level,
):
    records, frames_here, model_width = features.shape
    head_count = w_qkv.shape[2] // HEAD_DIM
    ctx_rank = lax.axis_index("ctx")
    ctx_count = lax.axis_size("ctx")
    score_scale = HEAD_DIM ** (-0.5)
    first_frame = ctx_rank * frames_here
    normed = layer_norm(features.astype(jnp.float32), attn_gain).astype(jnp.bfloat16)
    projected = jnp.einsum(
        "std,idc->istc", normed, w_qkv, preferred_element_type=jnp.float32
    ).astype(jnp.bfloat16)
    if head_count % ctx_count == 0:
        attended = attend_by_heads(projected, frame_counts, "ctx")
    else:
        query_heads = projected[0].reshape(records, frames_here, head_count, HEAD_DIM)
        kv_all = ring_gather(projected[1:], "ctx")
        key_heads = kv_all[:, 0].reshape(ctx_count, records, frames_here, head_count, HEAD_DIM)
        value_heads = kv_all[:, 1].reshape(ctx_count, records, frames_here, head_count, HEAD_DIM)
        block_rank = (ctx_rank + jnp.arange(ctx_count, dtype=jnp.int32)) % ctx_count
        positions = block_rank[:, None] * frames_here + jnp.arange(frames_here, dtype=jnp.int32)
        key_heads = key_heads.transpose(1, 0, 2, 3, 4).reshape(records, -1, head_count, HEAD_DIM)
        value_heads = value_heads.transpose(1, 0, 2, 3, 4).reshape(records, -1, head_count, HEAD_DIM)
        attended = attend(query_heads, key_heads, value_heads, positions.reshape(-1), frame_counts)
        attended = attended.transpose(0, 2, 1, 3).reshape(records, frames_here, head_count * HEAD_DIM)
    attn_part = jnp.einsum("stc,cd->std", attended, w_out, preferred_element_type=jnp.float32)
    mp_count = lax.axis_size("mp")
    mp_rank = lax.axis_index("mp")
    rows_mine = frames_here // mp_count
    row_start = mp_rank * rows_mine
    attn_mine = reduce_scatter_rows(attn_part.astype(jnp.bfloat16), "mp", 1)
    features_mine = lax.dynamic_slice_in_dim(features, row_start, rows_mine, 1)
    residual_mine = features_mine.astype(jnp.float32) + attn_mine
    normed_mine = layer_norm(residual_mine, conv_gain).astype(jnp.bfloat16)
    normed_conv = all_gather_rows(normed_mine, "mp", 1)
    gated_rows = gated_units(normed_conv, w_glu)
    frame_ids = first_frame + jnp.arange(frames_here, dtype=jnp.int32)
    frame_live = frame_ids[None, :] < frame_counts[:, None]
    gated_rows = jnp.where(frame_live[..., None], gated_rows, jnp.zeros((), jnp.bfloat16))
    rim_width = kernel.shape[0] // 2
    padded = with_halo(gated_rows, (("ctx", 1),), rim_width)
    depthwise = lax.conv_general_dilated(
        padded.astype(jnp.float32),
        kernel[:, None, :],
        window_strides=(1,),
        padding="VALID",
        dimension_numbers=("NWC", "WIO", "NWC"),
        feature_group_count=kernel.shape[1],
        precision=lax.Precision.HIGHEST,
    )
    activated = jax.nn.silu(depthwise * bn_scale + bn_shift).astype(jnp.bfloat16)
    conv_part = jnp.einsum("stc,cd->std", activated, w_pw, preferred_element_type=jnp.float32)
    conv_rows = reduce_scatter_rows(conv_part.astype(jnp.bfloat16), "mp", 1)
    combined = residual_mine + conv_rows
    clip_bound = clip_level.astype(jnp.float32) / 16.0
    clipped = jnp.clip(combined, -clip_bound, clip_bound)
    mine_ids = first_frame + row_start + jnp.arange(rows_mine, dtype=jnp.int32)
    mine_live = mine_ids[None, :] < frame_counts[:, None]
    return jnp.where(mine_live[..., None], clipped, 0.0).astype(jnp.bfloat16)


def solution(mesh):
    return jax.shard_map(
        shards,
        mesh=mesh,
        in_specs=(
            P("groups", "ctx", None),
            P("groups"),
            P(),
            P(None, None, "mp"),
            P("mp", None),
            P(),
            P(None, None, "mp"),
            P(None, "mp"),
            P("mp"),
            P("mp"),
            P("mp", None),
            P(),
        ),
        out_specs=P("groups", ("ctx", "mp"), None),
        check_vma=False,
    )
```

```python
import jax
import jax.numpy as jnp
from jax import lax
from jax.sharding import PartitionSpec as P

HEAD_DIM = 64


epsilon = 1e-05
masked_score = -1e30


def with_halo(x, sides, width):
    for axis, dim in sides:
        devices, length = (lax.axis_size(axis), x.shape[dim])
        up = [(i, (i + 1) % devices) for i in range(devices - 1)]
        down = [(j, i) for i, j in up]
        last = lax.slice_in_dim(x, length - width, length, axis=dim)
        initial = lax.slice_in_dim(x, 0, width, axis=dim)
        before = lax.ppermute(last, axis, up)
        after = lax.ppermute(initial, axis, down)
        x = jnp.concatenate([before, x, after], axis=dim)
    return x


def layer_norm(values, gain):
    centre = jnp.mean(values, axis=-1, keepdims=True)
    centred = values - centre
    variance = jnp.mean(centred * centred, axis=-1, keepdims=True)
    return centred * lax.rsqrt(variance + epsilon) * gain


def gated_units(normed, w_glu):
    halves = jnp.einsum("std,gdc->gstc", normed, w_glu, preferred_element_type=jnp.float32)
    return (halves[0] * jax.nn.sigmoid(halves[1])).astype(jnp.bfloat16)


def xor_pairs(count, mask):
    return [(i, i ^ mask) for i in range(count)]


def bit_count(count):
    bits = count.bit_length() - 1
    assert (1 << bits) == count
    return bits


def reduce_scatter_rows(x, axis, dim):
    count, rank = lax.axis_size(axis), lax.axis_index(axis)
    bits = bit_count(count)
    shape = x.shape
    block = shape[dim] // count
    acc = x.reshape(shape[:dim] + (2,) * bits + (block,) + shape[dim + 1 :])
    for b in range(bits):
        bit_axis = dim + bits - 1 - b
        mine = (rank >> b) & 1
        keep = lax.dynamic_index_in_dim(acc, mine, bit_axis, keepdims=False)
        send = lax.dynamic_index_in_dim(acc, 1 - mine, bit_axis, keepdims=False)
        got = lax.ppermute(send.astype(jnp.bfloat16), axis, xor_pairs(count, 1 << b))
        acc = keep.astype(jnp.float32) + got.astype(jnp.float32)
    return acc


def all_gather_rows(x, axis, dim):
    count, rank = lax.axis_size(axis), lax.axis_index(axis)
    bits = bit_count(count)
    shape = x.shape
    acc = x
    for k, b in enumerate(reversed(range(bits))):
        mine = (rank >> b) & 1
        got = lax.ppermute(acc, axis, xor_pairs(count, 1 << b))
        both = jnp.zeros(acc.shape[: dim + k] + (2,) + acc.shape[dim + k :], acc.dtype)
        both = lax.dynamic_update_index_in_dim(both, acc, mine, dim + k)
        acc = lax.dynamic_update_index_in_dim(both, got, 1 - mine, dim + k)
    return acc.reshape(shape[:dim] + (shape[dim] * count,) + shape[dim + 1 :])


def ring_gather(x, axis):
    count = lax.axis_size(axis)
    right = [(i, (i + 1) % count) for i in range(count)]
    left = [(i, (i - 1) % count) for i in range(count)]
    right_steps = count // 2
    left_steps = count - 1 - right_steps
    from_left, from_right = [], []
    going_right, going_left = x, x
    for step in range(right_steps):
        going_right = lax.ppermute(going_right, axis, right)
        from_left.append(going_right)
        if step < left_steps:
            going_left = lax.ppermute(going_left, axis, left)
            from_right.append(going_left)
    return jnp.stack([x] + from_right + from_left[::-1], axis=0)


def attend(queries, key_rows, value_rows, positions, frame_counts):
    scores = jnp.einsum(
        "sqhe,skhe->shqk", queries, key_rows, preferred_element_type=jnp.float32
    ) * HEAD_DIM ** (-0.5)
    is_live = positions[None, :] < frame_counts[:, None]
    scores = jnp.where(is_live[:, None, None, :], scores, masked_score)
    row_max = jnp.max(scores, axis=-1, keepdims=True)
    weights = jnp.exp(scores - row_max)
    row_sum = jnp.sum(weights, axis=-1)
    contrib = jnp.einsum(
        "shqk,skhe->shqe",
        weights.astype(jnp.bfloat16),
        value_rows,
        preferred_element_type=jnp.float32,
    )
    return (contrib / row_sum[..., None]).astype(jnp.bfloat16)


def attend_by_heads(projected, frame_counts, axis):
    _, records, frames, width = projected.shape
    count, rank = lax.axis_size(axis), lax.axis_index(axis)
    group = width // HEAD_DIM // count
    split = projected.reshape(3, records, frames, count, group, HEAD_DIM)
    pieces = [lax.dynamic_index_in_dim(split, rank, 3, keepdims=False)]
    sources = [rank]
    for shift in range(1, count):
        target = (rank + shift) % count
        send = lax.dynamic_index_in_dim(split, target, 3, keepdims=False)
        pairs = [(i, (i + shift) % count) for i in range(count)]
        pieces.append(lax.ppermute(send, axis, pairs))
        sources.append((rank - shift) % count)
    every = jnp.concatenate(pieces, axis=2)
    frame_steps = jnp.arange(frames, dtype=jnp.int32)
    positions = jnp.concatenate([source * frames + frame_steps for source in sources])
    attended = attend(every[0], every[1], every[2], positions, frame_counts)
    back = [attended[:, :, :frames]]
    for shift in range(1, count):
        rows = attended[:, :, shift * frames : (shift + 1) * frames]
        pairs = [(i, (i - shift) % count) for i in range(count)]
        back.append(lax.ppermute(rows, axis, pairs))
    ordered = jnp.roll(jnp.stack(back, axis=1), rank, axis=1)
    return ordered.transpose(0, 3, 1, 2, 4).reshape(records, frames, width)


def shards(
    features,
    frame_counts,
    attn_gain,
    w_qkv,
    w_out,
    conv_gain,
    w_glu,
    kernel,
    bn_scale,
    bn_shift,
    w_pw,
    clip_level,
):
    records, frames_here, model_width = features.shape
    head_count = w_qkv.shape[2] // HEAD_DIM
    ctx_rank = lax.axis_index("ctx")
    ctx_count = lax.axis_size("ctx")
    score_scale = HEAD_DIM ** (-0.5)
    first_frame = ctx_rank * frames_here
    normed = layer_norm(features.astype(jnp.float32), attn_gain).astype(jnp.bfloat16)
    projected = jnp.einsum(
        "std,idc->istc", normed, w_qkv, preferred_element_type=jnp.float32
    ).astype(jnp.bfloat16)
    if head_count % ctx_count == 0 and ctx_count > 4:
        attended = attend_by_heads(projected, frame_counts, "ctx")
    else:
        query_heads = projected[0].reshape(records, frames_here, head_count, HEAD_DIM)
        kv_all = ring_gather(projected[1:], "ctx")
        key_heads = kv_all[:, 0].reshape(ctx_count, records, frames_here, head_count, HEAD_DIM)
        value_heads = kv_all[:, 1].reshape(ctx_count, records, frames_here, head_count, HEAD_DIM)
        block_rank = (ctx_rank + jnp.arange(ctx_count, dtype=jnp.int32)) % ctx_count
        positions = block_rank[:, None] * frames_here + jnp.arange(frames_here, dtype=jnp.int32)
        key_heads = key_heads.transpose(1, 0, 2, 3, 4).reshape(records, -1, head_count, HEAD_DIM)
        value_heads = value_heads.transpose(1, 0, 2, 3, 4).reshape(records, -1, head_count, HEAD_DIM)
        attended = attend(query_heads, key_heads, value_heads, positions.reshape(-1), frame_counts)
        attended = attended.transpose(0, 2, 1, 3).reshape(records, frames_here, head_count * HEAD_DIM)
    attn_part = jnp.einsum("stc,cd->std", attended, w_out, preferred_element_type=jnp.float32)
    mp_count = lax.axis_size("mp")
    mp_rank = lax.axis_index("mp")
    rows_mine = frames_here // mp_count
    row_start = mp_rank * rows_mine
    attn_mine = reduce_scatter_rows(attn_part.astype(jnp.bfloat16), "mp", 1)
    features_mine = lax.dynamic_slice_in_dim(features, row_start, rows_mine, 1)
    residual_mine = features_mine.astype(jnp.float32) + attn_mine
    normed_mine = layer_norm(residual_mine, conv_gain).astype(jnp.bfloat16)
    normed_conv = all_gather_rows(normed_mine, "mp", 1)
    gated_rows = gated_units(normed_conv, w_glu)
    frame_ids = first_frame + jnp.arange(frames_here, dtype=jnp.int32)
    frame_live = frame_ids[None, :] < frame_counts[:, None]
    gated_rows = jnp.where(frame_live[..., None], gated_rows, jnp.zeros((), jnp.bfloat16))
    rim_width = kernel.shape[0] // 2
    padded = with_halo(gated_rows, (("ctx", 1),), rim_width)
    depthwise = lax.conv_general_dilated(
        padded.astype(jnp.float32),
        kernel[:, None, :],
        window_strides=(1,),
        padding="VALID",
        dimension_numbers=("NWC", "WIO", "NWC"),
        feature_group_count=kernel.shape[1],
        precision=lax.Precision.HIGHEST,
    )
    activated = jax.nn.silu(depthwise * bn_scale + bn_shift).astype(jnp.bfloat16)
    conv_part = jnp.einsum("stc,cd->std", activated, w_pw, preferred_element_type=jnp.float32)
    conv_rows = reduce_scatter_rows(conv_part.astype(jnp.bfloat16), "mp", 1)
    combined = residual_mine + conv_rows
    clip_bound = clip_level.astype(jnp.float32) / 16.0
    clipped = jnp.clip(combined, -clip_bound, clip_bound)
    mine_ids = first_frame + row_start + jnp.arange(rows_mine, dtype=jnp.int32)
    mine_live = mine_ids[None, :] < frame_counts[:, None]
    return jnp.where(mine_live[..., None], clipped, 0.0).astype(jnp.bfloat16)


def solution(mesh):
    return jax.shard_map(
        shards,
        mesh=mesh,
        in_specs=(
            P("groups", "ctx", None),
            P("groups"),
            P(),
            P(None, None, "mp"),
            P("mp", None),
            P(),
            P(None, None, "mp"),
            P(None, "mp"),
            P("mp"),
            P("mp"),
            P("mp", None),
            P(),
        ),
        out_specs=P("groups", ("ctx", "mp"), None),
        check_vma=False,
    )
```

```python
import jax
import jax.numpy as jnp
from jax import lax
from jax.sharding import PartitionSpec as P

HEAD_DIM = 64


epsilon = 1e-05
masked_score = -1e30


def with_halo(x, sides, width):
    for axis, dim in sides:
        devices, length = (lax.axis_size(axis), x.shape[dim])
        up = [(i, (i + 1) % devices) for i in range(devices - 1)]
        down = [(j, i) for i, j in up]
        last = lax.slice_in_dim(x, length - width, length, axis=dim)
        initial = lax.slice_in_dim(x, 0, width, axis=dim)
        before = lax.ppermute(last, axis, up)
        after = lax.ppermute(initial, axis, down)
        x = jnp.concatenate([before, x, after], axis=dim)
    return x


def layer_norm(values, gain):
    centre = jnp.mean(values, axis=-1, keepdims=True)
    centred = values - centre
    variance = jnp.mean(centred * centred, axis=-1, keepdims=True)
    return centred * lax.rsqrt(variance + epsilon) * gain


def gated_units(normed, w_glu):
    halves = jnp.einsum("std,gdc->gstc", normed, w_glu, preferred_element_type=jnp.float32)
    return (halves[0] * jax.nn.sigmoid(halves[1])).astype(jnp.bfloat16)


def xor_pairs(count, mask):
    return [(i, i ^ mask) for i in range(count)]


def bit_count(count):
    bits = count.bit_length() - 1
    assert (1 << bits) == count
    return bits


def reduce_scatter_rows(x, axis, dim):
    count, rank = lax.axis_size(axis), lax.axis_index(axis)
    bits = bit_count(count)
    shape = x.shape
    block = shape[dim] // count
    acc = x.reshape(shape[:dim] + (2,) * bits + (block,) + shape[dim + 1 :])
    for b in range(bits):
        bit_axis = dim + bits - 1 - b
        mine = (rank >> b) & 1
        keep = lax.dynamic_index_in_dim(acc, mine, bit_axis, keepdims=False)
        send = lax.dynamic_index_in_dim(acc, 1 - mine, bit_axis, keepdims=False)
        got = lax.ppermute(send.astype(jnp.bfloat16), axis, xor_pairs(count, 1 << b))
        acc = keep.astype(jnp.float32) + got.astype(jnp.float32)
    return acc


def all_gather_rows(x, axis, dim):
    count, rank = lax.axis_size(axis), lax.axis_index(axis)
    bits = bit_count(count)
    shape = x.shape
    acc = x
    for k, b in enumerate(reversed(range(bits))):
        mine = (rank >> b) & 1
        got = lax.ppermute(acc, axis, xor_pairs(count, 1 << b))
        both = jnp.zeros(acc.shape[: dim + k] + (2,) + acc.shape[dim + k :], acc.dtype)
        both = lax.dynamic_update_index_in_dim(both, acc, mine, dim + k)
        acc = lax.dynamic_update_index_in_dim(both, got, 1 - mine, dim + k)
    return acc.reshape(shape[:dim] + (shape[dim] * count,) + shape[dim + 1 :])


def ring_gather(x, axis):
    count = lax.axis_size(axis)
    right = [(i, (i + 1) % count) for i in range(count)]
    left = [(i, (i - 1) % count) for i in range(count)]
    right_steps = count // 2
    left_steps = count - 1 - right_steps
    from_left, from_right = [], []
    going_right, going_left = x, x
    for step in range(right_steps):
        going_right = lax.ppermute(going_right, axis, right)
        from_left.append(going_right)
        if step < left_steps:
            going_left = lax.ppermute(going_left, axis, left)
            from_right.append(going_left)
    return jnp.stack([x] + from_right + from_left[::-1], axis=0)


def attend(queries, key_rows, value_rows, positions, frame_counts):
    scores = jnp.einsum(
        "sqhe,skhe->shqk", queries, key_rows, preferred_element_type=jnp.float32
    ) * HEAD_DIM ** (-0.5)
    is_live = positions[None, :] < frame_counts[:, None]
    scores = jnp.where(is_live[:, None, None, :], scores, masked_score)
    row_max = jnp.max(scores, axis=-1, keepdims=True)
    weights = jnp.exp(scores - row_max)
    row_sum = jnp.sum(weights, axis=-1)
    contrib = jnp.einsum(
        "shqk,skhe->shqe",
        weights.astype(jnp.bfloat16),
        value_rows,
        preferred_element_type=jnp.float32,
    )
    return (contrib / row_sum[..., None]).astype(jnp.bfloat16)


def attend_by_heads(projected, frame_counts, axis):
    _, records, frames, width = projected.shape
    count, rank = lax.axis_size(axis), lax.axis_index(axis)
    group = width // HEAD_DIM // count
    split = projected.reshape(3, records, frames, count, group, HEAD_DIM)
    pieces = [lax.dynamic_index_in_dim(split, rank, 3, keepdims=False)]
    sources = [rank]
    for shift in range(1, count):
        target = (rank + shift) % count
        send = lax.dynamic_index_in_dim(split, target, 3, keepdims=False)
        pairs = [(i, (i + shift) % count) for i in range(count)]
        pieces.append(lax.ppermute(send, axis, pairs))
        sources.append((rank - shift) % count)
    every = jnp.concatenate(pieces, axis=2)
    frame_steps = jnp.arange(frames, dtype=jnp.int32)
    positions = jnp.concatenate([source * frames + frame_steps for source in sources])
    attended = attend(every[0], every[1], every[2], positions, frame_counts)
    back = [attended[:, :, :frames]]
    for shift in range(1, count):
        rows = attended[:, :, shift * frames : (shift + 1) * frames]
        pairs = [(i, (i - shift) % count) for i in range(count)]
        back.append(lax.ppermute(rows, axis, pairs))
    ordered = jnp.roll(jnp.stack(back, axis=1), rank, axis=1)
    return ordered.transpose(0, 3, 1, 2, 4).reshape(records, frames, width)


def shards(
    features,
    frame_counts,
    attn_gain,
    w_qkv,
    w_out,
    conv_gain,
    w_glu,
    kernel,
    bn_scale,
    bn_shift,
    w_pw,
    clip_level,
):
    records, frames_here, model_width = features.shape
    head_count = w_qkv.shape[2] // HEAD_DIM
    ctx_rank = lax.axis_index("ctx")
    ctx_count = lax.axis_size("ctx")
    score_scale = HEAD_DIM ** (-0.5)
    first_frame = ctx_rank * frames_here
    normed = layer_norm(features.astype(jnp.float32), attn_gain).astype(jnp.bfloat16)
    projected = jnp.einsum(
        "std,idc->istc", normed, w_qkv, preferred_element_type=jnp.float32
    ).astype(jnp.bfloat16)
    if head_count % ctx_count == 0:
        attended = attend_by_heads(projected, frame_counts, "ctx")
    else:
        query_heads = projected[0].reshape(records, frames_here, head_count, HEAD_DIM)
        kv_all = ring_gather(projected[1:], "ctx")
        key_heads = kv_all[:, 0].reshape(ctx_count, records, frames_here, head_count, HEAD_DIM)
        value_heads = kv_all[:, 1].reshape(ctx_count, records, frames_here, head_count, HEAD_DIM)
        block_rank = (ctx_rank + jnp.arange(ctx_count, dtype=jnp.int32)) % ctx_count
        positions = block_rank[:, None] * frames_here + jnp.arange(frames_here, dtype=jnp.int32)
        key_heads = key_heads.transpose(1, 0, 2, 3, 4).reshape(records, -1, head_count, HEAD_DIM)
        value_heads = value_heads.transpose(1, 0, 2, 3, 4).reshape(records, -1, head_count, HEAD_DIM)
        attended = attend(query_heads, key_heads, value_heads, positions.reshape(-1), frame_counts)
        attended = attended.transpose(0, 2, 1, 3).reshape(records, frames_here, head_count * HEAD_DIM)
    attn_part = jnp.einsum("stc,cd->std", attended, w_out, preferred_element_type=jnp.float32)
    mp_count = lax.axis_size("mp")
    mp_rank = lax.axis_index("mp")
    rows_mine = frames_here // mp_count
    row_start = mp_rank * rows_mine
    attn_mine = reduce_scatter_rows(attn_part.astype(jnp.bfloat16), "mp", 1)
    features_mine = lax.dynamic_slice_in_dim(features, row_start, rows_mine, 1)
    residual_mine = features_mine.astype(jnp.float32) + attn_mine
    normed_mine = layer_norm(residual_mine, conv_gain).astype(jnp.bfloat16)
    normed_conv = all_gather_rows(normed_mine, "mp", 1)
    gated_rows = gated_units(normed_conv, w_glu)
    frame_ids = first_frame + jnp.arange(frames_here, dtype=jnp.int32)
    frame_live = frame_ids[None, :] < frame_counts[:, None]
    gated_rows = jnp.where(frame_live[..., None], gated_rows, jnp.zeros((), jnp.bfloat16))
    rim_width = kernel.shape[0] // 2
    ctx_up = [(i, i + 1) for i in range(ctx_count - 1)]
    ctx_down = [(j, i) for i, j in ctx_up]
    before = lax.ppermute(gated_rows[:, frames_here - rim_width :], "ctx", ctx_up)
    after = lax.ppermute(gated_rows[:, :rim_width], "ctx", ctx_down)

    def depthwise_of(rows):
        return lax.conv_general_dilated(
            rows.astype(jnp.float32),
            kernel[:, None, :],
            window_strides=(1,),
            padding="VALID",
            dimension_numbers=("NWC", "WIO", "NWC"),
            feature_group_count=kernel.shape[1],
            precision=lax.Precision.HIGHEST,
        )

    middle = depthwise_of(gated_rows)
    low = depthwise_of(jnp.concatenate([before, gated_rows[:, : 2 * rim_width]], axis=1))
    high = depthwise_of(jnp.concatenate([gated_rows[:, frames_here - 2 * rim_width :], after], axis=1))
    depthwise = jnp.concatenate([low, middle, high], axis=1)
    activated = jax.nn.silu(depthwise * bn_scale + bn_shift).astype(jnp.bfloat16)
    conv_part = jnp.einsum("stc,cd->std", activated, w_pw, preferred_element_type=jnp.float32)
    conv_rows = reduce_scatter_rows(conv_part.astype(jnp.bfloat16), "mp", 1)
    combined = residual_mine + conv_rows
    clip_bound = clip_level.astype(jnp.float32) / 16.0
    clipped = jnp.clip(combined, -clip_bound, clip_bound)
    mine_ids = first_frame + row_start + jnp.arange(rows_mine, dtype=jnp.int32)
    mine_live = mine_ids[None, :] < frame_counts[:, None]
    return jnp.where(mine_live[..., None], clipped, 0.0).astype(jnp.bfloat16)


def solution(mesh):
    return jax.shard_map(
        shards,
        mesh=mesh,
        in_specs=(
            P("groups", "ctx", None),
            P("groups"),
            P(),
            P(None, None, "mp"),
            P("mp", None),
            P(),
            P(None, None, "mp"),
            P(None, "mp"),
            P("mp"),
            P("mp"),
            P("mp", None),
            P(),
        ),
        out_specs=P("groups", ("ctx", "mp"), None),
        check_vma=False,
    )
```

```python
import jax
import jax.numpy as jnp
from jax import lax
from jax.sharding import PartitionSpec as P

HEAD_DIM = 64


epsilon = 1e-05
masked_score = -1e30


def with_halo(x, sides, width):
    for axis, dim in sides:
        devices, length = (lax.axis_size(axis), x.shape[dim])
        up = [(i, (i + 1) % devices) for i in range(devices - 1)]
        down = [(j, i) for i, j in up]
        last = lax.slice_in_dim(x, length - width, length, axis=dim)
        initial = lax.slice_in_dim(x, 0, width, axis=dim)
        before = lax.ppermute(last, axis, up)
        after = lax.ppermute(initial, axis, down)
        x = jnp.concatenate([before, x, after], axis=dim)
    return x


def layer_norm(values, gain):
    centre = jnp.mean(values, axis=-1, keepdims=True)
    centred = values - centre
    variance = jnp.mean(centred * centred, axis=-1, keepdims=True)
    return centred * lax.rsqrt(variance + epsilon) * gain


def gated_units(normed, w_glu):
    halves = jnp.einsum("std,gdc->gstc", normed, w_glu, preferred_element_type=jnp.float32)
    return (halves[0] * jax.nn.sigmoid(halves[1])).astype(jnp.bfloat16)


def xor_pairs(count, mask):
    return [(i, i ^ mask) for i in range(count)]


def bit_count(count):
    bits = count.bit_length() - 1
    assert (1 << bits) == count
    return bits


def reduce_scatter_rows(x, axis, dim):
    count, rank = lax.axis_size(axis), lax.axis_index(axis)
    bits = bit_count(count)
    shape = x.shape
    block = shape[dim] // count
    acc = x.reshape(shape[:dim] + (2,) * bits + (block,) + shape[dim + 1 :])
    for b in range(bits):
        bit_axis = dim + bits - 1 - b
        mine = (rank >> b) & 1
        keep = lax.dynamic_index_in_dim(acc, mine, bit_axis, keepdims=False)
        send = lax.dynamic_index_in_dim(acc, 1 - mine, bit_axis, keepdims=False)
        got = lax.ppermute(send.astype(jnp.bfloat16), axis, xor_pairs(count, 1 << b))
        acc = keep.astype(jnp.float32) + got.astype(jnp.float32)
    return acc


def all_gather_rows(x, axis, dim, last_bit=0):
    count, rank = lax.axis_size(axis), lax.axis_index(axis)
    bits = bit_count(count)
    shape = x.shape
    acc = x
    for k, b in enumerate(reversed(range(last_bit, bits))):
        mine = (rank >> b) & 1
        got = lax.ppermute(acc, axis, xor_pairs(count, 1 << b))
        both = jnp.zeros(acc.shape[: dim + k] + (2,) + acc.shape[dim + k :], acc.dtype)
        both = lax.dynamic_update_index_in_dim(both, acc, mine, dim + k)
        acc = lax.dynamic_update_index_in_dim(both, got, 1 - mine, dim + k)
    return acc.reshape(shape[:dim] + (shape[dim] * (count >> last_bit),) + shape[dim + 1 :])


def ring_gather(x, axis):
    count = lax.axis_size(axis)
    right = [(i, (i + 1) % count) for i in range(count)]
    left = [(i, (i - 1) % count) for i in range(count)]
    right_steps = count // 2
    left_steps = count - 1 - right_steps
    from_left, from_right = [], []
    going_right, going_left = x, x
    for step in range(right_steps):
        going_right = lax.ppermute(going_right, axis, right)
        from_left.append(going_right)
        if step < left_steps:
            going_left = lax.ppermute(going_left, axis, left)
            from_right.append(going_left)
    return jnp.stack([x] + from_right + from_left[::-1], axis=0)


def attend(queries, key_rows, value_rows, positions, frame_counts):
    scores = jnp.einsum(
        "sqhe,skhe->shqk", queries, key_rows, preferred_element_type=jnp.float32
    ) * HEAD_DIM ** (-0.5)
    is_live = positions[None, :] < frame_counts[:, None]
    scores = jnp.where(is_live[:, None, None, :], scores, masked_score)
    row_max = jnp.max(scores, axis=-1, keepdims=True)
    weights = jnp.exp(scores - row_max)
    row_sum = jnp.sum(weights, axis=-1)
    contrib = jnp.einsum(
        "shqk,skhe->shqe",
        weights.astype(jnp.bfloat16),
        value_rows,
        preferred_element_type=jnp.float32,
    )
    return (contrib / row_sum[..., None]).astype(jnp.bfloat16)


def attend_by_heads(projected, frame_counts, axis):
    _, records, frames, width = projected.shape
    count, rank = lax.axis_size(axis), lax.axis_index(axis)
    group = width // HEAD_DIM // count
    split = projected.reshape(3, records, frames, count, group, HEAD_DIM)
    pieces = [lax.dynamic_index_in_dim(split, rank, 3, keepdims=False)]
    sources = [rank]
    for shift in range(1, count):
        target = (rank + shift) % count
        send = lax.dynamic_index_in_dim(split, target, 3, keepdims=False)
        pairs = [(i, (i + shift) % count) for i in range(count)]
        pieces.append(lax.ppermute(send, axis, pairs))
        sources.append((rank - shift) % count)
    every = jnp.concatenate(pieces, axis=2)
    frame_steps = jnp.arange(frames, dtype=jnp.int32)
    positions = jnp.concatenate([source * frames + frame_steps for source in sources])
    attended = attend(every[0], every[1], every[2], positions, frame_counts)
    back = [attended[:, :, :frames]]
    for shift in range(1, count):
        rows = attended[:, :, shift * frames : (shift + 1) * frames]
        pairs = [(i, (i - shift) % count) for i in range(count)]
        back.append(lax.ppermute(rows, axis, pairs))
    ordered = jnp.roll(jnp.stack(back, axis=1), rank, axis=1)
    return ordered.transpose(0, 3, 1, 2, 4).reshape(records, frames, width)


def shards(
    features,
    frame_counts,
    attn_gain,
    w_qkv,
    w_out,
    conv_gain,
    w_glu,
    kernel,
    bn_scale,
    bn_shift,
    w_pw,
    clip_level,
):
    records, frames_here, model_width = features.shape
    head_count = w_qkv.shape[2] // HEAD_DIM
    ctx_rank = lax.axis_index("ctx")
    ctx_count = lax.axis_size("ctx")
    score_scale = HEAD_DIM ** (-0.5)
    first_frame = ctx_rank * frames_here
    w_glu_pair = lax.ppermute(w_glu, "mp", xor_pairs(lax.axis_size("mp"), 1))
    normed = layer_norm(features.astype(jnp.float32), attn_gain).astype(jnp.bfloat16)
    projected = jnp.einsum(
        "std,idc->istc", normed, w_qkv, preferred_element_type=jnp.float32
    ).astype(jnp.bfloat16)
    if head_count % ctx_count == 0:
        attended = attend_by_heads(projected, frame_counts, "ctx")
    else:
        query_heads = projected[0].reshape(records, frames_here, head_count, HEAD_DIM)
        kv_all = ring_gather(projected[1:], "ctx")
        key_heads = kv_all[:, 0].reshape(ctx_count, records, frames_here, head_count, HEAD_DIM)
        value_heads = kv_all[:, 1].reshape(ctx_count, records, frames_here, head_count, HEAD_DIM)
        block_rank = (ctx_rank + jnp.arange(ctx_count, dtype=jnp.int32)) % ctx_count
        positions = block_rank[:, None] * frames_here + jnp.arange(frames_here, dtype=jnp.int32)
        key_heads = key_heads.transpose(1, 0, 2, 3, 4).reshape(records, -1, head_count, HEAD_DIM)
        value_heads = value_heads.transpose(1, 0, 2, 3, 4).reshape(records, -1, head_count, HEAD_DIM)
        attended = attend(query_heads, key_heads, value_heads, positions.reshape(-1), frame_counts)
        attended = attended.transpose(0, 2, 1, 3).reshape(records, frames_here, head_count * HEAD_DIM)
    attn_part = jnp.einsum("stc,cd->std", attended, w_out, preferred_element_type=jnp.float32)
    mp_count = lax.axis_size("mp")
    mp_rank = lax.axis_index("mp")
    rows_mine = frames_here // mp_count
    row_start = mp_rank * rows_mine
    attn_mine = reduce_scatter_rows(attn_part.astype(jnp.bfloat16), "mp", 1)
    features_mine = lax.dynamic_slice_in_dim(features, row_start, rows_mine, 1)
    residual_mine = features_mine.astype(jnp.float32) + attn_mine
    normed_mine = layer_norm(residual_mine, conv_gain).astype(jnp.bfloat16)
    pair = xor_pairs(mp_count, 1)
    held_rows = all_gather_rows(normed_mine, "mp", 1, last_bit=1)
    gated_mine = gated_units(held_rows, w_glu)
    gated_lent = lax.ppermute(gated_units(held_rows, w_glu_pair), "mp", pair)
    bit0 = mp_rank & 1
    split_rows = (records, mp_count // 2, rows_mine, gated_mine.shape[-1])
    gated_rows = jnp.zeros((records, mp_count // 2, 2, rows_mine, gated_mine.shape[-1]), jnp.bfloat16)
    gated_rows = lax.dynamic_update_index_in_dim(gated_rows, gated_mine.reshape(split_rows), bit0, 2)
    gated_rows = lax.dynamic_update_index_in_dim(gated_rows, gated_lent.reshape(split_rows), 1 - bit0, 2)
    gated_rows = gated_rows.reshape(records, frames_here, gated_mine.shape[-1])
    frame_ids = first_frame + jnp.arange(frames_here, dtype=jnp.int32)
    frame_live = frame_ids[None, :] < frame_counts[:, None]
    gated_rows = jnp.where(frame_live[..., None], gated_rows, jnp.zeros((), jnp.bfloat16))
    rim_width = kernel.shape[0] // 2
    padded = with_halo(gated_rows, (("ctx", 1),), rim_width)
    depthwise = lax.conv_general_dilated(
        padded.astype(jnp.float32),
        kernel[:, None, :],
        window_strides=(1,),
        padding="VALID",
        dimension_numbers=("NWC", "WIO", "NWC"),
        feature_group_count=kernel.shape[1],
        precision=lax.Precision.HIGHEST,
    )
    activated = jax.nn.silu(depthwise * bn_scale + bn_shift).astype(jnp.bfloat16)
    conv_part = jnp.einsum("stc,cd->std", activated, w_pw, preferred_element_type=jnp.float32)
    conv_rows = reduce_scatter_rows(conv_part.astype(jnp.bfloat16), "mp", 1)
    combined = residual_mine + conv_rows
    clip_bound = clip_level.astype(jnp.float32) / 16.0
    clipped = jnp.clip(combined, -clip_bound, clip_bound)
    mine_ids = first_frame + row_start + jnp.arange(rows_mine, dtype=jnp.int32)
    mine_live = mine_ids[None, :] < frame_counts[:, None]
    return jnp.where(mine_live[..., None], clipped, 0.0).astype(jnp.bfloat16)


def solution(mesh):
    return jax.shard_map(
        shards,
        mesh=mesh,
        in_specs=(
            P("groups", "ctx", None),
            P("groups"),
            P(),
            P(None, None, "mp"),
            P("mp", None),
            P(),
            P(None, None, "mp"),
            P(None, "mp"),
            P("mp"),
            P("mp"),
            P("mp", None),
            P(),
        ),
        out_specs=P("groups", ("ctx", "mp"), None),
        check_vma=False,
    )
```

```python
import jax
import jax.numpy as jnp
from jax import lax
from jax.sharding import PartitionSpec as P

HEAD_DIM = 64


epsilon = 1e-05
masked_score = -1e30


def with_halo(x, sides, width):
    for axis, dim in sides:
        devices, length = (lax.axis_size(axis), x.shape[dim])
        up = [(i, (i + 1) % devices) for i in range(devices - 1)]
        down = [(j, i) for i, j in up]
        last = lax.slice_in_dim(x, length - width, length, axis=dim)
        initial = lax.slice_in_dim(x, 0, width, axis=dim)
        before = lax.ppermute(last, axis, up)
        after = lax.ppermute(initial, axis, down)
        x = jnp.concatenate([before, x, after], axis=dim)
    return x


def layer_norm(values, gain):
    centre = jnp.mean(values, axis=-1, keepdims=True)
    centred = values - centre
    variance = jnp.mean(centred * centred, axis=-1, keepdims=True)
    return centred * lax.rsqrt(variance + epsilon) * gain


def gated_units(normed, w_glu):
    halves = jnp.einsum("std,gdc->gstc", normed, w_glu, preferred_element_type=jnp.float32)
    return (halves[0] * jax.nn.sigmoid(halves[1])).astype(jnp.bfloat16)


def xor_pairs(count, mask):
    return [(i, i ^ mask) for i in range(count)]


def bit_count(count):
    bits = count.bit_length() - 1
    assert (1 << bits) == count
    return bits


def reduce_scatter_rows(x, axis, dim):
    count, rank = lax.axis_size(axis), lax.axis_index(axis)
    bits = bit_count(count)
    shape = x.shape
    block = shape[dim] // count
    acc = x.reshape(shape[:dim] + (2,) * bits + (block,) + shape[dim + 1 :])
    first = 0
    if bits >= 2:
        mine, onward = rank & 1, (rank >> 1) & 1
        keep = lax.dynamic_index_in_dim(acc, mine, dim + bits - 1, keepdims=False)
        send = lax.dynamic_index_in_dim(acc, 1 - mine, dim + bits - 1, keepdims=False)
        got_far = lax.ppermute(
            lax.dynamic_index_in_dim(send, 1 - onward, dim + bits - 2, keepdims=False),
            axis, xor_pairs(count, 1),
        )
        got_near = lax.ppermute(
            lax.dynamic_index_in_dim(send, onward, dim + bits - 2, keepdims=False),
            axis, xor_pairs(count, 1),
        )
        far = lax.dynamic_index_in_dim(keep, 1 - onward, dim + bits - 2, keepdims=False)
        far = far.astype(jnp.float32) + got_far.astype(jnp.float32)
        near = lax.dynamic_index_in_dim(keep, onward, dim + bits - 2, keepdims=False)
        near = near.astype(jnp.float32) + got_near.astype(jnp.float32)
        got = lax.ppermute(far.astype(jnp.bfloat16), axis, xor_pairs(count, 2))
        acc = near + got.astype(jnp.float32)
        first = 2
    for b in range(first, bits):
        bit_axis = dim + bits - 1 - b
        mine = (rank >> b) & 1
        keep = lax.dynamic_index_in_dim(acc, mine, bit_axis, keepdims=False)
        send = lax.dynamic_index_in_dim(acc, 1 - mine, bit_axis, keepdims=False)
        got = lax.ppermute(send.astype(jnp.bfloat16), axis, xor_pairs(count, 1 << b))
        acc = keep.astype(jnp.float32) + got.astype(jnp.float32)
    return acc


def all_gather_rows(x, axis, dim):
    count, rank = lax.axis_size(axis), lax.axis_index(axis)
    bits = bit_count(count)
    shape = x.shape
    acc = x
    for k, b in enumerate(reversed(range(bits))):
        mine = (rank >> b) & 1
        got = lax.ppermute(acc, axis, xor_pairs(count, 1 << b))
        both = jnp.zeros(acc.shape[: dim + k] + (2,) + acc.shape[dim + k :], acc.dtype)
        both = lax.dynamic_update_index_in_dim(both, acc, mine, dim + k)
        acc = lax.dynamic_update_index_in_dim(both, got, 1 - mine, dim + k)
    return acc.reshape(shape[:dim] + (shape[dim] * count,) + shape[dim + 1 :])


def ring_gather(x, axis):
    count = lax.axis_size(axis)
    right = [(i, (i + 1) % count) for i in range(count)]
    left = [(i, (i - 1) % count) for i in range(count)]
    right_steps = count // 2
    left_steps = count - 1 - right_steps
    from_left, from_right = [], []
    going_right, going_left = x, x
    for step in range(right_steps):
        going_right = lax.ppermute(going_right, axis, right)
        from_left.append(going_right)
        if step < left_steps:
            going_left = lax.ppermute(going_left, axis, left)
            from_right.append(going_left)
    return jnp.stack([x] + from_right + from_left[::-1], axis=0)


def attend(queries, key_rows, value_rows, positions, frame_counts):
    scores = jnp.einsum(
        "sqhe,skhe->shqk", queries, key_rows, preferred_element_type=jnp.float32
    ) * HEAD_DIM ** (-0.5)
    is_live = positions[None, :] < frame_counts[:, None]
    scores = jnp.where(is_live[:, None, None, :], scores, masked_score)
    row_max = jnp.max(scores, axis=-1, keepdims=True)
    weights = jnp.exp(scores - row_max)
    row_sum = jnp.sum(weights, axis=-1)
    contrib = jnp.einsum(
        "shqk,skhe->shqe",
        weights.astype(jnp.bfloat16),
        value_rows,
        preferred_element_type=jnp.float32,
    )
    return (contrib / row_sum[..., None]).astype(jnp.bfloat16)


def attend_by_heads(projected, frame_counts, axis):
    _, records, frames, width = projected.shape
    count, rank = lax.axis_size(axis), lax.axis_index(axis)
    group = width // HEAD_DIM // count
    split = projected.reshape(3, records, frames, count, group, HEAD_DIM)
    pieces = [lax.dynamic_index_in_dim(split, rank, 3, keepdims=False)]
    sources = [rank]
    for shift in range(1, count):
        target = (rank + shift) % count
        send = lax.dynamic_index_in_dim(split, target, 3, keepdims=False)
        pairs = [(i, (i + shift) % count) for i in range(count)]
        pieces.append(lax.ppermute(send, axis, pairs))
        sources.append((rank - shift) % count)
    every = jnp.concatenate(pieces, axis=2)
    frame_steps = jnp.arange(frames, dtype=jnp.int32)
    positions = jnp.concatenate([source * frames + frame_steps for source in sources])
    attended = attend(every[0], every[1], every[2], positions, frame_counts)
    back = [attended[:, :, :frames]]
    for shift in range(1, count):
        rows = attended[:, :, shift * frames : (shift + 1) * frames]
        pairs = [(i, (i - shift) % count) for i in range(count)]
        back.append(lax.ppermute(rows, axis, pairs))
    ordered = jnp.roll(jnp.stack(back, axis=1), rank, axis=1)
    return ordered.transpose(0, 3, 1, 2, 4).reshape(records, frames, width)


def shards(
    features,
    frame_counts,
    attn_gain,
    w_qkv,
    w_out,
    conv_gain,
    w_glu,
    kernel,
    bn_scale,
    bn_shift,
    w_pw,
    clip_level,
):
    records, frames_here, model_width = features.shape
    head_count = w_qkv.shape[2] // HEAD_DIM
    ctx_rank = lax.axis_index("ctx")
    ctx_count = lax.axis_size("ctx")
    score_scale = HEAD_DIM ** (-0.5)
    first_frame = ctx_rank * frames_here
    normed = layer_norm(features.astype(jnp.float32), attn_gain).astype(jnp.bfloat16)
    projected = jnp.einsum(
        "std,idc->istc", normed, w_qkv, preferred_element_type=jnp.float32
    ).astype(jnp.bfloat16)
    if head_count % ctx_count == 0:
        attended = attend_by_heads(projected, frame_counts, "ctx")
    else:
        query_heads = projected[0].reshape(records, frames_here, head_count, HEAD_DIM)
        kv_all = ring_gather(projected[1:], "ctx")
        key_heads = kv_all[:, 0].reshape(ctx_count, records, frames_here, head_count, HEAD_DIM)
        value_heads = kv_all[:, 1].reshape(ctx_count, records, frames_here, head_count, HEAD_DIM)
        block_rank = (ctx_rank + jnp.arange(ctx_count, dtype=jnp.int32)) % ctx_count
        positions = block_rank[:, None] * frames_here + jnp.arange(frames_here, dtype=jnp.int32)
        key_heads = key_heads.transpose(1, 0, 2, 3, 4).reshape(records, -1, head_count, HEAD_DIM)
        value_heads = value_heads.transpose(1, 0, 2, 3, 4).reshape(records, -1, head_count, HEAD_DIM)
        attended = attend(query_heads, key_heads, value_heads, positions.reshape(-1), frame_counts)
        attended = attended.transpose(0, 2, 1, 3).reshape(records, frames_here, head_count * HEAD_DIM)
    attn_part = jnp.einsum("stc,cd->std", attended, w_out, preferred_element_type=jnp.float32)
    mp_count = lax.axis_size("mp")
    mp_rank = lax.axis_index("mp")
    rows_mine = frames_here // mp_count
    row_start = mp_rank * rows_mine
    attn_mine = reduce_scatter_rows(attn_part.astype(jnp.bfloat16), "mp", 1)
    features_mine = lax.dynamic_slice_in_dim(features, row_start, rows_mine, 1)
    residual_mine = features_mine.astype(jnp.float32) + attn_mine
    normed_mine = layer_norm(residual_mine, conv_gain).astype(jnp.bfloat16)
    normed_conv = all_gather_rows(normed_mine, "mp", 1)
    gated_rows = gated_units(normed_conv, w_glu)
    frame_ids = first_frame + jnp.arange(frames_here, dtype=jnp.int32)
    frame_live = frame_ids[None, :] < frame_counts[:, None]
    gated_rows = jnp.where(frame_live[..., None], gated_rows, jnp.zeros((), jnp.bfloat16))
    rim_width = kernel.shape[0] // 2
    padded = with_halo(gated_rows, (("ctx", 1),), rim_width)
    depthwise = lax.conv_general_dilated(
        padded.astype(jnp.float32),
        kernel[:, None, :],
        window_strides=(1,),
        padding="VALID",
        dimension_numbers=("NWC", "WIO", "NWC"),
        feature_group_count=kernel.shape[1],
        precision=lax.Precision.HIGHEST,
    )
    activated = jax.nn.silu(depthwise * bn_scale + bn_shift).astype(jnp.bfloat16)
    conv_part = jnp.einsum("stc,cd->std", activated, w_pw, preferred_element_type=jnp.float32)
    conv_rows = reduce_scatter_rows(conv_part.astype(jnp.bfloat16), "mp", 1)
    combined = residual_mine + conv_rows
    clip_bound = clip_level.astype(jnp.float32) / 16.0
    clipped = jnp.clip(combined, -clip_bound, clip_bound)
    mine_ids = first_frame + row_start + jnp.arange(rows_mine, dtype=jnp.int32)
    mine_live = mine_ids[None, :] < frame_counts[:, None]
    return jnp.where(mine_live[..., None], clipped, 0.0).astype(jnp.bfloat16)


def solution(mesh):
    return jax.shard_map(
        shards,
        mesh=mesh,
        in_specs=(
            P("groups", "ctx", None),
            P("groups"),
            P(),
            P(None, None, "mp"),
            P("mp", None),
            P(),
            P(None, None, "mp"),
            P(None, "mp"),
            P("mp"),
            P("mp"),
            P("mp", None),
            P(),
        ),
        out_specs=P("groups", ("ctx", "mp"), None),
        check_vma=False,
    )
```

```python
import jax
import jax.numpy as jnp
from jax import lax
from jax.sharding import PartitionSpec as P

HEAD_DIM = 64


epsilon = 1e-05
masked_score = -1e30


def with_halo(x, sides, width):
    for axis, dim in sides:
        devices, length = (lax.axis_size(axis), x.shape[dim])
        up = [(i, (i + 1) % devices) for i in range(devices - 1)]
        down = [(j, i) for i, j in up]
        last = lax.slice_in_dim(x, length - width, length, axis=dim)
        initial = lax.slice_in_dim(x, 0, width, axis=dim)
        before = lax.ppermute(last, axis, up)
        after = lax.ppermute(initial, axis, down)
        x = jnp.concatenate([before, x, after], axis=dim)
    return x


def layer_norm(values, gain):
    centre = jnp.mean(values, axis=-1, keepdims=True)
    centred = values - centre
    variance = jnp.mean(centred * centred, axis=-1, keepdims=True)
    return centred * lax.rsqrt(variance + epsilon) * gain


def gated_units(normed, w_glu):
    halves = jnp.einsum("std,gdc->gstc", normed, w_glu, preferred_element_type=jnp.float32)
    return (halves[0] * jax.nn.sigmoid(halves[1])).astype(jnp.bfloat16)


def xor_pairs(count, mask):
    return [(i, i ^ mask) for i in range(count)]


def bit_count(count):
    bits = count.bit_length() - 1
    assert (1 << bits) == count
    return bits


def reduce_scatter_rows(x, axis, dim):
    count, rank = lax.axis_size(axis), lax.axis_index(axis)
    bits = bit_count(count)
    shape = x.shape
    block = shape[dim] // count
    acc = x.reshape(shape[:dim] + (2,) * bits + (block,) + shape[dim + 1 :])
    first = 0
    if bits >= 2:
        mine, onward = rank & 1, (rank >> 1) & 1
        keep = lax.dynamic_index_in_dim(acc, mine, dim + bits - 1, keepdims=False)
        send = lax.dynamic_index_in_dim(acc, 1 - mine, dim + bits - 1, keepdims=False)
        got_far = lax.ppermute(
            lax.dynamic_index_in_dim(send, 1 - onward, dim + bits - 2, keepdims=False),
            axis, xor_pairs(count, 1),
        )
        got_near = lax.ppermute(
            lax.dynamic_index_in_dim(send, onward, dim + bits - 2, keepdims=False),
            axis, xor_pairs(count, 1),
        )
        far = lax.dynamic_index_in_dim(keep, 1 - onward, dim + bits - 2, keepdims=False)
        far = far.astype(jnp.float32) + got_far.astype(jnp.float32)
        near = lax.dynamic_index_in_dim(keep, onward, dim + bits - 2, keepdims=False)
        near = near.astype(jnp.float32) + got_near.astype(jnp.float32)
        got = lax.ppermute(far.astype(jnp.bfloat16), axis, xor_pairs(count, 2))
        acc = near + got.astype(jnp.float32)
        first = 2
    for b in range(first, bits):
        bit_axis = dim + bits - 1 - b
        mine = (rank >> b) & 1
        keep = lax.dynamic_index_in_dim(acc, mine, bit_axis, keepdims=False)
        send = lax.dynamic_index_in_dim(acc, 1 - mine, bit_axis, keepdims=False)
        got = lax.ppermute(send.astype(jnp.bfloat16), axis, xor_pairs(count, 1 << b))
        acc = keep.astype(jnp.float32) + got.astype(jnp.float32)
    return acc


def place_pair(mine, other, bit, axis):
    both = jnp.zeros(mine.shape[:axis] + (2,) + mine.shape[axis:], mine.dtype)
    both = lax.dynamic_update_index_in_dim(both, mine, bit, axis)
    return lax.dynamic_update_index_in_dim(both, other, 1 - bit, axis)


def all_gather_rows(x, axis, dim):
    count, rank = lax.axis_size(axis), lax.axis_index(axis)
    bits = bit_count(count)
    shape = x.shape
    mine_acc = x
    their_acc = lax.ppermute(x, axis, xor_pairs(count, 1))
    for k, b in enumerate(reversed(range(1, bits))):
        bit = (rank >> b) & 1
        got = lax.ppermute(mine_acc, axis, xor_pairs(count, 1 << b))
        forwarded = lax.ppermute(got, axis, xor_pairs(count, 1))
        mine_acc = place_pair(mine_acc, got, bit, dim + k)
        their_acc = place_pair(their_acc, forwarded, bit, dim + k)
    acc = place_pair(mine_acc, their_acc, rank & 1, dim + bits - 1)
    return acc.reshape(shape[:dim] + (shape[dim] * count,) + shape[dim + 1 :])


def ring_gather(x, axis):
    count = lax.axis_size(axis)
    right = [(i, (i + 1) % count) for i in range(count)]
    left = [(i, (i - 1) % count) for i in range(count)]
    right_steps = count // 2
    left_steps = count - 1 - right_steps
    from_left, from_right = [], []
    going_right, going_left = x, x
    for step in range(right_steps):
        going_right = lax.ppermute(going_right, axis, right)
        from_left.append(going_right)
        if step < left_steps:
            going_left = lax.ppermute(going_left, axis, left)
            from_right.append(going_left)
    return jnp.stack([x] + from_right + from_left[::-1], axis=0)


def attend(queries, key_rows, value_rows, positions, frame_counts):
    scores = jnp.einsum(
        "sqhe,skhe->shqk", queries, key_rows, preferred_element_type=jnp.float32
    ) * HEAD_DIM ** (-0.5)
    is_live = positions[None, :] < frame_counts[:, None]
    scores = jnp.where(is_live[:, None, None, :], scores, masked_score)
    row_max = jnp.max(scores, axis=-1, keepdims=True)
    weights = jnp.exp(scores - row_max)
    row_sum = jnp.sum(weights, axis=-1)
    contrib = jnp.einsum(
        "shqk,skhe->shqe",
        weights.astype(jnp.bfloat16),
        value_rows,
        preferred_element_type=jnp.float32,
    )
    return (contrib / row_sum[..., None]).astype(jnp.bfloat16)


def attend_by_heads(projected, frame_counts, axis):
    _, records, frames, width = projected.shape
    count, rank = lax.axis_size(axis), lax.axis_index(axis)
    group = width // HEAD_DIM // count
    split = projected.reshape(3, records, frames, count, group, HEAD_DIM)
    pieces = [lax.dynamic_index_in_dim(split, rank, 3, keepdims=False)]
    sources = [rank]
    for shift in range(1, count):
        target = (rank + shift) % count
        send = lax.dynamic_index_in_dim(split, target, 3, keepdims=False)
        pairs = [(i, (i + shift) % count) for i in range(count)]
        pieces.append(lax.ppermute(send, axis, pairs))
        sources.append((rank - shift) % count)
    every = jnp.concatenate(pieces, axis=2)
    frame_steps = jnp.arange(frames, dtype=jnp.int32)
    positions = jnp.concatenate([source * frames + frame_steps for source in sources])
    attended = attend(every[0], every[1], every[2], positions, frame_counts)
    back = [attended[:, :, :frames]]
    for shift in range(1, count):
        rows = attended[:, :, shift * frames : (shift + 1) * frames]
        pairs = [(i, (i - shift) % count) for i in range(count)]
        back.append(lax.ppermute(rows, axis, pairs))
    ordered = jnp.roll(jnp.stack(back, axis=1), rank, axis=1)
    return ordered.transpose(0, 3, 1, 2, 4).reshape(records, frames, width)


def shards(
    features,
    frame_counts,
    attn_gain,
    w_qkv,
    w_out,
    conv_gain,
    w_glu,
    kernel,
    bn_scale,
    bn_shift,
    w_pw,
    clip_level,
):
    records, frames_here, model_width = features.shape
    head_count = w_qkv.shape[2] // HEAD_DIM
    ctx_rank = lax.axis_index("ctx")
    ctx_count = lax.axis_size("ctx")
    score_scale = HEAD_DIM ** (-0.5)
    first_frame = ctx_rank * frames_here
    normed = layer_norm(features.astype(jnp.float32), attn_gain).astype(jnp.bfloat16)
    projected = jnp.einsum(
        "std,idc->istc", normed, w_qkv, preferred_element_type=jnp.float32
    ).astype(jnp.bfloat16)
    if head_count % ctx_count == 0:
        attended = attend_by_heads(projected, frame_counts, "ctx")
    else:
        query_heads = projected[0].reshape(records, frames_here, head_count, HEAD_DIM)
        kv_all = ring_gather(projected[1:], "ctx")
        key_heads = kv_all[:, 0].reshape(ctx_count, records, frames_here, head_count, HEAD_DIM)
        value_heads = kv_all[:, 1].reshape(ctx_count, records, frames_here, head_count, HEAD_DIM)
        block_rank = (ctx_rank + jnp.arange(ctx_count, dtype=jnp.int32)) % ctx_count
        positions = block_rank[:, None] * frames_here + jnp.arange(frames_here, dtype=jnp.int32)
        key_heads = key_heads.transpose(1, 0, 2, 3, 4).reshape(records, -1, head_count, HEAD_DIM)
        value_heads = value_heads.transpose(1, 0, 2, 3, 4).reshape(records, -1, head_count, HEAD_DIM)
        attended = attend(query_heads, key_heads, value_heads, positions.reshape(-1), frame_counts)
        attended = attended.transpose(0, 2, 1, 3).reshape(records, frames_here, head_count * HEAD_DIM)
    attn_part = jnp.einsum("stc,cd->std", attended, w_out, preferred_element_type=jnp.float32)
    mp_count = lax.axis_size("mp")
    mp_rank = lax.axis_index("mp")
    rows_mine = frames_here // mp_count
    row_start = mp_rank * rows_mine
    attn_mine = reduce_scatter_rows(attn_part.astype(jnp.bfloat16), "mp", 1)
    features_mine = lax.dynamic_slice_in_dim(features, row_start, rows_mine, 1)
    residual_mine = features_mine.astype(jnp.float32) + attn_mine
    normed_mine = layer_norm(residual_mine, conv_gain).astype(jnp.bfloat16)
    normed_conv = all_gather_rows(normed_mine, "mp", 1)
    gated_rows = gated_units(normed_conv, w_glu)
    frame_ids = first_frame + jnp.arange(frames_here, dtype=jnp.int32)
    frame_live = frame_ids[None, :] < frame_counts[:, None]
    gated_rows = jnp.where(frame_live[..., None], gated_rows, jnp.zeros((), jnp.bfloat16))
    rim_width = kernel.shape[0] // 2
    padded = with_halo(gated_rows, (("ctx", 1),), rim_width)
    depthwise = lax.conv_general_dilated(
        padded.astype(jnp.float32),
        kernel[:, None, :],
        window_strides=(1,),
        padding="VALID",
        dimension_numbers=("NWC", "WIO", "NWC"),
        feature_group_count=kernel.shape[1],
        precision=lax.Precision.HIGHEST,
    )
    activated = jax.nn.silu(depthwise * bn_scale + bn_shift).astype(jnp.bfloat16)
    conv_part = jnp.einsum("stc,cd->std", activated, w_pw, preferred_element_type=jnp.float32)
    conv_rows = reduce_scatter_rows(conv_part.astype(jnp.bfloat16), "mp", 1)
    combined = residual_mine + conv_rows
    clip_bound = clip_level.astype(jnp.float32) / 16.0
    clipped = jnp.clip(combined, -clip_bound, clip_bound)
    mine_ids = first_frame + row_start + jnp.arange(rows_mine, dtype=jnp.int32)
    mine_live = mine_ids[None, :] < frame_counts[:, None]
    return jnp.where(mine_live[..., None], clipped, 0.0).astype(jnp.bfloat16)


def solution(mesh):
    return jax.shard_map(
        shards,
        mesh=mesh,
        in_specs=(
            P("groups", "ctx", None),
            P("groups"),
            P(),
            P(None, None, "mp"),
            P("mp", None),
            P(),
            P(None, None, "mp"),
            P(None, "mp"),
            P("mp"),
            P("mp"),
            P("mp", None),
            P(),
        ),
        out_specs=P("groups", ("ctx", "mp"), None),
        check_vma=False,
    )
```

```python
import jax
import jax.numpy as jnp
from jax import lax
from jax.sharding import PartitionSpec as P

HEAD_DIM = 64


epsilon = 1e-05
masked_score = -1e30


def with_halo(x, sides, width):
    for axis, dim in sides:
        devices, length = (lax.axis_size(axis), x.shape[dim])
        up = [(i, (i + 1) % devices) for i in range(devices - 1)]
        down = [(j, i) for i, j in up]
        last = lax.slice_in_dim(x, length - width, length, axis=dim)
        initial = lax.slice_in_dim(x, 0, width, axis=dim)
        before = lax.ppermute(last, axis, up)
        after = lax.ppermute(initial, axis, down)
        x = jnp.concatenate([before, x, after], axis=dim)
    return x


def layer_norm(values, gain):
    centre = jnp.mean(values, axis=-1, keepdims=True)
    centred = values - centre
    variance = jnp.mean(centred * centred, axis=-1, keepdims=True)
    return centred * lax.rsqrt(variance + epsilon) * gain


def gated_units(normed, w_glu):
    halves = jnp.einsum("std,gdc->gstc", normed, w_glu, preferred_element_type=jnp.float32)
    return (halves[0] * jax.nn.sigmoid(halves[1])).astype(jnp.bfloat16)


def xor_pairs(count, mask):
    return [(i, i ^ mask) for i in range(count)]


def bit_count(count):
    bits = count.bit_length() - 1
    assert (1 << bits) == count
    return bits


def reduce_scatter_rows(x, axis, dim):
    count, rank = lax.axis_size(axis), lax.axis_index(axis)
    bits = bit_count(count)
    shape = x.shape
    block = shape[dim] // count
    acc = x.reshape(shape[:dim] + (2,) * bits + (block,) + shape[dim + 1 :])
    first = 0
    if bits >= 2:
        mine, onward = rank & 1, (rank >> 1) & 1
        keep = lax.dynamic_index_in_dim(acc, mine, dim + bits - 1, keepdims=False)
        send = lax.dynamic_index_in_dim(acc, 1 - mine, dim + bits - 1, keepdims=False)
        got_far = lax.ppermute(
            lax.dynamic_index_in_dim(send, 1 - onward, dim + bits - 2, keepdims=False),
            axis, xor_pairs(count, 1),
        )
        got_near = lax.ppermute(
            lax.dynamic_index_in_dim(send, onward, dim + bits - 2, keepdims=False),
            axis, xor_pairs(count, 1),
        )
        far = lax.dynamic_index_in_dim(keep, 1 - onward, dim + bits - 2, keepdims=False)
        far = far.astype(jnp.float32) + got_far.astype(jnp.float32)
        near = lax.dynamic_index_in_dim(keep, onward, dim + bits - 2, keepdims=False)
        near = near.astype(jnp.float32) + got_near.astype(jnp.float32)
        got = lax.ppermute(far.astype(jnp.bfloat16), axis, xor_pairs(count, 2))
        acc = near + got.astype(jnp.float32)
        first = 2
    for b in range(first, bits):
        bit_axis = dim + bits - 1 - b
        mine = (rank >> b) & 1
        keep = lax.dynamic_index_in_dim(acc, mine, bit_axis, keepdims=False)
        send = lax.dynamic_index_in_dim(acc, 1 - mine, bit_axis, keepdims=False)
        got = lax.ppermute(send.astype(jnp.bfloat16), axis, xor_pairs(count, 1 << b))
        acc = keep.astype(jnp.float32) + got.astype(jnp.float32)
    return acc


def place_pair(mine, other, bit, axis):
    both = jnp.zeros(mine.shape[:axis] + (2,) + mine.shape[axis:], mine.dtype)
    both = lax.dynamic_update_index_in_dim(both, mine, bit, axis)
    return lax.dynamic_update_index_in_dim(both, other, 1 - bit, axis)


def all_gather_rows(x, axis, dim, apply=None):
    count, rank = lax.axis_size(axis), lax.axis_index(axis)
    bits = bit_count(count)
    shape = x.shape
    mine_acc = x
    their_acc = lax.ppermute(x, axis, xor_pairs(count, 1))
    for k, b in enumerate(reversed(range(1, bits))):
        bit = (rank >> b) & 1
        got = lax.ppermute(mine_acc, axis, xor_pairs(count, 1 << b))
        forwarded = lax.ppermute(got, axis, xor_pairs(count, 1))
        mine_acc = place_pair(mine_acc, got, bit, dim + k)
        their_acc = place_pair(their_acc, forwarded, bit, dim + k)
    if apply is not None:
        mine_acc, their_acc = apply(mine_acc), apply(their_acc)
    acc = place_pair(mine_acc, their_acc, rank & 1, dim + bits - 1)
    return acc.reshape(acc.shape[:dim] + (shape[dim] * count,) + acc.shape[dim + bits + 1 :])


def ring_gather(x, axis):
    count = lax.axis_size(axis)
    right = [(i, (i + 1) % count) for i in range(count)]
    left = [(i, (i - 1) % count) for i in range(count)]
    right_steps = count // 2
    left_steps = count - 1 - right_steps
    from_left, from_right = [], []
    going_right, going_left = x, x
    for step in range(right_steps):
        going_right = lax.ppermute(going_right, axis, right)
        from_left.append(going_right)
        if step < left_steps:
            going_left = lax.ppermute(going_left, axis, left)
            from_right.append(going_left)
    return jnp.stack([x] + from_right + from_left[::-1], axis=0)


def attend(queries, key_rows, value_rows, positions, frame_counts):
    scores = jnp.einsum(
        "sqhe,skhe->shqk", queries, key_rows, preferred_element_type=jnp.float32
    ) * HEAD_DIM ** (-0.5)
    is_live = positions[None, :] < frame_counts[:, None]
    scores = jnp.where(is_live[:, None, None, :], scores, masked_score)
    row_max = jnp.max(scores, axis=-1, keepdims=True)
    weights = jnp.exp(scores - row_max)
    row_sum = jnp.sum(weights, axis=-1)
    contrib = jnp.einsum(
        "shqk,skhe->shqe",
        weights.astype(jnp.bfloat16),
        value_rows,
        preferred_element_type=jnp.float32,
    )
    return (contrib / row_sum[..., None]).astype(jnp.bfloat16)


def attend_by_heads(projected, frame_counts, axis):
    _, records, frames, width = projected.shape
    count, rank = lax.axis_size(axis), lax.axis_index(axis)
    group = width // HEAD_DIM // count
    split = projected.reshape(3, records, frames, count, group, HEAD_DIM)
    pieces = [lax.dynamic_index_in_dim(split, rank, 3, keepdims=False)]
    sources = [rank]
    for shift in range(1, count):
        target = (rank + shift) % count
        send = lax.dynamic_index_in_dim(split, target, 3, keepdims=False)
        pairs = [(i, (i + shift) % count) for i in range(count)]
        pieces.append(lax.ppermute(send, axis, pairs))
        sources.append((rank - shift) % count)
    every = jnp.concatenate(pieces, axis=2)
    frame_steps = jnp.arange(frames, dtype=jnp.int32)
    positions = jnp.concatenate([source * frames + frame_steps for source in sources])
    attended = attend(every[0], every[1], every[2], positions, frame_counts)
    back = [attended[:, :, :frames]]
    for shift in range(1, count):
        rows = attended[:, :, shift * frames : (shift + 1) * frames]
        pairs = [(i, (i - shift) % count) for i in range(count)]
        back.append(lax.ppermute(rows, axis, pairs))
    ordered = jnp.roll(jnp.stack(back, axis=1), rank, axis=1)
    return ordered.transpose(0, 3, 1, 2, 4).reshape(records, frames, width)


def shards(
    features,
    frame_counts,
    attn_gain,
    w_qkv,
    w_out,
    conv_gain,
    w_glu,
    kernel,
    bn_scale,
    bn_shift,
    w_pw,
    clip_level,
):
    records, frames_here, model_width = features.shape
    head_count = w_qkv.shape[2] // HEAD_DIM
    ctx_rank = lax.axis_index("ctx")
    ctx_count = lax.axis_size("ctx")
    score_scale = HEAD_DIM ** (-0.5)
    first_frame = ctx_rank * frames_here
    normed = layer_norm(features.astype(jnp.float32), attn_gain).astype(jnp.bfloat16)
    projected = jnp.einsum(
        "std,idc->istc", normed, w_qkv, preferred_element_type=jnp.float32
    ).astype(jnp.bfloat16)
    if head_count % ctx_count == 0:
        attended = attend_by_heads(projected, frame_counts, "ctx")
    else:
        query_heads = projected[0].reshape(records, frames_here, head_count, HEAD_DIM)
        kv_all = ring_gather(projected[1:], "ctx")
        key_heads = kv_all[:, 0].reshape(ctx_count, records, frames_here, head_count, HEAD_DIM)
        value_heads = kv_all[:, 1].reshape(ctx_count, records, frames_here, head_count, HEAD_DIM)
        block_rank = (ctx_rank + jnp.arange(ctx_count, dtype=jnp.int32)) % ctx_count
        positions = block_rank[:, None] * frames_here + jnp.arange(frames_here, dtype=jnp.int32)
        key_heads = key_heads.transpose(1, 0, 2, 3, 4).reshape(records, -1, head_count, HEAD_DIM)
        value_heads = value_heads.transpose(1, 0, 2, 3, 4).reshape(records, -1, head_count, HEAD_DIM)
        attended = attend(query_heads, key_heads, value_heads, positions.reshape(-1), frame_counts)
        attended = attended.transpose(0, 2, 1, 3).reshape(records, frames_here, head_count * HEAD_DIM)
    attn_part = jnp.einsum("stc,cd->std", attended, w_out, preferred_element_type=jnp.float32)
    mp_count = lax.axis_size("mp")
    mp_rank = lax.axis_index("mp")
    rows_mine = frames_here // mp_count
    row_start = mp_rank * rows_mine
    attn_mine = reduce_scatter_rows(attn_part.astype(jnp.bfloat16), "mp", 1)
    features_mine = lax.dynamic_slice_in_dim(features, row_start, rows_mine, 1)
    residual_mine = features_mine.astype(jnp.float32) + attn_mine
    normed_mine = layer_norm(residual_mine, conv_gain).astype(jnp.bfloat16)
    def glu_blocks(rows):
        flat = rows.reshape(records, -1, model_width)
        gated = gated_units(flat, w_glu)
        return gated.reshape(rows.shape[:-1] + gated.shape[-1:])

    gated_rows = all_gather_rows(normed_mine, "mp", 1, apply=glu_blocks)
    frame_ids = first_frame + jnp.arange(frames_here, dtype=jnp.int32)
    frame_live = frame_ids[None, :] < frame_counts[:, None]
    gated_rows = jnp.where(frame_live[..., None], gated_rows, jnp.zeros((), jnp.bfloat16))
    rim_width = kernel.shape[0] // 2
    padded = with_halo(gated_rows, (("ctx", 1),), rim_width)
    depthwise = lax.conv_general_dilated(
        padded.astype(jnp.float32),
        kernel[:, None, :],
        window_strides=(1,),
        padding="VALID",
        dimension_numbers=("NWC", "WIO", "NWC"),
        feature_group_count=kernel.shape[1],
        precision=lax.Precision.HIGHEST,
    )
    activated = jax.nn.silu(depthwise * bn_scale + bn_shift).astype(jnp.bfloat16)
    conv_part = jnp.einsum("stc,cd->std", activated, w_pw, preferred_element_type=jnp.float32)
    conv_rows = reduce_scatter_rows(conv_part.astype(jnp.bfloat16), "mp", 1)
    combined = residual_mine + conv_rows
    clip_bound = clip_level.astype(jnp.float32) / 16.0
    clipped = jnp.clip(combined, -clip_bound, clip_bound)
    mine_ids = first_frame + row_start + jnp.arange(rows_mine, dtype=jnp.int32)
    mine_live = mine_ids[None, :] < frame_counts[:, None]
    return jnp.where(mine_live[..., None], clipped, 0.0).astype(jnp.bfloat16)


def solution(mesh):
    return jax.shard_map(
        shards,
        mesh=mesh,
        in_specs=(
            P("groups", "ctx", None),
            P("groups"),
            P(),
            P(None, None, "mp"),
            P("mp", None),
            P(),
            P(None, None, "mp"),
            P(None, "mp"),
            P("mp"),
            P("mp"),
            P("mp", None),
            P(),
        ),
        out_specs=P("groups", ("ctx", "mp"), None),
        check_vma=False,
    )
```

```python
import jax
import jax.numpy as jnp
from jax import lax
from jax.sharding import PartitionSpec as P

HEAD_DIM = 64


epsilon = 1e-05
masked_score = -1e30


def with_halo(x, sides, width):
    for axis, dim in sides:
        devices, length = (lax.axis_size(axis), x.shape[dim])
        up = [(i, (i + 1) % devices) for i in range(devices - 1)]
        down = [(j, i) for i, j in up]
        last = lax.slice_in_dim(x, length - width, length, axis=dim)
        initial = lax.slice_in_dim(x, 0, width, axis=dim)
        before = lax.ppermute(last, axis, up)
        after = lax.ppermute(initial, axis, down)
        x = jnp.concatenate([before, x, after], axis=dim)
    return x


def layer_norm(values, gain):
    centre = jnp.mean(values, axis=-1, keepdims=True)
    centred = values - centre
    variance = jnp.mean(centred * centred, axis=-1, keepdims=True)
    return centred * lax.rsqrt(variance + epsilon) * gain


def gated_units(normed, w_glu):
    halves = jnp.einsum("std,gdc->gstc", normed, w_glu, preferred_element_type=jnp.float32)
    return (halves[0] * jax.nn.sigmoid(halves[1])).astype(jnp.bfloat16)


def xor_pairs(count, mask):
    return [(i, i ^ mask) for i in range(count)]


def bit_count(count):
    bits = count.bit_length() - 1
    assert (1 << bits) == count
    return bits


def reduce_scatter_rows(x, axis, dim):
    count, rank = lax.axis_size(axis), lax.axis_index(axis)
    bits = bit_count(count)
    shape = x.shape
    block = shape[dim] // count
    acc = x.reshape(shape[:dim] + (2,) * bits + (block,) + shape[dim + 1 :])
    first = 0
    if bits >= 2:
        mine, onward = rank & 1, (rank >> 1) & 1
        keep = lax.dynamic_index_in_dim(acc, mine, dim + bits - 1, keepdims=False)
        send = lax.dynamic_index_in_dim(acc, 1 - mine, dim + bits - 1, keepdims=False)
        send_far = lax.dynamic_index_in_dim(send, 1 - onward, dim + bits - 2, keepdims=False)
        cut = send_far.shape[0] // 2 if send_far.shape[0] > 1 else send_far.shape[0]
        got_far = [
            lax.ppermute(piece, axis, xor_pairs(count, 1))
            for piece in (send_far[:cut], send_far[cut:])
            if piece.shape[0] > 0
        ]
        got_near = lax.ppermute(
            lax.dynamic_index_in_dim(send, onward, dim + bits - 2, keepdims=False),
            axis, xor_pairs(count, 1),
        )
        far = lax.dynamic_index_in_dim(keep, 1 - onward, dim + bits - 2, keepdims=False)
        far = jnp.concatenate(
            [
                (piece_keep.astype(jnp.float32) + piece_got.astype(jnp.float32)).astype(jnp.bfloat16)
                for piece_keep, piece_got in zip((far[:cut], far[cut:]), got_far)
            ],
            axis=0,
        )
        near = lax.dynamic_index_in_dim(keep, onward, dim + bits - 2, keepdims=False)
        near = near.astype(jnp.float32) + got_near.astype(jnp.float32)
        got = lax.ppermute(far, axis, xor_pairs(count, 2))
        acc = near + got.astype(jnp.float32)
        first = 2
    for b in range(first, bits):
        bit_axis = dim + bits - 1 - b
        mine = (rank >> b) & 1
        keep = lax.dynamic_index_in_dim(acc, mine, bit_axis, keepdims=False)
        send = lax.dynamic_index_in_dim(acc, 1 - mine, bit_axis, keepdims=False)
        got = lax.ppermute(send.astype(jnp.bfloat16), axis, xor_pairs(count, 1 << b))
        acc = keep.astype(jnp.float32) + got.astype(jnp.float32)
    return acc


def place_pair(mine, other, bit, axis):
    both = jnp.zeros(mine.shape[:axis] + (2,) + mine.shape[axis:], mine.dtype)
    both = lax.dynamic_update_index_in_dim(both, mine, bit, axis)
    return lax.dynamic_update_index_in_dim(both, other, 1 - bit, axis)


def all_gather_rows(x, axis, dim):
    count, rank = lax.axis_size(axis), lax.axis_index(axis)
    bits = bit_count(count)
    shape = x.shape
    mine_acc = x
    their_acc = lax.ppermute(x, axis, xor_pairs(count, 1))
    for k, b in enumerate(reversed(range(1, bits))):
        bit = (rank >> b) & 1
        got = lax.ppermute(mine_acc, axis, xor_pairs(count, 1 << b))
        forwarded = lax.ppermute(got, axis, xor_pairs(count, 1))
        mine_acc = place_pair(mine_acc, got, bit, dim + k)
        their_acc = place_pair(their_acc, forwarded, bit, dim + k)
    acc = place_pair(mine_acc, their_acc, rank & 1, dim + bits - 1)
    return acc.reshape(shape[:dim] + (shape[dim] * count,) + shape[dim + 1 :])


def ring_gather(x, axis):
    count = lax.axis_size(axis)
    right = [(i, (i + 1) % count) for i in range(count)]
    left = [(i, (i - 1) % count) for i in range(count)]
    right_steps = count // 2
    left_steps = count - 1 - right_steps
    from_left, from_right = [], []
    going_right, going_left = x, x
    for step in range(right_steps):
        going_right = lax.ppermute(going_right, axis, right)
        from_left.append(going_right)
        if step < left_steps:
            going_left = lax.ppermute(going_left, axis, left)
            from_right.append(going_left)
    return jnp.stack([x] + from_right + from_left[::-1], axis=0)


def attend(queries, key_rows, value_rows, positions, frame_counts):
    scores = jnp.einsum(
        "sqhe,skhe->shqk", queries, key_rows, preferred_element_type=jnp.float32
    ) * HEAD_DIM ** (-0.5)
    is_live = positions[None, :] < frame_counts[:, None]
    scores = jnp.where(is_live[:, None, None, :], scores, masked_score)
    row_max = jnp.max(scores, axis=-1, keepdims=True)
    weights = jnp.exp(scores - row_max)
    row_sum = jnp.sum(weights, axis=-1)
    contrib = jnp.einsum(
        "shqk,skhe->shqe",
        weights.astype(jnp.bfloat16),
        value_rows,
        preferred_element_type=jnp.float32,
    )
    return (contrib / row_sum[..., None]).astype(jnp.bfloat16)


def attend_by_heads(projected, frame_counts, axis):
    _, records, frames, width = projected.shape
    count, rank = lax.axis_size(axis), lax.axis_index(axis)
    group = width // HEAD_DIM // count
    split = projected.reshape(3, records, frames, count, group, HEAD_DIM)
    pieces = [lax.dynamic_index_in_dim(split, rank, 3, keepdims=False)]
    sources = [rank]
    for shift in range(1, count):
        target = (rank + shift) % count
        send = lax.dynamic_index_in_dim(split, target, 3, keepdims=False)
        pairs = [(i, (i + shift) % count) for i in range(count)]
        pieces.append(lax.ppermute(send, axis, pairs))
        sources.append((rank - shift) % count)
    every = jnp.concatenate(pieces, axis=2)
    frame_steps = jnp.arange(frames, dtype=jnp.int32)
    positions = jnp.concatenate([source * frames + frame_steps for source in sources])
    attended = attend(every[0], every[1], every[2], positions, frame_counts)
    back = [attended[:, :, :frames]]
    for shift in range(1, count):
        rows = attended[:, :, shift * frames : (shift + 1) * frames]
        pairs = [(i, (i - shift) % count) for i in range(count)]
        back.append(lax.ppermute(rows, axis, pairs))
    ordered = jnp.roll(jnp.stack(back, axis=1), rank, axis=1)
    return ordered.transpose(0, 3, 1, 2, 4).reshape(records, frames, width)


def shards(
    features,
    frame_counts,
    attn_gain,
    w_qkv,
    w_out,
    conv_gain,
    w_glu,
    kernel,
    bn_scale,
    bn_shift,
    w_pw,
    clip_level,
):
    records, frames_here, model_width = features.shape
    head_count = w_qkv.shape[2] // HEAD_DIM
    ctx_rank = lax.axis_index("ctx")
    ctx_count = lax.axis_size("ctx")
    score_scale = HEAD_DIM ** (-0.5)
    first_frame = ctx_rank * frames_here
    normed = layer_norm(features.astype(jnp.float32), attn_gain).astype(jnp.bfloat16)
    projected = jnp.einsum(
        "std,idc->istc", normed, w_qkv, preferred_element_type=jnp.float32
    ).astype(jnp.bfloat16)
    if head_count % ctx_count == 0:
        attended = attend_by_heads(projected, frame_counts, "ctx")
    else:
        query_heads = projected[0].reshape(records, frames_here, head_count, HEAD_DIM)
        kv_all = ring_gather(projected[1:], "ctx")
        key_heads = kv_all[:, 0].reshape(ctx_count, records, frames_here, head_count, HEAD_DIM)
        value_heads = kv_all[:, 1].reshape(ctx_count, records, frames_here, head_count, HEAD_DIM)
        block_rank = (ctx_rank + jnp.arange(ctx_count, dtype=jnp.int32)) % ctx_count
        positions = block_rank[:, None] * frames_here + jnp.arange(frames_here, dtype=jnp.int32)
        key_heads = key_heads.transpose(1, 0, 2, 3, 4).reshape(records, -1, head_count, HEAD_DIM)
        value_heads = value_heads.transpose(1, 0, 2, 3, 4).reshape(records, -1, head_count, HEAD_DIM)
        attended = attend(query_heads, key_heads, value_heads, positions.reshape(-1), frame_counts)
        attended = attended.transpose(0, 2, 1, 3).reshape(records, frames_here, head_count * HEAD_DIM)
    attn_part = jnp.einsum("stc,cd->std", attended, w_out, preferred_element_type=jnp.float32)
    mp_count = lax.axis_size("mp")
    mp_rank = lax.axis_index("mp")
    rows_mine = frames_here // mp_count
    row_start = mp_rank * rows_mine
    attn_mine = reduce_scatter_rows(attn_part.astype(jnp.bfloat16), "mp", 1)
    features_mine = lax.dynamic_slice_in_dim(features, row_start, rows_mine, 1)
    residual_mine = features_mine.astype(jnp.float32) + attn_mine
    normed_mine = layer_norm(residual_mine, conv_gain).astype(jnp.bfloat16)
    normed_conv = all_gather_rows(normed_mine, "mp", 1)
    gated_rows = gated_units(normed_conv, w_glu)
    frame_ids = first_frame + jnp.arange(frames_here, dtype=jnp.int32)
    frame_live = frame_ids[None, :] < frame_counts[:, None]
    gated_rows = jnp.where(frame_live[..., None], gated_rows, jnp.zeros((), jnp.bfloat16))
    rim_width = kernel.shape[0] // 2
    padded = with_halo(gated_rows, (("ctx", 1),), rim_width)
    depthwise = lax.conv_general_dilated(
        padded.astype(jnp.float32),
        kernel[:, None, :],
        window_strides=(1,),
        padding="VALID",
        dimension_numbers=("NWC", "WIO", "NWC"),
        feature_group_count=kernel.shape[1],
        precision=lax.Precision.HIGHEST,
    )
    activated = jax.nn.silu(depthwise * bn_scale + bn_shift).astype(jnp.bfloat16)
    conv_part = jnp.einsum("stc,cd->std", activated, w_pw, preferred_element_type=jnp.float32)
    conv_rows = reduce_scatter_rows(conv_part.astype(jnp.bfloat16), "mp", 1)
    combined = residual_mine + conv_rows
    clip_bound = clip_level.astype(jnp.float32) / 16.0
    clipped = jnp.clip(combined, -clip_bound, clip_bound)
    mine_ids = first_frame + row_start + jnp.arange(rows_mine, dtype=jnp.int32)
    mine_live = mine_ids[None, :] < frame_counts[:, None]
    return jnp.where(mine_live[..., None], clipped, 0.0).astype(jnp.bfloat16)


def solution(mesh):
    return jax.shard_map(
        shards,
        mesh=mesh,
        in_specs=(
            P("groups", "ctx", None),
            P("groups"),
            P(),
            P(None, None, "mp"),
            P("mp", None),
            P(),
            P(None, None, "mp"),
            P(None, "mp"),
            P("mp"),
            P("mp"),
            P("mp", None),
            P(),
        ),
        out_specs=P("groups", ("ctx", "mp"), None),
        check_vma=False,
    )
```

```python
import jax
import jax.numpy as jnp
from jax import lax
from jax.sharding import PartitionSpec as P

HEAD_DIM = 64


epsilon = 1e-05
masked_score = -1e30


def with_halo(x, sides, width):
    for axis, dim in sides:
        devices, length = (lax.axis_size(axis), x.shape[dim])
        up = [(i, (i + 1) % devices) for i in range(devices - 1)]
        down = [(j, i) for i, j in up]
        last = lax.slice_in_dim(x, length - width, length, axis=dim)
        initial = lax.slice_in_dim(x, 0, width, axis=dim)
        before = lax.ppermute(last, axis, up)
        after = lax.ppermute(initial, axis, down)
        x = jnp.concatenate([before, x, after], axis=dim)
    return x


def layer_norm(values, gain):
    centre = jnp.mean(values, axis=-1, keepdims=True)
    centred = values - centre
    variance = jnp.mean(centred * centred, axis=-1, keepdims=True)
    return centred * lax.rsqrt(variance + epsilon) * gain


def gated_units(normed, w_glu):
    halves = jnp.einsum("std,gdc->gstc", normed, w_glu, preferred_element_type=jnp.float32)
    return (halves[0] * jax.nn.sigmoid(halves[1])).astype(jnp.bfloat16)


def xor_pairs(count, mask):
    return [(i, i ^ mask) for i in range(count)]


def bit_count(count):
    bits = count.bit_length() - 1
    assert (1 << bits) == count
    return bits


def reduce_scatter_rows(x, axis, dim):
    count, rank = lax.axis_size(axis), lax.axis_index(axis)
    bits = bit_count(count)
    shape = x.shape
    block = shape[dim] // count
    acc = x.reshape(shape[:dim] + (2,) * bits + (block,) + shape[dim + 1 :])
    first = 0
    if bits >= 2:
        mine, onward = rank & 1, (rank >> 1) & 1
        keep = lax.dynamic_index_in_dim(acc, mine, dim + bits - 1, keepdims=False)
        send = lax.dynamic_index_in_dim(acc, 1 - mine, dim + bits - 1, keepdims=False)
        send_far = lax.dynamic_index_in_dim(send, 1 - onward, dim + bits - 2, keepdims=False)
        rows = send_far.shape[dim]
        spans = [
            (r, r + 1, h, h + rows // 2)
            for r in range(send_far.shape[0])
            for h in (0, rows // 2)
        ] if rows % 2 == 0 and send_far.shape[0] <= 2 else [(0, send_far.shape[0], 0, rows)]
        got_far = [
            lax.ppermute(send_far[a:b, c:d], axis, xor_pairs(count, 1)) for a, b, c, d in spans
        ]
        far = lax.dynamic_index_in_dim(keep, 1 - onward, dim + bits - 2, keepdims=False)
        summed = [
            (far[a:b, c:d].astype(jnp.float32) + piece.astype(jnp.float32)).astype(jnp.bfloat16)
            for (a, b, c, d), piece in zip(spans, got_far)
        ]
        if len(spans) > 1:
            halves = [jnp.concatenate(summed[i : i + 2], axis=dim) for i in range(0, len(summed), 2)]
            far = jnp.concatenate(halves, axis=0)
        else:
            far = summed[0]
        got_near = lax.ppermute(
            lax.dynamic_index_in_dim(send, onward, dim + bits - 2, keepdims=False),
            axis, xor_pairs(count, 1),
        )
        near = lax.dynamic_index_in_dim(keep, onward, dim + bits - 2, keepdims=False)
        near = near.astype(jnp.float32) + got_near.astype(jnp.float32)
        got = lax.ppermute(far, axis, xor_pairs(count, 2))
        acc = near + got.astype(jnp.float32)
        first = 2
    for b in range(first, bits):
        bit_axis = dim + bits - 1 - b
        mine = (rank >> b) & 1
        keep = lax.dynamic_index_in_dim(acc, mine, bit_axis, keepdims=False)
        send = lax.dynamic_index_in_dim(acc, 1 - mine, bit_axis, keepdims=False)
        got = lax.ppermute(send.astype(jnp.bfloat16), axis, xor_pairs(count, 1 << b))
        acc = keep.astype(jnp.float32) + got.astype(jnp.float32)
    return acc


def place_pair(mine, other, bit, axis):
    both = jnp.zeros(mine.shape[:axis] + (2,) + mine.shape[axis:], mine.dtype)
    both = lax.dynamic_update_index_in_dim(both, mine, bit, axis)
    return lax.dynamic_update_index_in_dim(both, other, 1 - bit, axis)


def all_gather_rows(x, axis, dim):
    count, rank = lax.axis_size(axis), lax.axis_index(axis)
    bits = bit_count(count)
    shape = x.shape
    mine_acc = x
    their_acc = lax.ppermute(x, axis, xor_pairs(count, 1))
    for k, b in enumerate(reversed(range(1, bits))):
        bit = (rank >> b) & 1
        got = lax.ppermute(mine_acc, axis, xor_pairs(count, 1 << b))
        forwarded = lax.ppermute(got, axis, xor_pairs(count, 1))
        mine_acc = place_pair(mine_acc, got, bit, dim + k)
        their_acc = place_pair(their_acc, forwarded, bit, dim + k)
    acc = place_pair(mine_acc, their_acc, rank & 1, dim + bits - 1)
    return acc.reshape(shape[:dim] + (shape[dim] * count,) + shape[dim + 1 :])


def ring_gather(x, axis):
    count = lax.axis_size(axis)
    right = [(i, (i + 1) % count) for i in range(count)]
    left = [(i, (i - 1) % count) for i in range(count)]
    right_steps = count // 2
    left_steps = count - 1 - right_steps
    from_left, from_right = [], []
    going_right, going_left = x, x
    for step in range(right_steps):
        going_right = lax.ppermute(going_right, axis, right)
        from_left.append(going_right)
        if step < left_steps:
            going_left = lax.ppermute(going_left, axis, left)
            from_right.append(going_left)
    return jnp.stack([x] + from_right + from_left[::-1], axis=0)


def attend(queries, key_rows, value_rows, positions, frame_counts):
    scores = jnp.einsum(
        "sqhe,skhe->shqk", queries, key_rows, preferred_element_type=jnp.float32
    ) * HEAD_DIM ** (-0.5)
    is_live = positions[None, :] < frame_counts[:, None]
    scores = jnp.where(is_live[:, None, None, :], scores, masked_score)
    row_max = jnp.max(scores, axis=-1, keepdims=True)
    weights = jnp.exp(scores - row_max)
    row_sum = jnp.sum(weights, axis=-1)
    contrib = jnp.einsum(
        "shqk,skhe->shqe",
        weights.astype(jnp.bfloat16),
        value_rows,
        preferred_element_type=jnp.float32,
    )
    return (contrib / row_sum[..., None]).astype(jnp.bfloat16)


def attend_by_heads(projected, frame_counts, axis):
    _, records, frames, width = projected.shape
    count, rank = lax.axis_size(axis), lax.axis_index(axis)
    group = width // HEAD_DIM // count
    split = projected.reshape(3, records, frames, count, group, HEAD_DIM)
    pieces = [lax.dynamic_index_in_dim(split, rank, 3, keepdims=False)]
    sources = [rank]
    for shift in range(1, count):
        target = (rank + shift) % count
        send = lax.dynamic_index_in_dim(split, target, 3, keepdims=False)
        pairs = [(i, (i + shift) % count) for i in range(count)]
        pieces.append(lax.ppermute(send, axis, pairs))
        sources.append((rank - shift) % count)
    every = jnp.concatenate(pieces, axis=2)
    frame_steps = jnp.arange(frames, dtype=jnp.int32)
    positions = jnp.concatenate([source * frames + frame_steps for source in sources])
    attended = attend(every[0], every[1], every[2], positions, frame_counts)
    back = [attended[:, :, :frames]]
    for shift in range(1, count):
        rows = attended[:, :, shift * frames : (shift + 1) * frames]
        pairs = [(i, (i - shift) % count) for i in range(count)]
        back.append(lax.ppermute(rows, axis, pairs))
    ordered = jnp.roll(jnp.stack(back, axis=1), rank, axis=1)
    return ordered.transpose(0, 3, 1, 2, 4).reshape(records, frames, width)


def shards(
    features,
    frame_counts,
    attn_gain,
    w_qkv,
    w_out,
    conv_gain,
    w_glu,
    kernel,
    bn_scale,
    bn_shift,
    w_pw,
    clip_level,
):
    records, frames_here, model_width = features.shape
    head_count = w_qkv.shape[2] // HEAD_DIM
    ctx_rank = lax.axis_index("ctx")
    ctx_count = lax.axis_size("ctx")
    score_scale = HEAD_DIM ** (-0.5)
    first_frame = ctx_rank * frames_here
    normed = layer_norm(features.astype(jnp.float32), attn_gain).astype(jnp.bfloat16)
    projected = jnp.einsum(
        "std,idc->istc", normed, w_qkv, preferred_element_type=jnp.float32
    ).astype(jnp.bfloat16)
    if head_count % ctx_count == 0:
        attended = attend_by_heads(projected, frame_counts, "ctx")
    else:
        query_heads = projected[0].reshape(records, frames_here, head_count, HEAD_DIM)
        kv_all = ring_gather(projected[1:], "ctx")
        key_heads = kv_all[:, 0].reshape(ctx_count, records, frames_here, head_count, HEAD_DIM)
        value_heads = kv_all[:, 1].reshape(ctx_count, records, frames_here, head_count, HEAD_DIM)
        block_rank = (ctx_rank + jnp.arange(ctx_count, dtype=jnp.int32)) % ctx_count
        positions = block_rank[:, None] * frames_here + jnp.arange(frames_here, dtype=jnp.int32)
        key_heads = key_heads.transpose(1, 0, 2, 3, 4).reshape(records, -1, head_count, HEAD_DIM)
        value_heads = value_heads.transpose(1, 0, 2, 3, 4).reshape(records, -1, head_count, HEAD_DIM)
        attended = attend(query_heads, key_heads, value_heads, positions.reshape(-1), frame_counts)
        attended = attended.transpose(0, 2, 1, 3).reshape(records, frames_here, head_count * HEAD_DIM)
    attn_part = jnp.einsum("stc,cd->std", attended, w_out, preferred_element_type=jnp.float32)
    mp_count = lax.axis_size("mp")
    mp_rank = lax.axis_index("mp")
    rows_mine = frames_here // mp_count
    row_start = mp_rank * rows_mine
    attn_mine = reduce_scatter_rows(attn_part.astype(jnp.bfloat16), "mp", 1)
    features_mine = lax.dynamic_slice_in_dim(features, row_start, rows_mine, 1)
    residual_mine = features_mine.astype(jnp.float32) + attn_mine
    normed_mine = layer_norm(residual_mine, conv_gain).astype(jnp.bfloat16)
    normed_conv = all_gather_rows(normed_mine, "mp", 1)
    gated_rows = gated_units(normed_conv, w_glu)
    frame_ids = first_frame + jnp.arange(frames_here, dtype=jnp.int32)
    frame_live = frame_ids[None, :] < frame_counts[:, None]
    gated_rows = jnp.where(frame_live[..., None], gated_rows, jnp.zeros((), jnp.bfloat16))
    rim_width = kernel.shape[0] // 2
    padded = with_halo(gated_rows, (("ctx", 1),), rim_width)
    depthwise = lax.conv_general_dilated(
        padded.astype(jnp.float32),
        kernel[:, None, :],
        window_strides=(1,),
        padding="VALID",
        dimension_numbers=("NWC", "WIO", "NWC"),
        feature_group_count=kernel.shape[1],
        precision=lax.Precision.HIGHEST,
    )
    activated = jax.nn.silu(depthwise * bn_scale + bn_shift).astype(jnp.bfloat16)
    conv_part = jnp.einsum("stc,cd->std", activated, w_pw, preferred_element_type=jnp.float32)
    conv_rows = reduce_scatter_rows(conv_part.astype(jnp.bfloat16), "mp", 1)
    combined = residual_mine + conv_rows
    clip_bound = clip_level.astype(jnp.float32) / 16.0
    clipped = jnp.clip(combined, -clip_bound, clip_bound)
    mine_ids = first_frame + row_start + jnp.arange(rows_mine, dtype=jnp.int32)
    mine_live = mine_ids[None, :] < frame_counts[:, None]
    return jnp.where(mine_live[..., None], clipped, 0.0).astype(jnp.bfloat16)


def solution(mesh):
    return jax.shard_map(
        shards,
        mesh=mesh,
        in_specs=(
            P("groups", "ctx", None),
            P("groups"),
            P(),
            P(None, None, "mp"),
            P("mp", None),
            P(),
            P(None, None, "mp"),
            P(None, "mp"),
            P("mp"),
            P("mp"),
            P("mp", None),
            P(),
        ),
        out_specs=P("groups", ("ctx", "mp"), None),
        check_vma=False,
    )
```

```python
import jax
import jax.numpy as jnp
from jax import lax
from jax.sharding import PartitionSpec as P

HEAD_DIM = 64


epsilon = 1e-05
masked_score = -1e30


def with_halo(x, sides, width):
    for axis, dim in sides:
        devices, length = (lax.axis_size(axis), x.shape[dim])
        up = [(i, (i + 1) % devices) for i in range(devices - 1)]
        down = [(j, i) for i, j in up]
        last = lax.slice_in_dim(x, length - width, length, axis=dim)
        initial = lax.slice_in_dim(x, 0, width, axis=dim)
        before = lax.ppermute(last, axis, up)
        after = lax.ppermute(initial, axis, down)
        x = jnp.concatenate([before, x, after], axis=dim)
    return x


def layer_norm(values, gain):
    centre = jnp.mean(values, axis=-1, keepdims=True)
    centred = values - centre
    variance = jnp.mean(centred * centred, axis=-1, keepdims=True)
    return centred * lax.rsqrt(variance + epsilon) * gain


def gated_units(normed, w_glu):
    halves = jnp.einsum("std,gdc->gstc", normed, w_glu, preferred_element_type=jnp.float32)
    return (halves[0] * jax.nn.sigmoid(halves[1])).astype(jnp.bfloat16)


def xor_pairs(count, mask):
    return [(i, i ^ mask) for i in range(count)]


def bit_count(count):
    bits = count.bit_length() - 1
    assert (1 << bits) == count
    return bits


def reduce_scatter_rows(x, axis, dim):
    count, rank = lax.axis_size(axis), lax.axis_index(axis)
    bits = bit_count(count)
    shape = x.shape
    block = shape[dim] // count
    acc = x.reshape(shape[:dim] + (2,) * bits + (block,) + shape[dim + 1 :])
    first = 0
    if bits >= 2:
        mine, onward = rank & 1, (rank >> 1) & 1
        keep = lax.dynamic_index_in_dim(acc, mine, dim + bits - 1, keepdims=False)
        send = lax.dynamic_index_in_dim(acc, 1 - mine, dim + bits - 1, keepdims=False)
        send_far = lax.dynamic_index_in_dim(send, 1 - onward, dim + bits - 2, keepdims=False)
        cut = send_far.shape[0] // 2 if send_far.shape[0] > 1 else send_far.shape[0]
        got_far = [
            lax.ppermute(piece, axis, xor_pairs(count, 1))
            for piece in (send_far[:cut], send_far[cut:])
            if piece.shape[0] > 0
        ]
        got_near = lax.ppermute(
            lax.dynamic_index_in_dim(send, onward, dim + bits - 2, keepdims=False),
            axis, xor_pairs(count, 1),
        )
        far = lax.dynamic_index_in_dim(keep, 1 - onward, dim + bits - 2, keepdims=False)
        far = jnp.concatenate(
            [
                (piece_keep.astype(jnp.float32) + piece_got.astype(jnp.float32)).astype(jnp.bfloat16)
                for piece_keep, piece_got in zip((far[:cut], far[cut:]), got_far)
            ],
            axis=0,
        )
        near = lax.dynamic_index_in_dim(keep, onward, dim + bits - 2, keepdims=False)
        near = near.astype(jnp.float32) + got_near.astype(jnp.float32)
        got = lax.ppermute(far, axis, xor_pairs(count, 2))
        acc = near + got.astype(jnp.float32)
        first = 2
    for b in range(first, bits):
        bit_axis = dim + bits - 1 - b
        mine = (rank >> b) & 1
        keep = lax.dynamic_index_in_dim(acc, mine, bit_axis, keepdims=False)
        send = lax.dynamic_index_in_dim(acc, 1 - mine, bit_axis, keepdims=False)
        got = lax.ppermute(send.astype(jnp.bfloat16), axis, xor_pairs(count, 1 << b))
        acc = keep.astype(jnp.float32) + got.astype(jnp.float32)
    return acc


def place_pair(mine, other, bit, axis):
    both = jnp.zeros(mine.shape[:axis] + (2,) + mine.shape[axis:], mine.dtype)
    both = lax.dynamic_update_index_in_dim(both, mine, bit, axis)
    return lax.dynamic_update_index_in_dim(both, other, 1 - bit, axis)


def all_gather_rows(x, axis, dim):
    count, rank = lax.axis_size(axis), lax.axis_index(axis)
    bits = bit_count(count)
    shape = x.shape
    mine_acc = x
    their_acc = lax.ppermute(x, axis, xor_pairs(count, 1))
    for k, b in enumerate(reversed(range(1, bits))):
        bit = (rank >> b) & 1
        got = lax.ppermute(mine_acc, axis, xor_pairs(count, 1 << b))
        forwarded = lax.ppermute(got, axis, xor_pairs(count, 1))
        mine_acc = place_pair(mine_acc, got, bit, dim + k)
        their_acc = place_pair(their_acc, forwarded, bit, dim + k)
    acc = place_pair(mine_acc, their_acc, rank & 1, dim + bits - 1)
    return acc.reshape(shape[:dim] + (shape[dim] * count,) + shape[dim + 1 :])


def ring_gather(x, axis):
    count = lax.axis_size(axis)
    right = [(i, (i + 1) % count) for i in range(count)]
    left = [(i, (i - 1) % count) for i in range(count)]
    right_steps = count // 2
    left_steps = count - 1 - right_steps
    from_left, from_right = [], []
    going_right, going_left = x, x
    for step in range(right_steps):
        going_right = lax.ppermute(going_right, axis, right)
        from_left.append(going_right)
        if step < left_steps:
            going_left = lax.ppermute(going_left, axis, left)
            from_right.append(going_left)
    return jnp.stack([x] + from_right + from_left[::-1], axis=0)


def attend(queries, key_rows, value_rows, positions, frame_counts):
    scores = jnp.einsum(
        "sqhe,skhe->shqk", queries, key_rows, preferred_element_type=jnp.float32
    ) * HEAD_DIM ** (-0.5)
    is_live = positions[None, :] < frame_counts[:, None]
    scores = jnp.where(is_live[:, None, None, :], scores, masked_score)
    row_max = jnp.max(scores, axis=-1, keepdims=True)
    weights = jnp.exp(scores - row_max)
    row_sum = jnp.sum(weights, axis=-1)
    contrib = jnp.einsum(
        "shqk,skhe->shqe",
        weights.astype(jnp.bfloat16),
        value_rows,
        preferred_element_type=jnp.float32,
    )
    return (contrib / row_sum[..., None]).astype(jnp.bfloat16)


def attend_by_heads(projected, frame_counts, axis):
    _, records, frames, width = projected.shape
    count, rank = lax.axis_size(axis), lax.axis_index(axis)
    group = width // HEAD_DIM // count
    split = projected.reshape(3, records, frames, count, group, HEAD_DIM)
    pieces = [lax.dynamic_index_in_dim(split, rank, 3, keepdims=False)]
    sources = [rank]
    for shift in range(1, count):
        target = (rank + shift) % count
        send = lax.dynamic_index_in_dim(split, target, 3, keepdims=False)
        pairs = [(i, (i + shift) % count) for i in range(count)]
        pieces.append(lax.ppermute(send, axis, pairs))
        sources.append((rank - shift) % count)
    every = jnp.concatenate(pieces, axis=2)
    frame_steps = jnp.arange(frames, dtype=jnp.int32)
    positions = jnp.concatenate([source * frames + frame_steps for source in sources])
    attended = attend(every[0], every[1], every[2], positions, frame_counts)
    back = [attended[:, :, :frames]]
    for shift in range(1, count):
        rows = attended[:, :, shift * frames : (shift + 1) * frames]
        pairs = [(i, (i - shift) % count) for i in range(count)]
        back.append(lax.ppermute(rows, axis, pairs))
    ordered = jnp.roll(jnp.stack(back, axis=1), rank, axis=1)
    return ordered.transpose(0, 3, 1, 2, 4).reshape(records, frames, width)


def shards(
    features,
    frame_counts,
    attn_gain,
    w_qkv,
    w_out,
    conv_gain,
    w_glu,
    kernel,
    bn_scale,
    bn_shift,
    w_pw,
    clip_level,
):
    records, frames_here, model_width = features.shape
    head_count = w_qkv.shape[2] // HEAD_DIM
    ctx_rank = lax.axis_index("ctx")
    ctx_count = lax.axis_size("ctx")
    score_scale = HEAD_DIM ** (-0.5)
    first_frame = ctx_rank * frames_here
    normed = layer_norm(features.astype(jnp.float32), attn_gain).astype(jnp.bfloat16)
    projected = jnp.einsum(
        "std,idc->istc", normed, w_qkv, preferred_element_type=jnp.float32
    ).astype(jnp.bfloat16)
    if head_count % ctx_count == 0:
        attended = attend_by_heads(projected, frame_counts, "ctx")
    else:
        query_heads = projected[0].reshape(records, frames_here, head_count, HEAD_DIM)
        kv_all = ring_gather(projected[1:], "ctx")
        key_heads = kv_all[:, 0].reshape(ctx_count, records, frames_here, head_count, HEAD_DIM)
        value_heads = kv_all[:, 1].reshape(ctx_count, records, frames_here, head_count, HEAD_DIM)
        block_rank = (ctx_rank + jnp.arange(ctx_count, dtype=jnp.int32)) % ctx_count
        positions = block_rank[:, None] * frames_here + jnp.arange(frames_here, dtype=jnp.int32)
        key_heads = key_heads.transpose(1, 0, 2, 3, 4).reshape(records, -1, head_count, HEAD_DIM)
        value_heads = value_heads.transpose(1, 0, 2, 3, 4).reshape(records, -1, head_count, HEAD_DIM)
        attended = attend(query_heads, key_heads, value_heads, positions.reshape(-1), frame_counts)
        attended = attended.transpose(0, 2, 1, 3).reshape(records, frames_here, head_count * HEAD_DIM)
    attn_part = jnp.concatenate(
        [
            jnp.einsum("stc,cd->std", attended[r : r + 1], w_out, preferred_element_type=jnp.float32)
            for r in range(attended.shape[0])
        ],
        axis=0,
    )
    mp_count = lax.axis_size("mp")
    mp_rank = lax.axis_index("mp")
    rows_mine = frames_here // mp_count
    row_start = mp_rank * rows_mine
    attn_mine = reduce_scatter_rows(attn_part.astype(jnp.bfloat16), "mp", 1)
    features_mine = lax.dynamic_slice_in_dim(features, row_start, rows_mine, 1)
    residual_mine = features_mine.astype(jnp.float32) + attn_mine
    normed_mine = layer_norm(residual_mine, conv_gain).astype(jnp.bfloat16)
    normed_conv = all_gather_rows(normed_mine, "mp", 1)
    gated_rows = gated_units(normed_conv, w_glu)
    frame_ids = first_frame + jnp.arange(frames_here, dtype=jnp.int32)
    frame_live = frame_ids[None, :] < frame_counts[:, None]
    gated_rows = jnp.where(frame_live[..., None], gated_rows, jnp.zeros((), jnp.bfloat16))
    rim_width = kernel.shape[0] // 2
    padded = with_halo(gated_rows, (("ctx", 1),), rim_width)
    depthwise = lax.conv_general_dilated(
        padded.astype(jnp.float32),
        kernel[:, None, :],
        window_strides=(1,),
        padding="VALID",
        dimension_numbers=("NWC", "WIO", "NWC"),
        feature_group_count=kernel.shape[1],
        precision=lax.Precision.HIGHEST,
    )
    activated = jax.nn.silu(depthwise * bn_scale + bn_shift).astype(jnp.bfloat16)
    conv_part = jnp.concatenate(
        [
            jnp.einsum("stc,cd->std", activated[r : r + 1], w_pw, preferred_element_type=jnp.float32)
            for r in range(activated.shape[0])
        ],
        axis=0,
    )
    conv_rows = reduce_scatter_rows(conv_part.astype(jnp.bfloat16), "mp", 1)
    combined = residual_mine + conv_rows
    clip_bound = clip_level.astype(jnp.float32) / 16.0
    clipped = jnp.clip(combined, -clip_bound, clip_bound)
    mine_ids = first_frame + row_start + jnp.arange(rows_mine, dtype=jnp.int32)
    mine_live = mine_ids[None, :] < frame_counts[:, None]
    return jnp.where(mine_live[..., None], clipped, 0.0).astype(jnp.bfloat16)


def solution(mesh):
    return jax.shard_map(
        shards,
        mesh=mesh,
        in_specs=(
            P("groups", "ctx", None),
            P("groups"),
            P(),
            P(None, None, "mp"),
            P("mp", None),
            P(),
            P(None, None, "mp"),
            P(None, "mp"),
            P("mp"),
            P("mp"),
            P("mp", None),
            P(),
        ),
        out_specs=P("groups", ("ctx", "mp"), None),
        check_vma=False,
    )
```
